32 devices in a mesh: seq: 8 (over z, x), tensor: 4 (over y, core).
Axes of the slice: x: 2, y: 2, z: 4, core: 2. Of those that a mesh axis runs over, the one named last changes fastest.
Arguments:
- hidden: bfloat16 [4096, 1280], P(('seq', 'tensor')), may hold values from -6 to 6
- segment_ids: int32 [4096], P('seq'), may hold values from 0 to 3, never falling along the last dimension, each value on 1 to 2048 neighbouring positions
- page_slot: int32 [32], replicated, may hold values from 0 to 31, each once
- in_proj: bfloat16 [1280, 16, 192], P(None, 'tensor'), may hold values from -6 to 6
- out_proj: bfloat16 [1024, 1280], P('tensor'), may hold values from -0.1875 to 0.1875
- up_proj: bfloat16 [1280, 2, 5120], P(None, None, 'tensor'), may hold values from -6 to 6
- down_proj: bfloat16 [5120, 1280], P('tensor'), may hold values from -0.078125 to 0.078125
- score_scale: float32 [16, 64], P('tensor'), may hold values from 0.5 to 2
- mlp_scale: float32 [2, 5120], P(None, 'tensor'), may hold values from 0.5 to 2
- step_rates: float32 [2, 1280], replicated, may hold values from 0.05 to 0.5
Outputs:
- out_state: bfloat16 [4096, 1280], P(('seq', 'tensor'))
- page_cache: bfloat16 [32, 128, 2048], P('seq', None, 'tensor')
The draws below stay inside these ranges and needn't reach their ends.
Inputs may be any that keep to these rules, and one draw needn't show every extreme that they name: `segment_ids`: never falling along the tokens; each prompt has 1 to 2048 tokens, one exactly 2048. `page_slot`: each slot named by exactly one page.
All inputs are finite; a program needn't handle non-finite values.
Results may differ from the reference program's by a relative error of at most 0.012.
Values may be sent and summed in bfloat16 or wider, within the bound.
No kernel may reach another device: no remote copies, remote signals or barrier semaphores. Data moves between devices by JAX's collectives and lax.ppermute only.
A program may use at most 128 MiB of HBM per device.

```python
import math
import jax
import jax.numpy as jnp
import numpy as np
from jax import lax

D = 1280
HD = 64
FF = 5120
HEADS = 16
PAGE = 128
PROMPTS = 4
TOKENS = 4096
MOST = 2048
PAGES = 32
N_TENSOR = 4


def block_scale(stream_key, shape, split, smallest, top_value):
    loudness, own = 1.0, jax.random.fold_in(stream_key, 6)
    for axis_at, parts in split:
        draws = jnp.exp(jax.random.uniform(jax.random.fold_in(own, axis_at), (parts,), jnp.float32, smallest / len(split), top_value / len(split)))
        loudness = loudness * jnp.repeat(draws, shape[axis_at] // parts).reshape([-1 if axis == axis_at else 1 for axis in range(len(shape))])
    return loudness


def profile(amount, total, reach, lean):
    weights = [(1 << 20) // math.isqrt(grade ** lean) + 1 for grade in range(2, amount + 1)]
    surplus, holding = total - reach - (amount - 1), [1] * (amount - 1)
    while surplus > 0:
        candidates = [i for i in range(amount - 1) if holding[i] < reach]
        pool, remaining = sum([weights[i] for i in candidates]), surplus
        for i in candidates:
            addition = min(reach - holding[i], max(1, remaining * weights[i] // pool), surplus)
            holding[i] = holding[i] + addition
            surplus = surplus - addition
    return np.array([reach] + holding)


def uneven_parts(rng, amount, total, most, skew):
    if amount == 2:
        one = jax.random.randint(rng, (), max(1, total - most), min(most, total - 1) + 1)
        return jnp.stack([one, total - one])
    lengths = jnp.asarray(profile(amount, total, most, skew), jnp.int32)
    couples = (amount - 1) // 2
    source_of, receiver = lengths[1:1 + 2 * couples:2], lengths[2:2 + 2 * couples:2]
    room = jnp.minimum(source_of - 1, most - receiver)
    shifted = jax.random.randint(jax.random.fold_in(rng, 1), (couples,), 0, 1 << 20) % (room + 1)
    lengths = lengths.at[1:1 + 2 * couples:2].set(source_of - shifted).at[2:2 + 2 * couples:2].set(receiver + shifted)
    return lengths[jax.random.permutation(jax.random.fold_in(rng, 2), amount)]


def bell_draw(own_key, extent, width, reach, split=(), kind=jnp.bfloat16):
    values = width * jax.random.normal(own_key, extent, jnp.float32)
    if split:
        values = values * block_scale(own_key, extent, split, -0.22, 0.18)
    return jnp.clip(values, -reach, reach).astype(kind)


def setup_inputs(seed: int = 0) -> dict:
    keys = jax.random.split(jax.random.key(seed), 11)
    return {
        "hidden": bell_draw(keys[0], (TOKENS, D), 1.0, 6.0, ((0, 32),)),
        "segment_ids": jnp.searchsorted(jnp.cumsum(uneven_parts(keys[1], PROMPTS, TOKENS, MOST, 2)), jnp.arange(TOKENS), side="right").astype(jnp.int32),
        "page_slot": jax.random.permutation(keys[2], PAGES).astype(jnp.int32),
        "in_proj": bell_draw(keys[3], (D, HEADS, 3 * HD), 1.0, 6.0, ((1, 4),)),
        "out_proj": bell_draw(keys[4], (HEADS * HD, D), (HEADS * HD) ** -0.5, 0.1875, ((0, 4),)),
        "up_proj": bell_draw(keys[5], (D, 2, FF), 1.0, 6.0, ((2, 4),)),
        "down_proj": bell_draw(keys[6], (FF, D), FF ** -0.5, 0.078125, ((0, 4),)),
        "score_scale": jnp.clip(jnp.exp(math.log(2.0) - 1.3862944 * jax.random.uniform(keys[7], (HEADS, HD), jnp.float32) ** block_scale(keys[7], (HEADS, HD), ((0, 4),), -0.2, 0.2)), 0.5, 2.0),
        "mlp_scale": jnp.clip(jnp.exp(math.log(2.0) - 1.3862944 * jax.random.uniform(keys[8], (2, FF), jnp.float32) ** block_scale(keys[8], (2, FF), ((1, 4),), -0.2, 0.2)), 0.5, 2.0),
        "step_rates": jnp.clip(jnp.exp(jax.random.uniform(keys[9], (2, D), jnp.float32, math.log(0.05), math.log(0.5))), 0.05, 0.5),
    }


EPSILON = 1e-06
NEG_LARGE = -1e+30

def unit_rows(matrix):
    return matrix * lax.rsqrt(lax.optimization_barrier(jnp.sum(matrix * matrix, axis=-1, keepdims=True)) + EPSILON)

def attend(queries, keys_unit, values, segment_ids):
    block_rows = min(512, TOKENS)
    blocks = TOKENS // block_rows
    keys_pad = jnp.concatenate([jnp.zeros((MOST, HEADS, HD), jnp.bfloat16), keys_unit], axis=0)
    values_pad = jnp.concatenate([jnp.zeros((MOST, HEADS, HD), jnp.bfloat16), values], axis=0)
    segs_pad = jnp.concatenate([jnp.full((MOST,), -1, jnp.int32), segment_ids.astype(jnp.int32)], axis=0)

    def one_block(index):
        first_row = (index * block_rows).astype(jnp.int32)
        query_block = lax.dynamic_slice_in_dim(queries, first_row, block_rows, 0)
        query_segs = lax.dynamic_slice_in_dim(segment_ids.astype(jnp.int32), first_row, block_rows, 0)
        key_block = lax.dynamic_slice_in_dim(keys_pad, first_row, MOST + block_rows, 0)
        value_block = lax.dynamic_slice_in_dim(values_pad, first_row, MOST + block_rows, 0)
        key_segs = lax.dynamic_slice_in_dim(segs_pad, first_row, MOST + block_rows, 0)
        query_index = first_row + jnp.arange(block_rows, dtype=jnp.int32)
        key_index = first_row - MOST + jnp.arange(MOST + block_rows, dtype=jnp.int32)
        scores = math.sqrt(HD) * jnp.einsum('qhd,khd->hqk', query_block.astype(jnp.float32), key_block.astype(jnp.float32))
        allowed = (query_segs[:, None] == key_segs[None, :]) & (key_index[None, :] <= query_index[:, None])
        scores = jnp.where(allowed[None], scores, NEG_LARGE)
        top_score = lax.optimization_barrier(jnp.max(scores, axis=-1, keepdims=True))
        weights = jnp.where(allowed[None], jnp.exp(scores - top_score), 0.0)
        weight_sum = lax.optimization_barrier(jnp.sum(weights, axis=-1))
        rounded = lax.optimization_barrier(weights.astype(jnp.bfloat16)).astype(jnp.float32)
        mixed = jnp.einsum('hqk,khd->qhd', rounded, value_block.astype(jnp.float32))
        return (mixed / jnp.transpose(weight_sum)[:, :, None]).astype(jnp.bfloat16)
    return lax.map(one_block, jnp.arange(blocks, dtype=jnp.int32)).reshape(TOKENS, HEADS, HD)

def grouped_sum(make_term, groups):

    def add_group(running, group):
        term = make_term(group)
        rounded = lax.optimization_barrier(term.astype(jnp.bfloat16)).astype(jnp.float32)
        return (running + rounded, None)
    start_value = jnp.zeros((TOKENS, D), jnp.float32)
    return lax.scan(add_group, start_value, jnp.arange(groups, dtype=jnp.int32))[0]

def reference(hidden, segment_ids, page_slot, in_proj, out_proj, up_proj, down_proj, score_scale, mlp_scale, step_rates):
    state = unit_rows(hidden.astype(jnp.float32)).astype(jnp.bfloat16)
    state_f = state.astype(jnp.float32)
    projected = jnp.dot(state, in_proj.reshape(D, HEADS * 3 * HD), preferred_element_type=jnp.float32)
    projected = projected.reshape(TOKENS, HEADS, 3, HD)
    key_part = projected[:, :, 1].astype(jnp.bfloat16)
    value_part = projected[:, :, 2].astype(jnp.bfloat16)
    queries = (unit_rows(projected[:, :, 0]) * score_scale).astype(jnp.bfloat16)
    keys_unit = (unit_rows(key_part.astype(jnp.float32)) * score_scale).astype(jnp.bfloat16)
    heads_out = attend(queries, keys_unit, value_part, segment_ids)
    heads_flat = heads_out.reshape(TOKENS, HEADS * HD)
    head_cols = HEADS // N_TENSOR * HD

    def attn_term(group):
        left = lax.dynamic_slice_in_dim(heads_flat, group * head_cols, head_cols, 1)
        right = lax.dynamic_slice_in_dim(out_proj, group * head_cols, head_cols, 0)
        return jnp.dot(left, right, preferred_element_type=jnp.float32)
    attn_sum = grouped_sum(attn_term, N_TENSOR)
    mid = unit_rows(state_f + step_rates[0] * (unit_rows(attn_sum) - state_f))
    mid_b = mid.astype(jnp.bfloat16)
    unit_cols = FF // N_TENSOR

    def mlp_term(group):
        weights_uv = lax.dynamic_slice_in_dim(up_proj, group * unit_cols, unit_cols, 2)
        scales = lax.dynamic_slice_in_dim(mlp_scale, group * unit_cols, unit_cols, 1)
        both = jnp.dot(mid_b, weights_uv.reshape(D, 2 * unit_cols), preferred_element_type=jnp.float32)
        both = both.reshape(TOKENS, 2, unit_cols)
        act = (both[:, 0] * scales[0] * jax.nn.silu(both[:, 1] * scales[1] * math.sqrt(D))).astype(jnp.bfloat16)
        rows_down = lax.dynamic_slice_in_dim(down_proj, group * unit_cols, unit_cols, 0)
        return jnp.dot(act, rows_down, preferred_element_type=jnp.float32)
    mlp_sum = grouped_sum(mlp_term, N_TENSOR)
    final = unit_rows(mid + step_rates[1] * (unit_rows(mlp_sum) - mid))
    out_state = (math.sqrt(D) * final).astype(jnp.bfloat16)
    key_value = jnp.stack([key_part, value_part], axis=2).reshape(PAGES, PAGE, 2 * HEADS * HD)
    page_cache = jnp.zeros((PAGES, PAGE, 2 * HEADS * HD), jnp.bfloat16).at[page_slot].set(key_value)
    return (out_state, page_cache)
```

```python
import math

import jax
import jax.numpy as jnp
from jax import lax
from jax.sharding import PartitionSpec as P

PAGE = 128


EPSILON = 1e-06
NEG_LARGE = -1e30


def unit_rows(matrix):
    return matrix * lax.rsqrt(jnp.sum(matrix * matrix, axis=-1, keepdims=True) + EPSILON)


def gather_rows(part, axis):
    count = lax.axis_size(axis)
    index = lax.axis_index(axis)
    parts = [part]
    for shift in range(1, count):
        pairs = [(j, (j + shift) % count) for j in range(count)]
        parts.append(lax.ppermute(part, axis, pairs))
    stacked = jnp.stack(parts)
    order = (index - jnp.arange(count)) % count
    return jnp.zeros_like(stacked).at[order].set(stacked).reshape(-1, *part.shape[1:])


def scatter_sum(whole, axis):
    count = lax.axis_size(axis)
    index = lax.axis_index(axis)
    blocks = whole.reshape(count, whole.shape[0] // count, *whole.shape[1:])
    total = lax.dynamic_index_in_dim(blocks, index, 0, keepdims=False).astype(jnp.float32)
    for shift in range(1, count):
        pairs = [(j, (j + shift) % count) for j in range(count)]
        send = lax.dynamic_index_in_dim(blocks, (index + shift) % count, 0, keepdims=False)
        total = total + lax.ppermute(send, axis, pairs).astype(jnp.float32)
    return total


def body(
    hidden,
    segment_ids,
    page_slot,
    in_proj,
    out_proj,
    up_proj,
    down_proj,
    score_scale,
    mlp_scale,
    step_rates,
):
    seq_count = lax.axis_size("seq")
    seq_index = lax.axis_index("seq")
    local_tokens = segment_ids.shape[0]
    heads_dev, head_dim = score_scale.shape
    model_width = hidden.shape[1]
    hidden_dev = down_proj.shape[0]
    pages_dev = local_tokens // PAGE
    channels = heads_dev * 2 * head_dim
    state_own = unit_rows(hidden.astype(jnp.float32)).astype(jnp.bfloat16)
    gathered_state = gather_rows(state_own, "tensor")
    projected = jnp.dot(
        gathered_state,
        in_proj.reshape(model_width, heads_dev * 3 * head_dim),
        preferred_element_type=jnp.float32,
    )
    projected = projected.reshape(local_tokens, heads_dev, 3, head_dim)
    queries = (unit_rows(projected[:, :, 0]) * score_scale).astype(jnp.bfloat16)
    key_value = jnp.stack([projected[:, :, 1], projected[:, :, 2]], axis=2).astype(jnp.bfloat16)
    key_value = key_value.reshape(local_tokens, channels)
    first_token = seq_index * local_tokens
    query_index = first_token + jnp.arange(local_tokens, dtype=jnp.int32)
    first_segment = segment_ids[0]
    last_token = first_token + local_tokens - 1
    score_factor = math.sqrt(head_dim)

    def attend_block(running, block_parts):
        key_block, key_segs, key_start = block_parts

        def compute(state_in):
            top_score, weight_sum, weighted = state_in
            split_kv = key_block.reshape(-1, heads_dev, 2, head_dim)
            keys_unit = (unit_rows(split_kv[:, :, 0].astype(jnp.float32)) * score_scale).astype(
                jnp.bfloat16
            )
            scores = score_factor * jnp.einsum(
                "qhd,khd->hqk", queries, keys_unit, preferred_element_type=jnp.float32
            )
            key_index = key_start + jnp.arange(key_block.shape[0], dtype=jnp.int32)
            allowed = (segment_ids[:, None] == key_segs[None, :]) & (
                key_index[None, :] <= query_index[:, None]
            )
            scores = jnp.where(allowed[None], scores, NEG_LARGE)
            new_top = jnp.maximum(top_score, jnp.max(scores, axis=-1))
            weights = jnp.where(allowed[None], jnp.exp(scores - new_top[:, :, None]), 0.0)
            rescale = jnp.exp(top_score - new_top)
            new_sum = weight_sum * rescale + jnp.sum(weights, axis=-1)
            update = jnp.einsum(
                "hqk,khd->qhd",
                weights.astype(jnp.bfloat16),
                split_kv[:, :, 1],
                preferred_element_type=jnp.float32,
            )
            new_weighted = weighted * jnp.transpose(rescale)[:, :, None] + update
            return (new_top, new_sum, new_weighted)

        useful = (key_segs[-1] >= first_segment) & (key_start <= last_token)
        return (lax.cond(useful, compute, lambda state_in: state_in, running), None)

    start_state = (
        jnp.full((heads_dev, local_tokens), NEG_LARGE, jnp.float32),
        jnp.zeros((heads_dev, local_tokens), jnp.float32),
        jnp.zeros((local_tokens, heads_dev, head_dim), jnp.float32),
    )
    kv_piece = lax.all_gather(key_value, "seq", axis=0, tiled=True)
    seg_piece = lax.all_gather(segment_ids, "seq", axis=0, tiled=True)
    piece_rows = kv_piece.shape[0]
    block_rows = 512
    blocks = piece_rows // block_rows
    starts = block_rows * jnp.arange(blocks, dtype=jnp.int32)
    block_parts = (
        kv_piece.reshape(blocks, block_rows, channels),
        seg_piece.reshape(blocks, block_rows),
        starts,
    )
    attn_state = lax.scan(attend_block, start_state[:3], block_parts)[0]
    heads_out = (attn_state[2] / jnp.transpose(attn_state[1])[:, :, None]).astype(jnp.bfloat16)
    heads_flat = heads_out.reshape(local_tokens, heads_dev * head_dim)
    slots_dev = page_slot.shape[0] // seq_count
    my_slots = seq_index * slots_dev + jnp.arange(slots_dev, dtype=jnp.int32)
    page_ids = jnp.arange(page_slot.shape[0], dtype=jnp.int32)
    source_page = jnp.sum(
        jnp.where(page_slot[None, :] == my_slots[:, None], page_ids[None, :], 0), axis=1
    )
    all_pages = kv_piece.reshape(page_slot.shape[0], PAGE, channels)
    page_cache = jnp.take(all_pages, source_page, axis=0)
    chosen = heads_flat
    attn_own = scatter_sum(
        jnp.dot(chosen, out_proj, preferred_element_type=jnp.float32).astype(jnp.bfloat16),
        "tensor",
    )
    state_f = state_own.astype(jnp.float32)
    middle = unit_rows(state_f + step_rates[0] * (unit_rows(attn_own) - state_f))
    mid_rows = gather_rows(middle.astype(jnp.bfloat16), "tensor")
    both = jnp.einsum("td,dkf->tkf", mid_rows, up_proj, preferred_element_type=jnp.float32)
    act = (
        both[:, 0] * mlp_scale[0] * jax.nn.silu(both[:, 1] * mlp_scale[1] * math.sqrt(model_width))
    ).astype(jnp.bfloat16)
    chosen = act
    mlp_own = scatter_sum(
        jnp.dot(chosen, down_proj, preferred_element_type=jnp.float32).astype(jnp.bfloat16),
        "tensor",
    )
    final = unit_rows(middle + step_rates[1] * (unit_rows(mlp_own) - middle))
    out_state = (math.sqrt(model_width) * final).astype(jnp.bfloat16)
    return (out_state, page_cache)


def solution(mesh):
    return jax.shard_map(
        body,
        mesh=mesh,
        in_specs=(
            P(("seq", "tensor"), None),
            P("seq"),
            P(),
            P(None, "tensor", None),
            P("tensor", None),
            P(None, None, "tensor"),
            P("tensor", None),
            P("tensor", None),
            P(None, "tensor"),
            P(),
        ),
        out_specs=(P(("seq", "tensor"), None), P("seq", None, "tensor")),
        check_vma=False,
    )
```

```python
import math

import jax
import jax.numpy as jnp
from jax import lax
from jax.sharding import PartitionSpec as P

PAGE = 128


EPSILON = 1e-06
NEG_LARGE = -1e30


def unit_rows(matrix):
    return matrix * lax.rsqrt(jnp.sum(matrix * matrix, axis=-1, keepdims=True) + EPSILON)


def gather_rows(part, axis):
    count = lax.axis_size(axis)
    index = lax.axis_index(axis)
    parts = [part]
    for shift in range(1, count):
        pairs = [(j, (j + shift) % count) for j in range(count)]
        parts.append(lax.ppermute(part, axis, pairs))
    stacked = jnp.stack(parts)
    order = (index - jnp.arange(count)) % count
    return jnp.zeros_like(stacked).at[order].set(stacked).reshape(-1, *part.shape[1:])


def scatter_sum(whole, axis):
    count = lax.axis_size(axis)
    index = lax.axis_index(axis)
    blocks = whole.reshape(count, whole.shape[0] // count, *whole.shape[1:])
    total = lax.dynamic_index_in_dim(blocks, index, 0, keepdims=False).astype(jnp.float32)
    for shift in range(1, count):
        pairs = [(j, (j + shift) % count) for j in range(count)]
        send = lax.dynamic_index_in_dim(blocks, (index + shift) % count, 0, keepdims=False)
        total = total + lax.ppermute(send, axis, pairs).astype(jnp.float32)
    return total


def body(
    hidden,
    segment_ids,
    page_slot,
    in_proj,
    out_proj,
    up_proj,
    down_proj,
    score_scale,
    mlp_scale,
    step_rates,
):
    seq_count = lax.axis_size("seq")
    seq_index = lax.axis_index("seq")
    local_tokens = segment_ids.shape[0]
    heads_dev, head_dim = score_scale.shape
    model_width = hidden.shape[1]
    hidden_dev = down_proj.shape[0]
    pages_dev = local_tokens // PAGE
    channels = heads_dev * 2 * head_dim
    state_own = unit_rows(hidden.astype(jnp.float32)).astype(jnp.bfloat16)
    gathered_state = gather_rows(state_own, "tensor")
    projected = jnp.dot(
        gathered_state,
        in_proj.reshape(model_width, heads_dev * 3 * head_dim),
        preferred_element_type=jnp.float32,
    )
    projected = projected.reshape(local_tokens, heads_dev, 3, head_dim)
    queries = (unit_rows(projected[:, :, 0]) * score_scale).astype(jnp.bfloat16)
    key_value = jnp.stack([projected[:, :, 1], projected[:, :, 2]], axis=2).astype(jnp.bfloat16)
    key_value = key_value.reshape(local_tokens, channels)
    first_token = seq_index * local_tokens
    query_index = first_token + jnp.arange(local_tokens, dtype=jnp.int32)
    first_segment = segment_ids[0]
    last_token = first_token + local_tokens - 1
    score_factor = math.sqrt(head_dim)

    def attend_block(running, block_parts):
        key_block, key_segs, key_start = block_parts

        def compute(state_in):
            top_score, weight_sum, weighted = state_in
            split_kv = key_block.reshape(-1, heads_dev, 2, head_dim)
            keys_unit = (unit_rows(split_kv[:, :, 0].astype(jnp.float32)) * score_scale).astype(
                jnp.bfloat16
            )
            scores = score_factor * jnp.einsum(
                "qhd,khd->hqk", queries, keys_unit, preferred_element_type=jnp.float32
            )
            key_index = key_start + jnp.arange(key_block.shape[0], dtype=jnp.int32)
            allowed = (segment_ids[:, None] == key_segs[None, :]) & (
                key_index[None, :] <= query_index[:, None]
            )
            scores = jnp.where(allowed[None], scores, NEG_LARGE)
            new_top = jnp.maximum(top_score, jnp.max(scores, axis=-1))
            weights = jnp.where(allowed[None], jnp.exp(scores - new_top[:, :, None]), 0.0)
            rescale = jnp.exp(top_score - new_top)
            new_sum = weight_sum * rescale + jnp.sum(weights, axis=-1)
            update = jnp.einsum(
                "hqk,khd->qhd",
                weights.astype(jnp.bfloat16),
                split_kv[:, :, 1],
                preferred_element_type=jnp.float32,
            )
            new_weighted = weighted * jnp.transpose(rescale)[:, :, None] + update
            return (new_top, new_sum, new_weighted)

        useful = (key_segs[-1] >= first_segment) & (key_start <= last_token)
        return (lax.cond(useful, compute, lambda state_in: state_in, running), None)

    start_state = (
        jnp.full((heads_dev, local_tokens), NEG_LARGE, jnp.float32),
        jnp.zeros((heads_dev, local_tokens), jnp.float32),
        jnp.zeros((local_tokens, heads_dev, head_dim), jnp.float32),
    )
    seg_rows = -(-local_tokens // channels)
    seg_flat = jnp.pad(segment_ids, (0, seg_rows * channels - local_tokens))
    kv_ext = jnp.concatenate(
        [key_value, seg_flat.astype(jnp.bfloat16).reshape(seg_rows, channels)], axis=0
    )
    gathered = lax.all_gather(kv_ext, "seq", axis=0, tiled=False)
    kv_piece = gathered[:, :local_tokens].reshape(seq_count * local_tokens, channels)
    seg_piece = (
        gathered[:, local_tokens:].reshape(seq_count, seg_rows * channels)[:, :local_tokens]
        .reshape(-1)
        .astype(jnp.int32)
    )
    piece_rows = kv_piece.shape[0]
    block_rows = 512
    blocks = piece_rows // block_rows
    starts = block_rows * jnp.arange(blocks, dtype=jnp.int32)
    block_parts = (
        kv_piece.reshape(blocks, block_rows, channels),
        seg_piece.reshape(blocks, block_rows),
        starts,
    )
    attn_state = lax.scan(attend_block, start_state[:3], block_parts)[0]
    heads_out = (attn_state[2] / jnp.transpose(attn_state[1])[:, :, None]).astype(jnp.bfloat16)
    heads_flat = heads_out.reshape(local_tokens, heads_dev * head_dim)
    slots_dev = page_slot.shape[0] // seq_count
    my_slots = seq_index * slots_dev + jnp.arange(slots_dev, dtype=jnp.int32)
    page_ids = jnp.arange(page_slot.shape[0], dtype=jnp.int32)
    source_page = jnp.sum(
        jnp.where(page_slot[None, :] == my_slots[:, None], page_ids[None, :], 0), axis=1
    )
    all_pages = kv_piece.reshape(page_slot.shape[0], PAGE, channels)
    page_cache = jnp.take(all_pages, source_page, axis=0)
    chosen = heads_flat
    attn_own = scatter_sum(
        jnp.dot(chosen, out_proj, preferred_element_type=jnp.float32).astype(jnp.bfloat16),
        "tensor",
    )
    state_f = state_own.astype(jnp.float32)
    middle = unit_rows(state_f + step_rates[0] * (unit_rows(attn_own) - state_f))
    mid_rows = gather_rows(middle.astype(jnp.bfloat16), "tensor")
    both = jnp.einsum("td,dkf->tkf", mid_rows, up_proj, preferred_element_type=jnp.float32)
    act = (
        both[:, 0] * mlp_scale[0] * jax.nn.silu(both[:, 1] * mlp_scale[1] * math.sqrt(model_width))
    ).astype(jnp.bfloat16)
    chosen = act
    mlp_own = scatter_sum(
        jnp.dot(chosen, down_proj, preferred_element_type=jnp.float32).astype(jnp.bfloat16),
        "tensor",
    )
    final = unit_rows(middle + step_rates[1] * (unit_rows(mlp_own) - middle))
    out_state = (math.sqrt(model_width) * final).astype(jnp.bfloat16)
    return (out_state, page_cache)


def solution(mesh):
    return jax.shard_map(
        body,
        mesh=mesh,
        in_specs=(
            P(("seq", "tensor"), None),
            P("seq"),
            P(),
            P(None, "tensor", None),
            P("tensor", None),
            P(None, None, "tensor"),
            P("tensor", None),
            P("tensor", None),
            P(None, "tensor"),
            P(),
        ),
        out_specs=(P(("seq", "tensor"), None), P("seq", None, "tensor")),
        check_vma=False,
    )
```

```python
import functools
import math

import jax
import jax.numpy as jnp
from jax import lax
from jax.experimental import pallas as pl
from jax.experimental.pallas import tpu as pltpu
from jax.sharding import PartitionSpec as P

PAGE = 128


EPSILON = 1e-06
NEG_LARGE = -1e30


def unit_rows(matrix):
    return matrix * lax.rsqrt(jnp.sum(matrix * matrix, axis=-1, keepdims=True) + EPSILON)


def gather_rows(part, axis):
    count = lax.axis_size(axis)
    index = lax.axis_index(axis)
    parts = [part]
    for shift in range(1, count):
        pairs = [(j, (j + shift) % count) for j in range(count)]
        parts.append(lax.ppermute(part, axis, pairs))
    stacked = jnp.stack(parts)
    order = (index - jnp.arange(count)) % count
    return jnp.zeros_like(stacked).at[order].set(stacked).reshape(-1, *part.shape[1:])


def scatter_sum(whole, axis):
    count = lax.axis_size(axis)
    index = lax.axis_index(axis)
    blocks = whole.reshape(count, whole.shape[0] // count, *whole.shape[1:])
    total = lax.dynamic_index_in_dim(blocks, index, 0, keepdims=False).astype(jnp.float32)
    for shift in range(1, count):
        pairs = [(j, (j + shift) % count) for j in range(count)]
        send = lax.dynamic_index_in_dim(blocks, (index + shift) % count, 0, keepdims=False)
        total = total + lax.ppermute(send, axis, pairs).astype(jnp.float32)
    return total


Q_TILE = 256
K_TILE = 256


def attend_kernel(bounds_ref, q_ref, k_ref, v_ref, qseg_ref, kseg_ref, out_ref, *, factor):
    heads, rows, width = q_ref.shape
    tiles = rows // Q_TILE
    first = bounds_ref[2 * tiles]
    for head in range(heads):
        for tile in range(tiles):
            q_tile = q_ref[head, tile * Q_TILE : (tile + 1) * Q_TILE, :]
            q_seg = qseg_ref[tile * Q_TILE : (tile + 1) * Q_TILE, :]
            q_pos = first + tile * Q_TILE + lax.broadcasted_iota(jnp.int32, (Q_TILE, K_TILE), 0)

            def step(block, carry, q_tile=q_tile, q_seg=q_seg, q_pos=q_pos, head=head):
                top, total, acc = carry
                key_at = pl.multiple_of(block * K_TILE, K_TILE)
                k_blk = k_ref[head, pl.ds(key_at, K_TILE), :]
                v_blk = v_ref[head, pl.ds(key_at, K_TILE), :]
                k_seg = kseg_ref[:, pl.ds(key_at, K_TILE)]
                scores = factor * lax.dot_general(
                    q_tile, k_blk, (((1,), (1,)), ((), ())), preferred_element_type=jnp.float32
                )
                k_pos = key_at + lax.broadcasted_iota(jnp.int32, (Q_TILE, K_TILE), 1)
                allowed = (q_seg == k_seg) & (k_pos <= q_pos)
                scores = jnp.where(allowed, scores, NEG_LARGE)
                new_top = jnp.maximum(top, jnp.max(scores, axis=1, keepdims=True))
                weights = jnp.where(allowed, jnp.exp(scores - new_top), 0.0)
                rescale = jnp.exp(top - new_top)
                new_total = total * rescale + jnp.sum(weights, axis=1, keepdims=True)
                update = jnp.dot(
                    weights.astype(jnp.bfloat16), v_blk, preferred_element_type=jnp.float32
                )
                return (new_top, new_total, acc * rescale + update)

            start = (
                jnp.full((Q_TILE, 1), NEG_LARGE, jnp.float32),
                jnp.zeros((Q_TILE, 1), jnp.float32),
                jnp.zeros((Q_TILE, width), jnp.float32),
            )
            top, total, acc = lax.fori_loop(
                bounds_ref[tile], bounds_ref[tiles + tile] + 1, step, start
            )
            out_ref[head, tile * Q_TILE : (tile + 1) * Q_TILE, :] = (acc / total).astype(
                out_ref.dtype
            )


def flash_attend(bounds, queries_t, keys_t, values_t, query_segs, key_segs, factor):
    heads, rows, width = queries_t.shape
    keys = keys_t.shape[1]
    vmem = pl.BlockSpec(memory_space=pltpu.VMEM)
    return pl.pallas_call(
        functools.partial(attend_kernel, factor=factor),
        out_shape=jax.ShapeDtypeStruct((heads, rows, width), jnp.bfloat16),
        in_specs=[pl.BlockSpec(memory_space=pltpu.SMEM)] + [vmem] * 5,
        out_specs=vmem,
        cost_estimate=pl.CostEstimate(
            flops=4 * heads * rows * keys * width,
            transcendentals=heads * rows * keys,
            bytes_accessed=2 * heads * keys * width * 2,
        ),
    )(bounds, queries_t, keys_t, values_t, query_segs, key_segs)


def body(
    hidden,
    segment_ids,
    page_slot,
    in_proj,
    out_proj,
    up_proj,
    down_proj,
    score_scale,
    mlp_scale,
    step_rates,
):
    seq_count = lax.axis_size("seq")
    seq_index = lax.axis_index("seq")
    local_tokens = segment_ids.shape[0]
    heads_dev, head_dim = score_scale.shape
    model_width = hidden.shape[1]
    hidden_dev = down_proj.shape[0]
    pages_dev = local_tokens // PAGE
    channels = heads_dev * 2 * head_dim
    state_own = unit_rows(hidden.astype(jnp.float32)).astype(jnp.bfloat16)
    gathered_state = gather_rows(state_own, "tensor")
    projected = jnp.dot(
        gathered_state,
        in_proj.reshape(model_width, heads_dev * 3 * head_dim),
        preferred_element_type=jnp.float32,
    )
    projected = projected.reshape(local_tokens, heads_dev, 3, head_dim)
    queries = (unit_rows(projected[:, :, 0]) * score_scale).astype(jnp.bfloat16)
    key_value = jnp.stack([projected[:, :, 1], projected[:, :, 2]], axis=2).astype(jnp.bfloat16)
    key_value = key_value.reshape(local_tokens, channels)
    first_token = seq_index * local_tokens
    seg_rows = -(-local_tokens // channels)
    seg_flat = jnp.pad(segment_ids, (0, seg_rows * channels - local_tokens))
    kv_ext = jnp.concatenate(
        [key_value, seg_flat.astype(jnp.bfloat16).reshape(seg_rows, channels)], axis=0
    )
    gathered = lax.all_gather(kv_ext, "seq", axis=0, tiled=False)
    kv_piece = gathered[:, :local_tokens].reshape(seq_count * local_tokens, channels)
    seg_piece = (
        gathered[:, local_tokens:].reshape(seq_count, seg_rows * channels)[:, :local_tokens]
        .reshape(-1)
        .astype(jnp.int32)
    )
    piece_rows = kv_piece.shape[0]
    split_kv = kv_piece.reshape(piece_rows, heads_dev, 2, head_dim)
    keys_unit = (unit_rows(split_kv[:, :, 0].astype(jnp.float32)) * score_scale).astype(
        jnp.bfloat16
    )
    keys_t = jnp.transpose(keys_unit, (1, 0, 2))
    values_t = jnp.transpose(split_kv[:, :, 1], (1, 0, 2))
    queries_t = jnp.transpose(queries, (1, 0, 2))
    tiles = local_tokens // Q_TILE
    tile_first = first_token + Q_TILE * jnp.arange(tiles, dtype=jnp.int32)
    tile_seg = segment_ids.reshape(tiles, Q_TILE)[:, 0]
    block_last_seg = seg_piece.reshape(piece_rows // K_TILE, K_TILE)[:, -1]
    block_lo = jnp.sum(
        (block_last_seg[None, :] < tile_seg[:, None]).astype(jnp.int32), axis=1
    )
    block_hi = (tile_first + Q_TILE - 1) // K_TILE
    bounds = jnp.concatenate([block_lo, block_hi, first_token[None]]).astype(jnp.int32)
    heads_t = flash_attend(
        bounds,
        queries_t,
        keys_t,
        values_t,
        segment_ids.reshape(local_tokens, 1),
        seg_piece.reshape(1, piece_rows),
        math.sqrt(head_dim),
    )
    heads_out = jnp.transpose(heads_t, (1, 0, 2))
    heads_flat = heads_out.reshape(local_tokens, heads_dev * head_dim)
    slots_dev = page_slot.shape[0] // seq_count
    my_slots = seq_index * slots_dev + jnp.arange(slots_dev, dtype=jnp.int32)
    page_ids = jnp.arange(page_slot.shape[0], dtype=jnp.int32)
    source_page = jnp.sum(
        jnp.where(page_slot[None, :] == my_slots[:, None], page_ids[None, :], 0), axis=1
    )
    all_pages = kv_piece.reshape(page_slot.shape[0], PAGE, channels)
    page_cache = jnp.take(all_pages, source_page, axis=0)
    chosen = heads_flat
    attn_own = scatter_sum(
        jnp.dot(chosen, out_proj, preferred_element_type=jnp.float32).astype(jnp.bfloat16),
        "tensor",
    )
    state_f = state_own.astype(jnp.float32)
    middle = unit_rows(state_f + step_rates[0] * (unit_rows(attn_own) - state_f))
    mid_rows = gather_rows(middle.astype(jnp.bfloat16), "tensor")
    both = jnp.einsum("td,dkf->tkf", mid_rows, up_proj, preferred_element_type=jnp.float32)
    act = (
        both[:, 0] * mlp_scale[0] * jax.nn.silu(both[:, 1] * mlp_scale[1] * math.sqrt(model_width))
    ).astype(jnp.bfloat16)
    chosen = act
    mlp_own = scatter_sum(
        jnp.dot(chosen, down_proj, preferred_element_type=jnp.float32).astype(jnp.bfloat16),
        "tensor",
    )
    final = unit_rows(middle + step_rates[1] * (unit_rows(mlp_own) - middle))
    out_state = (math.sqrt(model_width) * final).astype(jnp.bfloat16)
    return (out_state, page_cache)


def solution(mesh):
    return jax.shard_map(
        body,
        mesh=mesh,
        in_specs=(
            P(("seq", "tensor"), None),
            P("seq"),
            P(),
            P(None, "tensor", None),
            P("tensor", None),
            P(None, None, "tensor"),
            P("tensor", None),
            P("tensor", None),
            P(None, "tensor"),
            P(),
        ),
        out_specs=(P(("seq", "tensor"), None), P("seq", None, "tensor")),
        check_vma=False,
    )
```

```python
import functools
import math

import jax
import jax.numpy as jnp
from jax import lax
from jax.experimental import pallas as pl
from jax.experimental.pallas import tpu as pltpu
from jax.sharding import PartitionSpec as P

PAGE = 128


EPSILON = 1e-06
NEG_LARGE = -1e30


def unit_rows(matrix):
    return matrix * lax.rsqrt(jnp.sum(matrix * matrix, axis=-1, keepdims=True) + EPSILON)


def gather_rows(part, axis):
    count = lax.axis_size(axis)
    index = lax.axis_index(axis)
    parts = [part]
    for shift in range(1, count):
        pairs = [(j, (j + shift) % count) for j in range(count)]
        parts.append(lax.ppermute(part, axis, pairs))
    stacked = jnp.stack(parts)
    order = (index - jnp.arange(count)) % count
    return jnp.zeros_like(stacked).at[order].set(stacked).reshape(-1, *part.shape[1:])


def scatter_sum(whole, axis):
    count = lax.axis_size(axis)
    index = lax.axis_index(axis)
    blocks = whole.reshape(count, whole.shape[0] // count, *whole.shape[1:])
    total = lax.dynamic_index_in_dim(blocks, index, 0, keepdims=False).astype(jnp.float32)
    for shift in range(1, count):
        pairs = [(j, (j + shift) % count) for j in range(count)]
        send = lax.dynamic_index_in_dim(blocks, (index + shift) % count, 0, keepdims=False)
        total = total + lax.ppermute(send, axis, pairs).astype(jnp.float32)
    return total


Q_TILE = 256
K_TILE = 256


def attend_kernel(
    bounds_ref, proj_ref, kv_ref, scale_ref, qseg_ref, kseg_ref, out_ref, *, factor, half
):
    rows = qseg_ref.shape[0]
    heads = scale_ref.shape[0]
    lanes = 2 * half
    shard_blocks = (kv_ref.shape[1] - kv_ref.shape[1] % K_TILE) // K_TILE
    tiles = rows // Q_TILE
    first = bounds_ref[2 * tiles]
    key_lane = lax.broadcasted_iota(jnp.int32, (K_TILE, lanes), 1)
    for head in range(heads):
        scale = scale_ref[head]
        for tile in range(tiles):
            q_raw = proj_ref[tile * Q_TILE : (tile + 1) * Q_TILE, head * 2 * lanes : head * 2 * lanes + lanes]
            q_tile = (
                q_raw * lax.rsqrt(jnp.sum(q_raw * q_raw, axis=1, keepdims=True) + EPSILON) * scale
            ).astype(jnp.bfloat16)
            q_seg = qseg_ref[tile * Q_TILE : (tile + 1) * Q_TILE, :]
            q_pos = first + tile * Q_TILE + lax.broadcasted_iota(jnp.int32, (Q_TILE, K_TILE), 0)

            def step(block, carry, q_tile=q_tile, q_seg=q_seg, q_pos=q_pos, head=head, scale=scale):
                top, total, acc = carry
                shard = block // shard_blocks
                row_at = pl.multiple_of((block % shard_blocks) * K_TILE, K_TILE)
                key_at = pl.multiple_of(block * K_TILE, K_TILE)
                kv_blk = kv_ref[shard, pl.ds(row_at, K_TILE), head * lanes : (head + 1) * lanes]
                kv_f = kv_blk.astype(jnp.float32)
                k_sq = jnp.where(key_lane < half, kv_f * kv_f, 0.0)
                k_unit = (
                    kv_f * lax.rsqrt(jnp.sum(k_sq, axis=1, keepdims=True) + EPSILON) * scale
                ).astype(jnp.bfloat16)
                k_seg = kseg_ref[:, pl.ds(key_at, K_TILE)]
                scores = factor * lax.dot_general(
                    q_tile, k_unit, (((1,), (1,)), ((), ())), preferred_element_type=jnp.float32
                )
                k_pos = key_at + lax.broadcasted_iota(jnp.int32, (Q_TILE, K_TILE), 1)
                allowed = (q_seg == k_seg) & (k_pos <= q_pos)
                scores = jnp.where(allowed, scores, NEG_LARGE)
                new_top = jnp.maximum(top, jnp.max(scores, axis=1, keepdims=True))
                weights = jnp.where(allowed, jnp.exp(scores - new_top), 0.0)
                rescale = jnp.exp(top - new_top)
                new_total = total * rescale + jnp.sum(weights, axis=1, keepdims=True)
                update = jnp.dot(
                    weights.astype(jnp.bfloat16), kv_blk, preferred_element_type=jnp.float32
                )
                return (new_top, new_total, acc * rescale + update)

            start = (
                jnp.full((Q_TILE, 1), NEG_LARGE, jnp.float32),
                jnp.zeros((Q_TILE, 1), jnp.float32),
                jnp.zeros((Q_TILE, lanes), jnp.float32),
            )
            top, total, acc = lax.fori_loop(
                bounds_ref[tile], bounds_ref[tiles + tile] + 1, step, start
            )
            out_ref[tile * Q_TILE : (tile + 1) * Q_TILE, head * lanes : (head + 1) * lanes] = (
                acc / total
            ).astype(out_ref.dtype)


def flash_attend(bounds, proj, gathered, scale_pad, query_segs, key_segs, factor, half):
    rows = query_segs.shape[0]
    heads, _, lanes = scale_pad.shape
    keys = key_segs.shape[1]
    vmem = pl.BlockSpec(memory_space=pltpu.VMEM)
    return pl.pallas_call(
        functools.partial(attend_kernel, factor=factor, half=half),
        out_shape=jax.ShapeDtypeStruct((rows, heads * lanes), jnp.bfloat16),
        in_specs=[pl.BlockSpec(memory_space=pltpu.SMEM)] + [vmem] * 5,
        out_specs=vmem,
        cost_estimate=pl.CostEstimate(
            flops=4 * heads * rows * keys * lanes,
            transcendentals=heads * rows * keys,
            bytes_accessed=heads * keys * lanes * 2,
        ),
    )(bounds, proj, gathered, scale_pad, query_segs, key_segs)


def body(
    hidden,
    segment_ids,
    page_slot,
    in_proj,
    out_proj,
    up_proj,
    down_proj,
    score_scale,
    mlp_scale,
    step_rates,
):
    seq_count = lax.axis_size("seq")
    seq_index = lax.axis_index("seq")
    local_tokens = segment_ids.shape[0]
    heads_dev, head_dim = score_scale.shape
    model_width = hidden.shape[1]
    hidden_dev = down_proj.shape[0]
    pages_dev = local_tokens // PAGE
    channels = heads_dev * 2 * head_dim
    state_own = unit_rows(hidden.astype(jnp.float32)).astype(jnp.bfloat16)
    gathered_state = gather_rows(state_own, "tensor")
    lanes = 2 * head_dim
    weight_pad = jnp.concatenate(
        [
            in_proj[:, :, :head_dim],
            jnp.zeros((model_width, heads_dev, head_dim), in_proj.dtype),
            in_proj[:, :, head_dim:],
        ],
        axis=2,
    ).reshape(model_width, heads_dev * 2 * lanes)
    projected = jnp.dot(gathered_state, weight_pad, preferred_element_type=jnp.float32)
    key_value = jnp.concatenate(
        [projected[:, (2 * h + 1) * lanes : (2 * h + 2) * lanes] for h in range(heads_dev)],
        axis=1,
    ).astype(jnp.bfloat16)
    first_token = seq_index * local_tokens
    seg_rows = -(-local_tokens // channels)
    seg_flat = jnp.pad(segment_ids, (0, seg_rows * channels - local_tokens))
    kv_ext = jnp.concatenate(
        [key_value, seg_flat.astype(jnp.bfloat16).reshape(seg_rows, channels)], axis=0
    )
    gathered = lax.all_gather(kv_ext, "seq", axis=0, tiled=False)
    seg_piece = (
        gathered[:, local_tokens:].reshape(seq_count, seg_rows * channels)[:, :local_tokens]
        .reshape(-1)
        .astype(jnp.int32)
    )
    piece_rows = seq_count * local_tokens
    scale_pad = jnp.pad(score_scale, ((0, 0), (0, lanes - head_dim))).reshape(heads_dev, 1, lanes)
    tiles = local_tokens // Q_TILE
    tile_first = first_token + Q_TILE * jnp.arange(tiles, dtype=jnp.int32)
    tile_seg = segment_ids.reshape(tiles, Q_TILE)[:, 0]
    block_last_seg = seg_piece.reshape(piece_rows // K_TILE, K_TILE)[:, -1]
    block_lo = jnp.sum(
        (block_last_seg[None, :] < tile_seg[:, None]).astype(jnp.int32), axis=1
    )
    block_hi = (tile_first + Q_TILE - 1) // K_TILE
    bounds = jnp.concatenate([block_lo, block_hi, first_token[None]]).astype(jnp.int32)
    heads_pad = flash_attend(
        bounds,
        projected,
        gathered,
        scale_pad,
        segment_ids.reshape(local_tokens, 1),
        seg_piece.reshape(1, piece_rows),
        math.sqrt(head_dim),
        head_dim,
    )
    out_pad = jnp.pad(
        out_proj.reshape(heads_dev, head_dim, model_width), ((0, 0), (head_dim, 0), (0, 0))
    ).reshape(heads_dev * lanes, model_width)
    slots_dev = page_slot.shape[0] // seq_count
    my_slots = seq_index * slots_dev + jnp.arange(slots_dev, dtype=jnp.int32)
    page_ids = jnp.arange(page_slot.shape[0], dtype=jnp.int32)
    source_page = jnp.sum(
        jnp.where(page_slot[None, :] == my_slots[:, None], page_ids[None, :], 0), axis=1
    )
    page_cache = jnp.stack(
        [
            lax.dynamic_slice(
                gathered,
                (source_page[j] // pages_dev, (source_page[j] % pages_dev) * PAGE, 0),
                (1, PAGE, channels),
            )[0]
            for j in range(slots_dev)
        ]
    )
    chosen = heads_pad
    attn_own = scatter_sum(
        jnp.dot(chosen, out_pad, preferred_element_type=jnp.float32).astype(jnp.bfloat16),
        "tensor",
    )
    state_f = state_own.astype(jnp.float32)
    middle = unit_rows(state_f + step_rates[0] * (unit_rows(attn_own) - state_f))
    mid_rows = gather_rows(middle.astype(jnp.bfloat16), "tensor")
    both = jnp.einsum("td,dkf->tkf", mid_rows, up_proj, preferred_element_type=jnp.float32)
    act = (
        both[:, 0] * mlp_scale[0] * jax.nn.silu(both[:, 1] * mlp_scale[1] * math.sqrt(model_width))
    ).astype(jnp.bfloat16)
    chosen = act
    mlp_own = scatter_sum(
        jnp.dot(chosen, down_proj, preferred_element_type=jnp.float32).astype(jnp.bfloat16),
        "tensor",
    )
    final = unit_rows(middle + step_rates[1] * (unit_rows(mlp_own) - middle))
    out_state = (math.sqrt(model_width) * final).astype(jnp.bfloat16)
    return (out_state, page_cache)


def solution(mesh):
    return jax.shard_map(
        body,
        mesh=mesh,
        in_specs=(
            P(("seq", "tensor"), None),
            P("seq"),
            P(),
            P(None, "tensor", None),
            P("tensor", None),
            P(None, None, "tensor"),
            P("tensor", None),
            P("tensor", None),
            P(None, "tensor"),
            P(),
        ),
        out_specs=(P(("seq", "tensor"), None), P("seq", None, "tensor")),
        check_vma=False,
    )
```

```python
import functools
import math

import jax
import jax.numpy as jnp
from jax import lax
from jax.experimental import pallas as pl
from jax.experimental.pallas import tpu as pltpu
from jax.sharding import PartitionSpec as P

PAGE = 128


EPSILON = 1e-06
NEG_LARGE = -1e30


def unit_rows(matrix):
    return matrix * lax.rsqrt(jnp.sum(matrix * matrix, axis=-1, keepdims=True) + EPSILON)


def gather_rows(part, axis):
    count = lax.axis_size(axis)
    index = lax.axis_index(axis)
    rows = part.shape[0]
    out = jnp.zeros((count * rows, *part.shape[1:]), part.dtype)
    out = lax.dynamic_update_slice_in_dim(out, part, index * rows, 0)
    for shift in range(1, count):
        pairs = [(j, (j + shift) % count) for j in range(count)]
        came = lax.ppermute(part, axis, pairs)
        out = lax.dynamic_update_slice_in_dim(out, came, ((index - shift) % count) * rows, 0)
    return out


def scatter_sum(whole, axis):
    count = lax.axis_size(axis)
    index = lax.axis_index(axis)
    blocks = whole.reshape(count, whole.shape[0] // count, *whole.shape[1:])
    total = lax.dynamic_index_in_dim(blocks, index, 0, keepdims=False).astype(jnp.float32)
    for shift in range(1, count):
        pairs = [(j, (j + shift) % count) for j in range(count)]
        send = lax.dynamic_index_in_dim(blocks, (index + shift) % count, 0, keepdims=False)
        total = total + lax.ppermute(send, axis, pairs).astype(jnp.float32)
    return total


Q_TILE = 256
K_TILE = 256


def attend_kernel(
    bounds_ref, proj_ref, kv_ref, scale_ref, qseg_ref, kseg_ref, out_ref, *, factor, half
):
    rows = qseg_ref.shape[0]
    heads = scale_ref.shape[0]
    lanes = 2 * half
    shard_blocks = (kv_ref.shape[1] - kv_ref.shape[1] % K_TILE) // K_TILE
    tiles = rows // Q_TILE
    first = bounds_ref[2 * tiles]
    key_lane = lax.broadcasted_iota(jnp.int32, (K_TILE, lanes), 1)
    held = {}
    for head in range(heads):
        scale = scale_ref[head]
        for tile in range(tiles):
            q_raw = proj_ref[tile * Q_TILE : (tile + 1) * Q_TILE, head * lanes : (head + 1) * lanes]
            q_tile = (
                q_raw * lax.rsqrt(jnp.sum(q_raw * q_raw, axis=1, keepdims=True) + EPSILON) * scale
            ).astype(jnp.bfloat16)
            q_seg = qseg_ref[tile * Q_TILE : (tile + 1) * Q_TILE, :]
            q_pos = first + tile * Q_TILE + lax.broadcasted_iota(jnp.int32, (Q_TILE, K_TILE), 0)

            def step(block, carry, q_tile=q_tile, q_seg=q_seg, q_pos=q_pos, head=head, scale=scale):
                top, total, acc = carry
                shard = block // shard_blocks
                row_at = pl.multiple_of((block % shard_blocks) * K_TILE, K_TILE)
                key_at = pl.multiple_of(block * K_TILE, K_TILE)
                kv_blk = kv_ref[shard, pl.ds(row_at, K_TILE), head * lanes : (head + 1) * lanes]
                kv_f = kv_blk.astype(jnp.float32)
                k_sq = jnp.where(key_lane < half, kv_f * kv_f, 0.0)
                k_unit = (
                    kv_f * lax.rsqrt(jnp.sum(k_sq, axis=1, keepdims=True) + EPSILON) * scale
                ).astype(jnp.bfloat16)
                k_seg = kseg_ref[:, pl.ds(key_at, K_TILE)]
                scores = factor * lax.dot_general(
                    q_tile, k_unit, (((1,), (1,)), ((), ())), preferred_element_type=jnp.float32
                )
                k_pos = key_at + lax.broadcasted_iota(jnp.int32, (Q_TILE, K_TILE), 1)
                allowed = (q_seg == k_seg) & (k_pos <= q_pos)
                scores = jnp.where(allowed, scores, NEG_LARGE)
                new_top = jnp.maximum(top, jnp.max(scores, axis=1, keepdims=True))
                weights = jnp.where(allowed, jnp.exp(scores - new_top), 0.0)
                rescale = jnp.exp(top - new_top)
                new_total = total * rescale + jnp.sum(weights, axis=1, keepdims=True)
                update = jnp.dot(
                    weights.astype(jnp.bfloat16), kv_blk, preferred_element_type=jnp.float32
                )
                return (new_top, new_total, acc * rescale + update)

            start = (
                jnp.full((Q_TILE, 1), NEG_LARGE, jnp.float32),
                jnp.zeros((Q_TILE, 1), jnp.float32),
                jnp.zeros((Q_TILE, lanes), jnp.float32),
            )
            top, total, acc = lax.fori_loop(
                bounds_ref[tile], bounds_ref[tiles + tile] + 1, step, start
            )
            result = acc / total
            pair = head // 2
            rows_at = slice(tile * Q_TILE, (tile + 1) * Q_TILE)
            if head % 2 == 0:
                held[tile] = pltpu.roll(result, half, 1)
                if head == heads - 1:
                    out_ref[rows_at, pair * lanes : (pair + 1) * lanes] = held[tile].astype(
                        out_ref.dtype
                    )
            else:
                joined = jnp.where(
                    lax.broadcasted_iota(jnp.int32, (Q_TILE, lanes), 1) < half, held[tile], result
                )
                out_ref[rows_at, pair * lanes : (pair + 1) * lanes] = joined.astype(out_ref.dtype)


def flash_attend(bounds, proj, gathered, scale_pad, query_segs, key_segs, factor, half):
    rows = query_segs.shape[0]
    heads, _, lanes = scale_pad.shape
    keys = key_segs.shape[1]
    vmem = pl.BlockSpec(memory_space=pltpu.VMEM)
    return pl.pallas_call(
        functools.partial(attend_kernel, factor=factor, half=half),
        out_shape=jax.ShapeDtypeStruct((rows, -(-heads // 2) * lanes), jnp.bfloat16),
        in_specs=[pl.BlockSpec(memory_space=pltpu.SMEM)] + [vmem] * 5,
        out_specs=vmem,
        cost_estimate=pl.CostEstimate(
            flops=4 * heads * rows * keys * lanes,
            transcendentals=heads * rows * keys,
            bytes_accessed=heads * keys * lanes * 2,
        ),
    )(bounds, proj, gathered, scale_pad, query_segs, key_segs)


def body(
    hidden,
    segment_ids,
    page_slot,
    in_proj,
    out_proj,
    up_proj,
    down_proj,
    score_scale,
    mlp_scale,
    step_rates,
):
    seq_count = lax.axis_size("seq")
    seq_index = lax.axis_index("seq")
    local_tokens = segment_ids.shape[0]
    heads_dev, head_dim = score_scale.shape
    model_width = hidden.shape[1]
    hidden_dev = down_proj.shape[0]
    pages_dev = local_tokens // PAGE
    channels = heads_dev * 2 * head_dim
    state_own = unit_rows(hidden.astype(jnp.float32)).astype(jnp.bfloat16)
    gathered_state = gather_rows(state_own, "tensor")
    lanes = 2 * head_dim
    projected = jnp.dot(
        gathered_state,
        in_proj.reshape(model_width, heads_dev * 3 * head_dim),
        preferred_element_type=jnp.float32,
    )
    width = 3 * head_dim
    query_pad = jnp.concatenate(
        sum(
            [
                [
                    projected[:, h * width : h * width + head_dim],
                    jnp.zeros((local_tokens, head_dim), jnp.float32),
                ]
                for h in range(heads_dev)
            ],
            [],
        ),
        axis=1,
    )
    key_value = jnp.concatenate(
        [projected[:, h * width + head_dim : (h + 1) * width] for h in range(heads_dev)], axis=1
    ).astype(jnp.bfloat16)
    first_token = seq_index * local_tokens
    seg_rows = -(-local_tokens // channels)
    seg_flat = jnp.pad(segment_ids, (0, seg_rows * channels - local_tokens))
    kv_ext = jnp.concatenate(
        [key_value, seg_flat.astype(jnp.bfloat16).reshape(seg_rows, channels)], axis=0
    )
    gathered = lax.all_gather(kv_ext, "seq", axis=0, tiled=False)
    seg_piece = (
        gathered[:, local_tokens:].reshape(seq_count, seg_rows * channels)[:, :local_tokens]
        .reshape(-1)
        .astype(jnp.int32)
    )
    piece_rows = seq_count * local_tokens
    scale_pad = jnp.pad(score_scale, ((0, 0), (0, lanes - head_dim))).reshape(heads_dev, 1, lanes)
    tiles = local_tokens // Q_TILE
    tile_first = first_token + Q_TILE * jnp.arange(tiles, dtype=jnp.int32)
    tile_seg = segment_ids.reshape(tiles, Q_TILE)[:, 0]
    block_last_seg = seg_piece.reshape(piece_rows // K_TILE, K_TILE)[:, -1]
    block_lo = jnp.sum(
        (block_last_seg[None, :] < tile_seg[:, None]).astype(jnp.int32), axis=1
    )
    block_hi = (tile_first + Q_TILE - 1) // K_TILE
    bounds = jnp.concatenate([block_lo, block_hi, first_token[None]]).astype(jnp.int32)
    heads_pad = flash_attend(
        bounds,
        query_pad,
        gathered,
        scale_pad,
        segment_ids.reshape(local_tokens, 1),
        seg_piece.reshape(1, piece_rows),
        math.sqrt(head_dim),
        head_dim,
    )
    heads_flat = heads_pad[:, : heads_dev * head_dim]
    slots_dev = page_slot.shape[0] // seq_count
    my_slots = seq_index * slots_dev + jnp.arange(slots_dev, dtype=jnp.int32)
    page_ids = jnp.arange(page_slot.shape[0], dtype=jnp.int32)
    source_page = jnp.sum(
        jnp.where(page_slot[None, :] == my_slots[:, None], page_ids[None, :], 0), axis=1
    )
    page_cache = jnp.stack(
        [
            lax.dynamic_slice(
                gathered,
                (source_page[j] // pages_dev, (source_page[j] % pages_dev) * PAGE, 0),
                (1, PAGE, channels),
            )[0]
            for j in range(slots_dev)
        ]
    )
    chosen = heads_flat
    attn_own = scatter_sum(
        jnp.dot(chosen, out_proj, preferred_element_type=jnp.float32).astype(jnp.bfloat16),
        "tensor",
    )
    state_f = state_own.astype(jnp.float32)
    middle = unit_rows(state_f + step_rates[0] * (unit_rows(attn_own) - state_f))
    mid_rows = gather_rows(middle.astype(jnp.bfloat16), "tensor")
    both = jnp.einsum("td,dkf->tkf", mid_rows, up_proj, preferred_element_type=jnp.float32)
    act = (
        both[:, 0] * mlp_scale[0] * jax.nn.silu(both[:, 1] * mlp_scale[1] * math.sqrt(model_width))
    ).astype(jnp.bfloat16)
    chosen = act
    mlp_own = scatter_sum(
        jnp.dot(chosen, down_proj, preferred_element_type=jnp.float32).astype(jnp.bfloat16),
        "tensor",
    )
    final = unit_rows(middle + step_rates[1] * (unit_rows(mlp_own) - middle))
    out_state = (math.sqrt(model_width) * final).astype(jnp.bfloat16)
    return (out_state, page_cache)


def solution(mesh):
    return jax.shard_map(
        body,
        mesh=mesh,
        in_specs=(
            P(("seq", "tensor"), None),
            P("seq"),
            P(),
            P(None, "tensor", None),
            P("tensor", None),
            P(None, None, "tensor"),
            P("tensor", None),
            P("tensor", None),
            P(None, "tensor"),
            P(),
        ),
        out_specs=(P(("seq", "tensor"), None), P("seq", None, "tensor")),
        check_vma=False,
    )
```

```python
import functools
import math

import jax
import jax.numpy as jnp
from jax import lax
from jax.experimental import pallas as pl
from jax.experimental.pallas import tpu as pltpu
from jax.sharding import PartitionSpec as P

PAGE = 128


EPSILON = 1e-06
NEG_LARGE = -1e30


def unit_rows(matrix):
    return matrix * lax.rsqrt(jnp.sum(matrix * matrix, axis=-1, keepdims=True) + EPSILON)


def gather_rows(part, axis):
    count = lax.axis_size(axis)
    index = lax.axis_index(axis)
    rows = part.shape[0]
    out = jnp.zeros((count * rows, *part.shape[1:]), part.dtype)
    out = lax.dynamic_update_slice_in_dim(out, part, index * rows, 0)
    for shift in range(1, count):
        pairs = [(j, (j + shift) % count) for j in range(count)]
        came = lax.ppermute(part, axis, pairs)
        out = lax.dynamic_update_slice_in_dim(out, came, ((index - shift) % count) * rows, 0)
    return out


def scatter_sum(whole, axis):
    count = lax.axis_size(axis)
    index = lax.axis_index(axis)
    blocks = whole.reshape(count, whole.shape[0] // count, *whole.shape[1:])
    total = lax.dynamic_index_in_dim(blocks, index, 0, keepdims=False).astype(jnp.float32)
    for shift in range(1, count):
        pairs = [(j, (j + shift) % count) for j in range(count)]
        send = lax.dynamic_index_in_dim(blocks, (index + shift) % count, 0, keepdims=False)
        total = total + lax.ppermute(send, axis, pairs).astype(jnp.float32)
    return total


Q_TILE = 256
K_TILE = 256


def attend_kernel(
    bounds_ref, proj_ref, kv_ref, scale_ref, qseg_ref, kseg_ref, out_ref, *, factor, half
):
    rows = qseg_ref.shape[0]
    heads = scale_ref.shape[0]
    lanes = 2 * half
    shard_blocks = (kv_ref.shape[1] - kv_ref.shape[1] % K_TILE) // K_TILE
    tiles = rows // Q_TILE
    first = bounds_ref[2 * tiles]
    key_base = bounds_ref[2 * tiles + 1]
    key_lane = lax.broadcasted_iota(jnp.int32, (K_TILE, lanes), 1)
    held = {}
    for head in range(heads):
        scale = scale_ref[head]
        for tile in range(tiles):
            q_raw = proj_ref[tile * Q_TILE : (tile + 1) * Q_TILE, head * lanes : (head + 1) * lanes]
            q_tile = (
                q_raw * lax.rsqrt(jnp.sum(q_raw * q_raw, axis=1, keepdims=True) + EPSILON) * scale
            ).astype(jnp.bfloat16)
            q_seg = qseg_ref[tile * Q_TILE : (tile + 1) * Q_TILE, :]
            q_pos = first + tile * Q_TILE + lax.broadcasted_iota(jnp.int32, (Q_TILE, K_TILE), 0)

            def step(block, carry, q_tile=q_tile, q_seg=q_seg, q_pos=q_pos, head=head, scale=scale):
                top, total, acc = carry
                shard = block // shard_blocks
                row_at = pl.multiple_of((block % shard_blocks) * K_TILE, K_TILE)
                key_at = pl.multiple_of(block * K_TILE, K_TILE)
                kv_blk = kv_ref[shard, pl.ds(row_at, K_TILE), head * lanes : (head + 1) * lanes]
                kv_f = kv_blk.astype(jnp.float32)
                k_sq = jnp.where(key_lane < half, kv_f * kv_f, 0.0)
                k_unit = (
                    kv_f * lax.rsqrt(jnp.sum(k_sq, axis=1, keepdims=True) + EPSILON) * scale
                ).astype(jnp.bfloat16)
                k_seg = kseg_ref[:, pl.ds(key_at, K_TILE)]
                scores = factor * lax.dot_general(
                    q_tile, k_unit, (((1,), (1,)), ((), ())), preferred_element_type=jnp.float32
                )
                k_pos = key_base + key_at + lax.broadcasted_iota(jnp.int32, (Q_TILE, K_TILE), 1)
                allowed = (q_seg == k_seg) & (k_pos <= q_pos)
                scores = jnp.where(allowed, scores, NEG_LARGE)
                new_top = jnp.maximum(top, jnp.max(scores, axis=1, keepdims=True))
                weights = jnp.where(allowed, jnp.exp(scores - new_top), 0.0)
                rescale = jnp.exp(top - new_top)
                new_total = total * rescale + jnp.sum(weights, axis=1, keepdims=True)
                update = jnp.dot(
                    weights.astype(jnp.bfloat16), kv_blk, preferred_element_type=jnp.float32
                )
                return (new_top, new_total, acc * rescale + update)

            start = (
                jnp.full((Q_TILE, 1), NEG_LARGE, jnp.float32),
                jnp.zeros((Q_TILE, 1), jnp.float32),
                jnp.zeros((Q_TILE, lanes), jnp.float32),
            )
            top, total, acc = lax.fori_loop(
                bounds_ref[tile], bounds_ref[tiles + tile] + 1, step, start
            )
            result = acc / total
            pair = head // 2
            rows_at = slice(tile * Q_TILE, (tile + 1) * Q_TILE)
            if head % 2 == 0:
                held[tile] = pltpu.roll(result, half, 1)
                if head == heads - 1:
                    out_ref[rows_at, pair * lanes : (pair + 1) * lanes] = held[tile].astype(
                        out_ref.dtype
                    )
            else:
                joined = jnp.where(
                    lax.broadcasted_iota(jnp.int32, (Q_TILE, lanes), 1) < half, held[tile], result
                )
                out_ref[rows_at, pair * lanes : (pair + 1) * lanes] = joined.astype(out_ref.dtype)


def flash_attend(bounds, proj, gathered, scale_pad, query_segs, key_segs, factor, half):
    rows = query_segs.shape[0]
    heads, _, lanes = scale_pad.shape
    keys = key_segs.shape[1]
    vmem = pl.BlockSpec(memory_space=pltpu.VMEM)
    return pl.pallas_call(
        functools.partial(attend_kernel, factor=factor, half=half),
        out_shape=jax.ShapeDtypeStruct((rows, -(-heads // 2) * lanes), jnp.bfloat16),
        in_specs=[pl.BlockSpec(memory_space=pltpu.SMEM)] + [vmem] * 5,
        out_specs=vmem,
        cost_estimate=pl.CostEstimate(
            flops=4 * heads * rows * keys * lanes,
            transcendentals=heads * rows * keys,
            bytes_accessed=heads * keys * lanes * 2,
        ),
    )(bounds, proj, gathered, scale_pad, query_segs, key_segs)


def body(
    hidden,
    segment_ids,
    page_slot,
    in_proj,
    out_proj,
    up_proj,
    down_proj,
    score_scale,
    mlp_scale,
    step_rates,
):
    seq_count = lax.axis_size("seq")
    seq_index = lax.axis_index("seq")
    local_tokens = segment_ids.shape[0]
    heads_dev, head_dim = score_scale.shape
    model_width = hidden.shape[1]
    hidden_dev = down_proj.shape[0]
    pages_dev = local_tokens // PAGE
    channels = heads_dev * 2 * head_dim
    state_own = unit_rows(hidden.astype(jnp.float32)).astype(jnp.bfloat16)
    gathered_state = gather_rows(state_own, "tensor")
    lanes = 2 * head_dim
    projected = jnp.dot(
        gathered_state,
        in_proj.reshape(model_width, heads_dev * 3 * head_dim),
        preferred_element_type=jnp.float32,
    )
    width = 3 * head_dim
    query_pad = jnp.concatenate(
        sum(
            [
                [
                    projected[:, h * width : h * width + head_dim],
                    jnp.zeros((local_tokens, head_dim), jnp.float32),
                ]
                for h in range(heads_dev)
            ],
            [],
        ),
        axis=1,
    )
    key_value = jnp.concatenate(
        [projected[:, h * width + head_dim : (h + 1) * width] for h in range(heads_dev)], axis=1
    ).astype(jnp.bfloat16)
    first_token = seq_index * local_tokens
    seg_rows = -(-local_tokens // channels)
    seg_flat = jnp.pad(segment_ids, (0, seg_rows * channels - local_tokens))
    kv_ext = jnp.concatenate(
        [key_value, seg_flat.astype(jnp.bfloat16).reshape(seg_rows, channels)], axis=0
    )
    longest = seq_count * local_tokens // 2
    back = min(seq_count - 1, -(-(longest - 1) // local_tokens))
    arrived = []
    for shift in range(back, 0, -1):
        pairs = [(j, j + shift) for j in range(seq_count - shift)]
        arrived.append(lax.ppermute(kv_ext, "seq", pairs))
    window = jnp.stack(arrived + [kv_ext])
    window_first = (seq_index - back) * local_tokens
    window_shard = seq_index - back + jnp.arange(back + 1, dtype=jnp.int32)
    seg_piece = (
        window[:, local_tokens:].reshape(back + 1, seg_rows * channels)[:, :local_tokens]
        .astype(jnp.int32)
    )
    seg_piece = jnp.where(window_shard[:, None] >= 0, seg_piece, -1).reshape(-1)
    piece_rows = (back + 1) * local_tokens
    scale_pad = jnp.pad(score_scale, ((0, 0), (0, lanes - head_dim))).reshape(heads_dev, 1, lanes)
    tiles = local_tokens // Q_TILE
    tile_first = first_token + Q_TILE * jnp.arange(tiles, dtype=jnp.int32)
    tile_seg = segment_ids.reshape(tiles, Q_TILE)[:, 0]
    block_last_seg = seg_piece.reshape(piece_rows // K_TILE, K_TILE)[:, -1]
    block_lo = jnp.sum(
        (block_last_seg[None, :] < tile_seg[:, None]).astype(jnp.int32), axis=1
    )
    block_hi = (tile_first + Q_TILE - 1 - window_first) // K_TILE
    bounds = jnp.concatenate(
        [block_lo, block_hi, first_token[None], window_first[None]]
    ).astype(jnp.int32)
    heads_pad = flash_attend(
        bounds,
        query_pad,
        window,
        scale_pad,
        segment_ids.reshape(local_tokens, 1),
        seg_piece.reshape(1, piece_rows),
        math.sqrt(head_dim),
        head_dim,
    )
    heads_flat = heads_pad[:, : heads_dev * head_dim]
    kv_late, heads_flat = lax.optimization_barrier((kv_ext, heads_flat))
    gathered = lax.all_gather(kv_late, "seq", axis=0, tiled=False)
    slots_dev = page_slot.shape[0] // seq_count
    my_slots = seq_index * slots_dev + jnp.arange(slots_dev, dtype=jnp.int32)
    page_ids = jnp.arange(page_slot.shape[0], dtype=jnp.int32)
    source_page = jnp.sum(
        jnp.where(page_slot[None, :] == my_slots[:, None], page_ids[None, :], 0), axis=1
    )
    page_cache = jnp.stack(
        [
            lax.dynamic_slice(
                gathered,
                (source_page[j] // pages_dev, (source_page[j] % pages_dev) * PAGE, 0),
                (1, PAGE, channels),
            )[0]
            for j in range(slots_dev)
        ]
    )
    chosen = heads_flat
    attn_own = scatter_sum(
        jnp.dot(chosen, out_proj, preferred_element_type=jnp.float32).astype(jnp.bfloat16),
        "tensor",
    )
    state_f = state_own.astype(jnp.float32)
    middle = unit_rows(state_f + step_rates[0] * (unit_rows(attn_own) - state_f))
    mid_rows = gather_rows(middle.astype(jnp.bfloat16), "tensor")
    both = jnp.einsum("td,dkf->tkf", mid_rows, up_proj, preferred_element_type=jnp.float32)
    act = (
        both[:, 0] * mlp_scale[0] * jax.nn.silu(both[:, 1] * mlp_scale[1] * math.sqrt(model_width))
    ).astype(jnp.bfloat16)
    chosen = act
    mlp_own = scatter_sum(
        jnp.dot(chosen, down_proj, preferred_element_type=jnp.float32).astype(jnp.bfloat16),
        "tensor",
    )
    final = unit_rows(middle + step_rates[1] * (unit_rows(mlp_own) - middle))
    out_state = (math.sqrt(model_width) * final).astype(jnp.bfloat16)
    return (out_state, page_cache)


def solution(mesh):
    return jax.shard_map(
        body,
        mesh=mesh,
        in_specs=(
            P(("seq", "tensor"), None),
            P("seq"),
            P(),
            P(None, "tensor", None),
            P("tensor", None),
            P(None, None, "tensor"),
            P("tensor", None),
            P("tensor", None),
            P(None, "tensor"),
            P(),
        ),
        out_specs=(P(("seq", "tensor"), None), P("seq", None, "tensor")),
        check_vma=False,
    )
```

```python
import functools
import math

import jax
import jax.numpy as jnp
from jax import lax
from jax.experimental import pallas as pl
from jax.experimental.pallas import tpu as pltpu
from jax.sharding import PartitionSpec as P

PAGE = 128


EPSILON = 1e-06
NEG_LARGE = -1e30


def unit_rows(matrix):
    return matrix * lax.rsqrt(jnp.sum(matrix * matrix, axis=-1, keepdims=True) + EPSILON)


def gather_rows(part, axis):
    count = lax.axis_size(axis)
    index = lax.axis_index(axis)
    rows = part.shape[0]
    out = jnp.zeros((count * rows, *part.shape[1:]), part.dtype)
    out = lax.dynamic_update_slice_in_dim(out, part, index * rows, 0)
    for shift in range(1, count):
        pairs = [(j, (j + shift) % count) for j in range(count)]
        came = lax.ppermute(part, axis, pairs)
        out = lax.dynamic_update_slice_in_dim(out, came, ((index - shift) % count) * rows, 0)
    return out


def scatter_sum(whole, axis):
    count = lax.axis_size(axis)
    index = lax.axis_index(axis)
    blocks = whole.reshape(count, whole.shape[0] // count, *whole.shape[1:])
    total = lax.dynamic_index_in_dim(blocks, index, 0, keepdims=False).astype(jnp.float32)
    for shift in range(1, count):
        pairs = [(j, (j + shift) % count) for j in range(count)]
        send = lax.dynamic_index_in_dim(blocks, (index + shift) % count, 0, keepdims=False)
        total = total + lax.ppermute(send, axis, pairs).astype(jnp.float32)
    return total


Q_TILE = 256
K_TILE = 256


def attend_kernel(
    bounds_ref, proj_ref, kv_ref, scale_ref, qseg_ref, kseg_ref, out_ref, *, factor, half
):
    rows = qseg_ref.shape[0]
    heads = scale_ref.shape[0]
    lanes = 2 * half
    shard_blocks = (kv_ref.shape[1] - kv_ref.shape[1] % K_TILE) // K_TILE
    tiles = rows // Q_TILE
    first = bounds_ref[2 * tiles]
    key_base = bounds_ref[2 * tiles + 1]
    key_lane = lax.broadcasted_iota(jnp.int32, (K_TILE, lanes), 1)
    held = {}
    for head in range(heads):
        scale = scale_ref[head]
        for tile in range(tiles):
            q_raw = proj_ref[tile * Q_TILE : (tile + 1) * Q_TILE, head * lanes : (head + 1) * lanes]
            q_tile = (
                q_raw * lax.rsqrt(jnp.sum(q_raw * q_raw, axis=1, keepdims=True) + EPSILON) * scale
            ).astype(jnp.bfloat16)
            q_seg = qseg_ref[tile * Q_TILE : (tile + 1) * Q_TILE, :]
            q_pos = first + tile * Q_TILE + lax.broadcasted_iota(jnp.int32, (Q_TILE, K_TILE), 0)

            def step(block, carry, q_tile=q_tile, q_seg=q_seg, q_pos=q_pos, head=head, scale=scale):
                top, total, acc = carry
                shard = block // shard_blocks
                row_at = pl.multiple_of((block % shard_blocks) * K_TILE, K_TILE)
                key_at = pl.multiple_of(block * K_TILE, K_TILE)
                kv_blk = kv_ref[shard, pl.ds(row_at, K_TILE), head * lanes : (head + 1) * lanes]
                kv_f = kv_blk.astype(jnp.float32)
                k_sq = jnp.where(key_lane < half, kv_f * kv_f, 0.0)
                k_unit = (
                    kv_f * lax.rsqrt(jnp.sum(k_sq, axis=1, keepdims=True) + EPSILON) * scale
                ).astype(jnp.bfloat16)
                k_seg = kseg_ref[:, pl.ds(key_at, K_TILE)]
                scores = factor * lax.dot_general(
                    q_tile, k_unit, (((1,), (1,)), ((), ())), preferred_element_type=jnp.float32
                )
                k_pos = key_base + key_at + lax.broadcasted_iota(jnp.int32, (Q_TILE, K_TILE), 1)
                allowed = (q_seg == k_seg) & (k_pos <= q_pos)
                scores = jnp.where(allowed, scores, NEG_LARGE)
                new_top = jnp.maximum(top, jnp.max(scores, axis=1, keepdims=True))
                weights = jnp.where(allowed, jnp.exp(scores - new_top), 0.0)
                rescale = jnp.exp(top - new_top)
                new_total = total * rescale + jnp.sum(weights, axis=1, keepdims=True)
                update = jnp.dot(
                    weights.astype(jnp.bfloat16), kv_blk, preferred_element_type=jnp.float32
                )
                return (new_top, new_total, acc * rescale + update)

            start = (
                jnp.full((Q_TILE, 1), NEG_LARGE, jnp.float32),
                jnp.zeros((Q_TILE, 1), jnp.float32),
                jnp.zeros((Q_TILE, lanes), jnp.float32),
            )
            top, total, acc = lax.fori_loop(
                bounds_ref[tile], bounds_ref[tiles + tile] + 1, step, start
            )
            result = acc / total
            pair = head // 2
            rows_at = slice(tile * Q_TILE, (tile + 1) * Q_TILE)
            if head % 2 == 0:
                held[tile] = pltpu.roll(result, half, 1)
                if head == heads - 1:
                    out_ref[rows_at, pair * lanes : (pair + 1) * lanes] = held[tile].astype(
                        out_ref.dtype
                    )
            else:
                joined = jnp.where(
                    lax.broadcasted_iota(jnp.int32, (Q_TILE, lanes), 1) < half, held[tile], result
                )
                out_ref[rows_at, pair * lanes : (pair + 1) * lanes] = joined.astype(out_ref.dtype)


def flash_attend(bounds, proj, gathered, scale_pad, query_segs, key_segs, factor, half):
    rows = query_segs.shape[0]
    heads, _, lanes = scale_pad.shape
    keys = key_segs.shape[1]
    vmem = pl.BlockSpec(memory_space=pltpu.VMEM)
    return pl.pallas_call(
        functools.partial(attend_kernel, factor=factor, half=half),
        out_shape=jax.ShapeDtypeStruct((rows, -(-heads // 2) * lanes), jnp.bfloat16),
        in_specs=[pl.BlockSpec(memory_space=pltpu.SMEM)] + [vmem] * 5,
        out_specs=vmem,
        cost_estimate=pl.CostEstimate(
            flops=4 * heads * rows * keys * lanes,
            transcendentals=heads * rows * keys,
            bytes_accessed=heads * keys * lanes * 2,
        ),
    )(bounds, proj, gathered, scale_pad, query_segs, key_segs)


def body(
    hidden,
    segment_ids,
    page_slot,
    in_proj,
    out_proj,
    up_proj,
    down_proj,
    score_scale,
    mlp_scale,
    step_rates,
):
    seq_count = lax.axis_size("seq")
    seq_index = lax.axis_index("seq")
    local_tokens = segment_ids.shape[0]
    heads_dev, head_dim = score_scale.shape
    model_width = hidden.shape[1]
    hidden_dev = down_proj.shape[0]
    pages_dev = local_tokens // PAGE
    channels = heads_dev * 2 * head_dim
    state_own = unit_rows(hidden.astype(jnp.float32)).astype(jnp.bfloat16)
    gathered_state = gather_rows(state_own, "tensor")
    lanes = 2 * head_dim
    projected = jnp.dot(
        gathered_state,
        in_proj.reshape(model_width, heads_dev * 3 * head_dim),
        preferred_element_type=jnp.float32,
    )
    width = 3 * head_dim
    query_pad = jnp.concatenate(
        sum(
            [
                [
                    projected[:, h * width : h * width + head_dim],
                    jnp.zeros((local_tokens, head_dim), jnp.float32),
                ]
                for h in range(heads_dev)
            ],
            [],
        ),
        axis=1,
    )
    key_value = jnp.concatenate(
        [projected[:, h * width + head_dim : (h + 1) * width] for h in range(heads_dev)], axis=1
    ).astype(jnp.bfloat16)
    first_token = seq_index * local_tokens
    seg_rows = -(-local_tokens // channels)
    seg_flat = jnp.pad(segment_ids, (0, seg_rows * channels - local_tokens))
    kv_ext = jnp.concatenate(
        [key_value, seg_flat.astype(jnp.bfloat16).reshape(seg_rows, channels)], axis=0
    )
    longest = seq_count * local_tokens // 2
    back = min(seq_count - 1, -(-(longest - 1) // local_tokens))
    arrived = []
    for shift in range(back, 0, -1):
        pairs = [(j, j + shift) for j in range(seq_count - shift)]
        arrived.append(lax.ppermute(kv_ext, "seq", pairs))
    window = jnp.stack(arrived + [kv_ext])
    kv_late, window = lax.optimization_barrier((kv_ext, window))
    gathered = lax.all_gather(kv_late, "seq", axis=0, tiled=False)
    window_first = (seq_index - back) * local_tokens
    window_shard = seq_index - back + jnp.arange(back + 1, dtype=jnp.int32)
    seg_piece = (
        window[:, local_tokens:].reshape(back + 1, seg_rows * channels)[:, :local_tokens]
        .astype(jnp.int32)
    )
    seg_piece = jnp.where(window_shard[:, None] >= 0, seg_piece, -1).reshape(-1)
    piece_rows = (back + 1) * local_tokens
    scale_pad = jnp.pad(score_scale, ((0, 0), (0, lanes - head_dim))).reshape(heads_dev, 1, lanes)
    tiles = local_tokens // Q_TILE
    tile_first = first_token + Q_TILE * jnp.arange(tiles, dtype=jnp.int32)
    tile_seg = segment_ids.reshape(tiles, Q_TILE)[:, 0]
    block_last_seg = seg_piece.reshape(piece_rows // K_TILE, K_TILE)[:, -1]
    block_lo = jnp.sum(
        (block_last_seg[None, :] < tile_seg[:, None]).astype(jnp.int32), axis=1
    )
    block_hi = (tile_first + Q_TILE - 1 - window_first) // K_TILE
    bounds = jnp.concatenate(
        [block_lo, block_hi, first_token[None], window_first[None]]
    ).astype(jnp.int32)
    heads_pad = flash_attend(
        bounds,
        query_pad,
        window,
        scale_pad,
        segment_ids.reshape(local_tokens, 1),
        seg_piece.reshape(1, piece_rows),
        math.sqrt(head_dim),
        head_dim,
    )
    heads_flat = heads_pad[:, : heads_dev * head_dim]
    slots_dev = page_slot.shape[0] // seq_count
    my_slots = seq_index * slots_dev + jnp.arange(slots_dev, dtype=jnp.int32)
    page_ids = jnp.arange(page_slot.shape[0], dtype=jnp.int32)
    source_page = jnp.sum(
        jnp.where(page_slot[None, :] == my_slots[:, None], page_ids[None, :], 0), axis=1
    )
    page_cache = jnp.stack(
        [
            lax.dynamic_slice(
                gathered,
                (source_page[j] // pages_dev, (source_page[j] % pages_dev) * PAGE, 0),
                (1, PAGE, channels),
            )[0]
            for j in range(slots_dev)
        ]
    )
    chosen = heads_flat
    attn_own = scatter_sum(
        jnp.dot(chosen, out_proj, preferred_element_type=jnp.float32).astype(jnp.bfloat16),
        "tensor",
    )
    state_f = state_own.astype(jnp.float32)
    middle = unit_rows(state_f + step_rates[0] * (unit_rows(attn_own) - state_f))
    mid_rows = gather_rows(middle.astype(jnp.bfloat16), "tensor")
    both = jnp.einsum("td,dkf->tkf", mid_rows, up_proj, preferred_element_type=jnp.float32)
    act = (
        both[:, 0] * mlp_scale[0] * jax.nn.silu(both[:, 1] * mlp_scale[1] * math.sqrt(model_width))
    ).astype(jnp.bfloat16)
    chosen = act
    mlp_own = scatter_sum(
        jnp.dot(chosen, down_proj, preferred_element_type=jnp.float32).astype(jnp.bfloat16),
        "tensor",
    )
    final = unit_rows(middle + step_rates[1] * (unit_rows(mlp_own) - middle))
    out_state = (math.sqrt(model_width) * final).astype(jnp.bfloat16)
    return (out_state, page_cache)


def solution(mesh):
    return jax.shard_map(
        body,
        mesh=mesh,
        in_specs=(
            P(("seq", "tensor"), None),
            P("seq"),
            P(),
            P(None, "tensor", None),
            P("tensor", None),
            P(None, None, "tensor"),
            P("tensor", None),
            P("tensor", None),
            P(None, "tensor"),
            P(),
        ),
        out_specs=(P(("seq", "tensor"), None), P("seq", None, "tensor")),
        check_vma=False,
    )
```

```python
import functools
import math

import jax
import jax.numpy as jnp
from jax import lax
from jax.experimental import pallas as pl
from jax.experimental.pallas import tpu as pltpu
from jax.sharding import PartitionSpec as P

PAGE = 128


EPSILON = 1e-06
NEG_LARGE = -1e30


def unit_rows(matrix):
    return matrix * lax.rsqrt(jnp.sum(matrix * matrix, axis=-1, keepdims=True) + EPSILON)


def gather_rows(part, axis):
    count = lax.axis_size(axis)
    index = lax.axis_index(axis)
    if count & (count - 1):
        return gather_rows_ring(part, axis)
    held = part
    bit = 1
    while bit < count:
        pairs = [(j, j ^ bit) for j in range(count)]
        came = lax.ppermute(held, axis, pairs)
        low = (index & bit) == 0
        held = jnp.concatenate(
            [jnp.where(low, held, came), jnp.where(low, came, held)], axis=0
        )
        bit *= 2
    return held


def gather_rows_ring(part, axis):
    count = lax.axis_size(axis)
    index = lax.axis_index(axis)
    rows = part.shape[0]
    out = jnp.zeros((count * rows, *part.shape[1:]), part.dtype)
    out = lax.dynamic_update_slice_in_dim(out, part, index * rows, 0)
    for shift in range(1, count):
        pairs = [(j, (j + shift) % count) for j in range(count)]
        came = lax.ppermute(part, axis, pairs)
        out = lax.dynamic_update_slice_in_dim(out, came, ((index - shift) % count) * rows, 0)
    return out


def scatter_sum(whole, axis):
    count = lax.axis_size(axis)
    index = lax.axis_index(axis)
    if count & (count - 1):
        return scatter_sum_ring(whole, axis)
    held = whole.reshape(count, whole.shape[0] // count, *whole.shape[1:])
    bit = 1
    while bit < count:
        pairs = [(j, j ^ bit) for j in range(count)]
        halves = held.reshape(held.shape[0] // 2, 2, *held.shape[1:])
        low = (index & bit) == 0
        keep = jnp.where(low, halves[:, 0], halves[:, 1])
        send = jnp.where(low, halves[:, 1], halves[:, 0])
        held = keep.astype(jnp.float32) + lax.ppermute(send, axis, pairs).astype(jnp.float32)
        bit *= 2
    return held[0]


def scatter_sum_ring(whole, axis):
    count = lax.axis_size(axis)
    index = lax.axis_index(axis)
    blocks = whole.reshape(count, whole.shape[0] // count, *whole.shape[1:])
    total = lax.dynamic_index_in_dim(blocks, index, 0, keepdims=False).astype(jnp.float32)
    for shift in range(1, count):
        pairs = [(j, (j + shift) % count) for j in range(count)]
        send = lax.dynamic_index_in_dim(blocks, (index + shift) % count, 0, keepdims=False)
        total = total + lax.ppermute(send, axis, pairs).astype(jnp.float32)
    return total


Q_TILE = 256
K_TILE = 256


def attend_kernel(
    bounds_ref, proj_ref, kv_ref, scale_ref, qseg_ref, kseg_ref, out_ref, *, factor, half
):
    rows = qseg_ref.shape[0]
    heads = scale_ref.shape[0]
    lanes = 2 * half
    shard_blocks = (kv_ref.shape[1] - kv_ref.shape[1] % K_TILE) // K_TILE
    tiles = rows // Q_TILE
    first = bounds_ref[2 * tiles]
    key_lane = lax.broadcasted_iota(jnp.int32, (K_TILE, lanes), 1)
    held = {}
    for head in range(heads):
        scale = scale_ref[head]
        for tile in range(tiles):
            q_raw = proj_ref[tile * Q_TILE : (tile + 1) * Q_TILE, head * lanes : (head + 1) * lanes]
            q_tile = (
                q_raw * lax.rsqrt(jnp.sum(q_raw * q_raw, axis=1, keepdims=True) + EPSILON) * scale
            ).astype(jnp.bfloat16)
            q_seg = qseg_ref[tile * Q_TILE : (tile + 1) * Q_TILE, :]
            q_pos = first + tile * Q_TILE + lax.broadcasted_iota(jnp.int32, (Q_TILE, K_TILE), 0)

            def step(block, carry, q_tile=q_tile, q_seg=q_seg, q_pos=q_pos, head=head, scale=scale):
                top, total, acc = carry
                shard = block // shard_blocks
                row_at = pl.multiple_of((block % shard_blocks) * K_TILE, K_TILE)
                key_at = pl.multiple_of(block * K_TILE, K_TILE)
                kv_blk = kv_ref[shard, pl.ds(row_at, K_TILE), head * lanes : (head + 1) * lanes]
                kv_f = kv_blk.astype(jnp.float32)
                k_sq = jnp.where(key_lane < half, kv_f * kv_f, 0.0)
                k_unit = (
                    kv_f * lax.rsqrt(jnp.sum(k_sq, axis=1, keepdims=True) + EPSILON) * scale
                ).astype(jnp.bfloat16)
                k_seg = kseg_ref[:, pl.ds(key_at, K_TILE)]
                scores = factor * lax.dot_general(
                    q_tile, k_unit, (((1,), (1,)), ((), ())), preferred_element_type=jnp.float32
                )
                k_pos = key_at + lax.broadcasted_iota(jnp.int32, (Q_TILE, K_TILE), 1)
                allowed = (q_seg == k_seg) & (k_pos <= q_pos)
                scores = jnp.where(allowed, scores, NEG_LARGE)
                new_top = jnp.maximum(top, jnp.max(scores, axis=1, keepdims=True))
                weights = jnp.where(allowed, jnp.exp(scores - new_top), 0.0)
                rescale = jnp.exp(top - new_top)
                new_total = total * rescale + jnp.sum(weights, axis=1, keepdims=True)
                update = jnp.dot(
                    weights.astype(jnp.bfloat16), kv_blk, preferred_element_type=jnp.float32
                )
                return (new_top, new_total, acc * rescale + update)

            start = (
                jnp.full((Q_TILE, 1), NEG_LARGE, jnp.float32),
                jnp.zeros((Q_TILE, 1), jnp.float32),
                jnp.zeros((Q_TILE, lanes), jnp.float32),
            )
            top, total, acc = lax.fori_loop(
                bounds_ref[tile], bounds_ref[tiles + tile] + 1, step, start
            )
            result = acc / total
            pair = head // 2
            rows_at = slice(tile * Q_TILE, (tile + 1) * Q_TILE)
            if head % 2 == 0:
                held[tile] = pltpu.roll(result, half, 1)
                if head == heads - 1:
                    out_ref[rows_at, pair * lanes : (pair + 1) * lanes] = held[tile].astype(
                        out_ref.dtype
                    )
            else:
                joined = jnp.where(
                    lax.broadcasted_iota(jnp.int32, (Q_TILE, lanes), 1) < half, held[tile], result
                )
                out_ref[rows_at, pair * lanes : (pair + 1) * lanes] = joined.astype(out_ref.dtype)


def flash_attend(bounds, proj, gathered, scale_pad, query_segs, key_segs, factor, half):
    rows = query_segs.shape[0]
    heads, _, lanes = scale_pad.shape
    keys = key_segs.shape[1]
    vmem = pl.BlockSpec(memory_space=pltpu.VMEM)
    return pl.pallas_call(
        functools.partial(attend_kernel, factor=factor, half=half),
        out_shape=jax.ShapeDtypeStruct((rows, -(-heads // 2) * lanes), jnp.bfloat16),
        in_specs=[pl.BlockSpec(memory_space=pltpu.SMEM)] + [vmem] * 5,
        out_specs=vmem,
        cost_estimate=pl.CostEstimate(
            flops=4 * heads * rows * keys * lanes,
            transcendentals=heads * rows * keys,
            bytes_accessed=heads * keys * lanes * 2,
        ),
    )(bounds, proj, gathered, scale_pad, query_segs, key_segs)


def body(
    hidden,
    segment_ids,
    page_slot,
    in_proj,
    out_proj,
    up_proj,
    down_proj,
    score_scale,
    mlp_scale,
    step_rates,
):
    seq_count = lax.axis_size("seq")
    seq_index = lax.axis_index("seq")
    local_tokens = segment_ids.shape[0]
    heads_dev, head_dim = score_scale.shape
    model_width = hidden.shape[1]
    hidden_dev = down_proj.shape[0]
    pages_dev = local_tokens // PAGE
    channels = heads_dev * 2 * head_dim
    state_own = unit_rows(hidden.astype(jnp.float32)).astype(jnp.bfloat16)
    gathered_state = gather_rows(state_own, "tensor")
    lanes = 2 * head_dim
    projected = jnp.dot(
        gathered_state,
        in_proj.reshape(model_width, heads_dev * 3 * head_dim),
        preferred_element_type=jnp.float32,
    )
    width = 3 * head_dim
    query_pad = jnp.concatenate(
        sum(
            [
                [
                    projected[:, h * width : h * width + head_dim],
                    jnp.zeros((local_tokens, head_dim), jnp.float32),
                ]
                for h in range(heads_dev)
            ],
            [],
        ),
        axis=1,
    )
    key_value = jnp.concatenate(
        [projected[:, h * width + head_dim : (h + 1) * width] for h in range(heads_dev)], axis=1
    ).astype(jnp.bfloat16)
    first_token = seq_index * local_tokens
    seg_rows = -(-local_tokens // channels)
    seg_flat = jnp.pad(segment_ids, (0, seg_rows * channels - local_tokens))
    kv_ext = jnp.concatenate(
        [key_value, seg_flat.astype(jnp.bfloat16).reshape(seg_rows, channels)], axis=0
    )
    gathered = lax.all_gather(kv_ext, "seq", axis=0, tiled=False)
    seg_piece = (
        gathered[:, local_tokens:].reshape(seq_count, seg_rows * channels)[:, :local_tokens]
        .reshape(-1)
        .astype(jnp.int32)
    )
    piece_rows = seq_count * local_tokens
    scale_pad = jnp.pad(score_scale, ((0, 0), (0, lanes - head_dim))).reshape(heads_dev, 1, lanes)
    tiles = local_tokens // Q_TILE
    tile_first = first_token + Q_TILE * jnp.arange(tiles, dtype=jnp.int32)
    tile_seg = segment_ids.reshape(tiles, Q_TILE)[:, 0]
    block_last_seg = seg_piece.reshape(piece_rows // K_TILE, K_TILE)[:, -1]
    block_lo = jnp.sum(
        (block_last_seg[None, :] < tile_seg[:, None]).astype(jnp.int32), axis=1
    )
    block_hi = (tile_first + Q_TILE - 1) // K_TILE
    bounds = jnp.concatenate([block_lo, block_hi, first_token[None]]).astype(jnp.int32)
    heads_pad = flash_attend(
        bounds,
        query_pad,
        gathered,
        scale_pad,
        segment_ids.reshape(local_tokens, 1),
        seg_piece.reshape(1, piece_rows),
        math.sqrt(head_dim),
        head_dim,
    )
    heads_flat = heads_pad[:, : heads_dev * head_dim]
    slots_dev = page_slot.shape[0] // seq_count
    my_slots = seq_index * slots_dev + jnp.arange(slots_dev, dtype=jnp.int32)
    page_ids = jnp.arange(page_slot.shape[0], dtype=jnp.int32)
    source_page = jnp.sum(
        jnp.where(page_slot[None, :] == my_slots[:, None], page_ids[None, :], 0), axis=1
    )
    page_cache = jnp.stack(
        [
            lax.dynamic_slice(
                gathered,
                (source_page[j] // pages_dev, (source_page[j] % pages_dev) * PAGE, 0),
                (1, PAGE, channels),
            )[0]
            for j in range(slots_dev)
        ]
    )
    chosen = heads_flat
    attn_own = scatter_sum(
        jnp.dot(chosen, out_proj, preferred_element_type=jnp.float32).astype(jnp.bfloat16),
        "tensor",
    )
    state_f = state_own.astype(jnp.float32)
    middle = unit_rows(state_f + step_rates[0] * (unit_rows(attn_own) - state_f))
    mid_rows = gather_rows(middle.astype(jnp.bfloat16), "tensor")
    both = jnp.einsum("td,dkf->tkf", mid_rows, up_proj, preferred_element_type=jnp.float32)
    act = (
        both[:, 0] * mlp_scale[0] * jax.nn.silu(both[:, 1] * mlp_scale[1] * math.sqrt(model_width))
    ).astype(jnp.bfloat16)
    chosen = act
    mlp_own = scatter_sum(
        jnp.dot(chosen, down_proj, preferred_element_type=jnp.float32).astype(jnp.bfloat16),
        "tensor",
    )
    final = unit_rows(middle + step_rates[1] * (unit_rows(mlp_own) - middle))
    out_state = (math.sqrt(model_width) * final).astype(jnp.bfloat16)
    return (out_state, page_cache)


def solution(mesh):
    return jax.shard_map(
        body,
        mesh=mesh,
        in_specs=(
            P(("seq", "tensor"), None),
            P("seq"),
            P(),
            P(None, "tensor", None),
            P("tensor", None),
            P(None, None, "tensor"),
            P("tensor", None),
            P("tensor", None),
            P(None, "tensor"),
            P(),
        ),
        out_specs=(P(("seq", "tensor"), None), P("seq", None, "tensor")),
        check_vma=False,
    )
```

```python
import functools
import math

import jax
import jax.numpy as jnp
from jax import lax
from jax.experimental import pallas as pl
from jax.experimental.pallas import tpu as pltpu
from jax.sharding import PartitionSpec as P

PAGE = 128


EPSILON = 1e-06
NEG_LARGE = -1e30


def unit_rows(matrix):
    return matrix * lax.rsqrt(jnp.sum(matrix * matrix, axis=-1, keepdims=True) + EPSILON)


def gather_rows(part, axis):
    count = lax.axis_size(axis)
    index = lax.axis_index(axis)
    rows = part.shape[0]
    out = jnp.zeros((count * rows, *part.shape[1:]), part.dtype)
    out = lax.dynamic_update_slice_in_dim(out, part, index * rows, 0)
    for shift in range(1, count):
        pairs = [(j, (j + shift) % count) for j in range(count)]
        came = lax.ppermute(part, axis, pairs)
        out = lax.dynamic_update_slice_in_dim(out, came, ((index - shift) % count) * rows, 0)
    return out


def scatter_sum(whole, axis):
    count = lax.axis_size(axis)
    index = lax.axis_index(axis)
    blocks = whole.reshape(count, whole.shape[0] // count, *whole.shape[1:])
    total = lax.dynamic_index_in_dim(blocks, index, 0, keepdims=False).astype(jnp.float32)
    for shift in range(1, count):
        pairs = [(j, (j + shift) % count) for j in range(count)]
        send = lax.dynamic_index_in_dim(blocks, (index + shift) % count, 0, keepdims=False)
        total = total + lax.ppermute(send, axis, pairs).astype(jnp.float32)
    return total


Q_TILE = 256
K_TILE = 256


def attend_kernel(
    bounds_ref, proj_ref, kv_ref, kvb_ref, scale_ref, qseg_ref, kseg_ref, out_ref, *, factor, half
):
    rows = qseg_ref.shape[0]
    heads = scale_ref.shape[0]
    lanes = 2 * half
    half_blocks = kvb_ref.shape[1] // K_TILE
    shard_blocks = 2 * half_blocks
    tiles = rows // Q_TILE
    first = bounds_ref[2 * tiles]
    high = bounds_ref[2 * tiles + 1]
    key_lane = lax.broadcasted_iota(jnp.int32, (K_TILE, lanes), 1)
    held = {}
    for head in range(heads):
        scale = scale_ref[head]
        for tile in range(tiles):
            q_raw = proj_ref[tile * Q_TILE : (tile + 1) * Q_TILE, head * lanes : (head + 1) * lanes]
            q_tile = (
                q_raw * lax.rsqrt(jnp.sum(q_raw * q_raw, axis=1, keepdims=True) + EPSILON) * scale
            ).astype(jnp.bfloat16)
            q_seg = qseg_ref[tile * Q_TILE : (tile + 1) * Q_TILE, :]
            q_pos = first + tile * Q_TILE + lax.broadcasted_iota(jnp.int32, (Q_TILE, K_TILE), 0)

            def step(block, carry, q_tile=q_tile, q_seg=q_seg, q_pos=q_pos, head=head, scale=scale):
                top, total, acc = carry
                shard = block // shard_blocks
                inner = block % shard_blocks
                row_at = pl.multiple_of((inner % half_blocks) * K_TILE, K_TILE)
                key_at = pl.multiple_of(block * K_TILE, K_TILE)
                kv_own = kv_ref[shard, pl.ds(row_at, K_TILE), head * lanes : (head + 1) * lanes]
                kv_far = kvb_ref[shard, pl.ds(row_at, K_TILE), head * lanes : (head + 1) * lanes]
                kv_blk = jnp.where(inner // half_blocks == high, kv_own, kv_far)
                kv_f = kv_blk.astype(jnp.float32)
                k_sq = jnp.where(key_lane < half, kv_f * kv_f, 0.0)
                k_unit = (
                    kv_f * lax.rsqrt(jnp.sum(k_sq, axis=1, keepdims=True) + EPSILON) * scale
                ).astype(jnp.bfloat16)
                k_seg = kseg_ref[:, pl.ds(key_at, K_TILE)]
                scores = factor * lax.dot_general(
                    q_tile, k_unit, (((1,), (1,)), ((), ())), preferred_element_type=jnp.float32
                )
                k_pos = key_at + lax.broadcasted_iota(jnp.int32, (Q_TILE, K_TILE), 1)
                allowed = (q_seg == k_seg) & (k_pos <= q_pos)
                scores = jnp.where(allowed, scores, NEG_LARGE)
                new_top = jnp.maximum(top, jnp.max(scores, axis=1, keepdims=True))
                weights = jnp.where(allowed, jnp.exp(scores - new_top), 0.0)
                rescale = jnp.exp(top - new_top)
                new_total = total * rescale + jnp.sum(weights, axis=1, keepdims=True)
                update = jnp.dot(
                    weights.astype(jnp.bfloat16), kv_blk, preferred_element_type=jnp.float32
                )
                return (new_top, new_total, acc * rescale + update)

            start = (
                jnp.full((Q_TILE, 1), NEG_LARGE, jnp.float32),
                jnp.zeros((Q_TILE, 1), jnp.float32),
                jnp.zeros((Q_TILE, lanes), jnp.float32),
            )
            top, total, acc = lax.fori_loop(
                bounds_ref[tile], bounds_ref[tiles + tile] + 1, step, start
            )
            result = acc / total
            pair = head // 2
            rows_at = slice(tile * Q_TILE, (tile + 1) * Q_TILE)
            if head % 2 == 0:
                held[tile] = pltpu.roll(result, half, 1)
                if head == heads - 1:
                    out_ref[rows_at, pair * lanes : (pair + 1) * lanes] = held[tile].astype(
                        out_ref.dtype
                    )
            else:
                joined = jnp.where(
                    lax.broadcasted_iota(jnp.int32, (Q_TILE, lanes), 1) < half, held[tile], result
                )
                out_ref[rows_at, pair * lanes : (pair + 1) * lanes] = joined.astype(out_ref.dtype)


def flash_attend(bounds, proj, gathered, gathered_far, scale_pad, query_segs, key_segs, factor, half):
    rows = query_segs.shape[0]
    heads, _, lanes = scale_pad.shape
    keys = key_segs.shape[1]
    vmem = pl.BlockSpec(memory_space=pltpu.VMEM)
    return pl.pallas_call(
        functools.partial(attend_kernel, factor=factor, half=half),
        out_shape=jax.ShapeDtypeStruct((rows, -(-heads // 2) * lanes), jnp.bfloat16),
        in_specs=[pl.BlockSpec(memory_space=pltpu.SMEM)] + [vmem] * 6,
        out_specs=vmem,
        cost_estimate=pl.CostEstimate(
            flops=4 * heads * rows * keys * lanes,
            transcendentals=heads * rows * keys,
            bytes_accessed=heads * keys * lanes * 2,
        ),
    )(bounds, proj, gathered, gathered_far, scale_pad, query_segs, key_segs)


def body(
    hidden,
    segment_ids,
    page_slot,
    in_proj,
    out_proj,
    up_proj,
    down_proj,
    score_scale,
    mlp_scale,
    step_rates,
):
    seq_count = lax.axis_size("seq")
    seq_index = lax.axis_index("seq")
    local_tokens = segment_ids.shape[0]
    heads_dev, head_dim = score_scale.shape
    model_width = hidden.shape[1]
    hidden_dev = down_proj.shape[0]
    pages_dev = local_tokens // PAGE
    channels = heads_dev * 2 * head_dim
    state_own = unit_rows(hidden.astype(jnp.float32)).astype(jnp.bfloat16)
    tensor_count = lax.axis_size("tensor")
    tensor_index = lax.axis_index("tensor")
    top = tensor_count // 2
    near = state_own
    bit = 1
    while bit < top:
        came = lax.ppermute(near, "tensor", [(j, j ^ bit) for j in range(tensor_count)])
        low = (tensor_index & bit) == 0
        near = jnp.concatenate([jnp.where(low, near, came), jnp.where(low, came, near)], axis=0)
        bit *= 2
    far = lax.ppermute(near, "tensor", [(j, j ^ top) for j in range(tensor_count)])
    high = (tensor_index & top) // top
    lanes = 2 * head_dim
    width = 3 * head_dim
    weight = in_proj.reshape(model_width, heads_dev * 3 * head_dim)

    def project(rows_in):
        projected = jnp.dot(rows_in, weight, preferred_element_type=jnp.float32)
        pieces = []
        for h in range(heads_dev):
            pieces.append(projected[:, h * width : h * width + head_dim])
            pieces.append(jnp.zeros((rows_in.shape[0], head_dim), jnp.float32))
        query_part = jnp.concatenate(pieces, axis=1)
        kv_part = jnp.concatenate(
            [projected[:, h * width + head_dim : (h + 1) * width] for h in range(heads_dev)],
            axis=1,
        ).astype(jnp.bfloat16)
        return query_part, kv_part

    query_near, kv_near = project(near)
    first_token = seq_index * local_tokens
    seg_rows = -(-local_tokens // channels)
    seg_flat = jnp.pad(segment_ids, (0, seg_rows * channels - local_tokens))
    kv_ext = jnp.concatenate(
        [kv_near, seg_flat.astype(jnp.bfloat16).reshape(seg_rows, channels)], axis=0
    )
    gathered = lax.all_gather(kv_ext, "seq", axis=0, tiled=False)
    query_far, kv_far = project(far)
    gathered_far = lax.all_gather(kv_far, "seq", axis=0, tiled=False)
    near_first = high == 0
    query_pad = jnp.concatenate(
        [jnp.where(near_first, query_near, query_far), jnp.where(near_first, query_far, query_near)],
        axis=0,
    )
    half_tokens = local_tokens // 2
    seg_piece = (
        gathered[:, half_tokens:].reshape(seq_count, seg_rows * channels)[:, :local_tokens]
        .reshape(-1)
        .astype(jnp.int32)
    )
    piece_rows = seq_count * local_tokens
    scale_pad = jnp.pad(score_scale, ((0, 0), (0, lanes - head_dim))).reshape(heads_dev, 1, lanes)
    tiles = local_tokens // Q_TILE
    tile_first = first_token + Q_TILE * jnp.arange(tiles, dtype=jnp.int32)
    tile_seg = segment_ids.reshape(tiles, Q_TILE)[:, 0]
    block_last_seg = seg_piece.reshape(piece_rows // K_TILE, K_TILE)[:, -1]
    block_lo = jnp.sum(
        (block_last_seg[None, :] < tile_seg[:, None]).astype(jnp.int32), axis=1
    )
    block_hi = (tile_first + Q_TILE - 1) // K_TILE
    bounds = jnp.concatenate([block_lo, block_hi, first_token[None], high[None]]).astype(
        jnp.int32
    )
    heads_pad = flash_attend(
        bounds,
        query_pad,
        gathered,
        gathered_far,
        scale_pad,
        segment_ids.reshape(local_tokens, 1),
        seg_piece.reshape(1, piece_rows),
        math.sqrt(head_dim),
        head_dim,
    )
    heads_flat = heads_pad[:, : heads_dev * head_dim]
    slots_dev = page_slot.shape[0] // seq_count
    my_slots = seq_index * slots_dev + jnp.arange(slots_dev, dtype=jnp.int32)
    page_ids = jnp.arange(page_slot.shape[0], dtype=jnp.int32)
    source_page = jnp.sum(
        jnp.where(page_slot[None, :] == my_slots[:, None], page_ids[None, :], 0), axis=1
    )
    half_pages = pages_dev // 2
    taken = []
    for j in range(slots_dev):
        shard = source_page[j] // pages_dev
        quarter = source_page[j] % pages_dev
        at = (shard, (quarter % half_pages) * PAGE, 0)
        from_near = lax.dynamic_slice(gathered, at, (1, PAGE, channels))[0]
        from_far = lax.dynamic_slice(gathered_far, at, (1, PAGE, channels))[0]
        taken.append(jnp.where(quarter // half_pages == high, from_near, from_far))
    page_cache = jnp.stack(taken)
    chosen = heads_flat
    attn_own = scatter_sum(
        jnp.dot(chosen, out_proj, preferred_element_type=jnp.float32).astype(jnp.bfloat16),
        "tensor",
    )
    state_f = state_own.astype(jnp.float32)
    middle = unit_rows(state_f + step_rates[0] * (unit_rows(attn_own) - state_f))
    mid_rows = gather_rows(middle.astype(jnp.bfloat16), "tensor")
    both = jnp.einsum("td,dkf->tkf", mid_rows, up_proj, preferred_element_type=jnp.float32)
    act = (
        both[:, 0] * mlp_scale[0] * jax.nn.silu(both[:, 1] * mlp_scale[1] * math.sqrt(model_width))
    ).astype(jnp.bfloat16)
    chosen = act
    mlp_own = scatter_sum(
        jnp.dot(chosen, down_proj, preferred_element_type=jnp.float32).astype(jnp.bfloat16),
        "tensor",
    )
    final = unit_rows(middle + step_rates[1] * (unit_rows(mlp_own) - middle))
    out_state = (math.sqrt(model_width) * final).astype(jnp.bfloat16)
    return (out_state, page_cache)


def solution(mesh):
    return jax.shard_map(
        body,
        mesh=mesh,
        in_specs=(
            P(("seq", "tensor"), None),
            P("seq"),
            P(),
            P(None, "tensor", None),
            P("tensor", None),
            P(None, None, "tensor"),
            P("tensor", None),
            P("tensor", None),
            P(None, "tensor"),
            P(),
        ),
        out_specs=(P(("seq", "tensor"), None), P("seq", None, "tensor")),
        check_vma=False,
    )
```

```python
import functools
import math

import jax
import jax.numpy as jnp
from jax import lax
from jax.experimental import pallas as pl
from jax.experimental.pallas import tpu as pltpu
from jax.sharding import PartitionSpec as P

PAGE = 128


EPSILON = 1e-06
NEG_LARGE = -1e30


def unit_rows(matrix):
    return matrix * lax.rsqrt(jnp.sum(matrix * matrix, axis=-1, keepdims=True) + EPSILON)


def gather_rows(part, axis):
    count = lax.axis_size(axis)
    index = lax.axis_index(axis)
    rows = part.shape[0]
    out = jnp.zeros((count * rows, *part.shape[1:]), part.dtype)
    out = lax.dynamic_update_slice_in_dim(out, part, index * rows, 0)
    for shift in range(1, count):
        pairs = [(j, (j + shift) % count) for j in range(count)]
        came = lax.ppermute(part, axis, pairs)
        out = lax.dynamic_update_slice_in_dim(out, came, ((index - shift) % count) * rows, 0)
    return out


def scatter_sum(whole, axis):
    count = lax.axis_size(axis)
    index = lax.axis_index(axis)
    blocks = whole.reshape(count, whole.shape[0] // count, *whole.shape[1:])
    total = lax.dynamic_index_in_dim(blocks, index, 0, keepdims=False).astype(jnp.float32)
    for shift in range(1, count):
        pairs = [(j, (j + shift) % count) for j in range(count)]
        send = lax.dynamic_index_in_dim(blocks, (index + shift) % count, 0, keepdims=False)
        total = total + lax.ppermute(send, axis, pairs).astype(jnp.float32)
    return total


Q_TILE = 256
K_TILE = 256


def attend_kernel(
    bounds_ref, proj_ref, kv_ref, scale_ref, qseg_ref, kseg_ref, out_ref, *, factor, half
):
    rows = qseg_ref.shape[0]
    heads = scale_ref.shape[0]
    lanes = 2 * half
    shard_blocks = (kv_ref.shape[1] - kv_ref.shape[1] % K_TILE) // K_TILE
    tiles = rows // Q_TILE
    first = bounds_ref[2 * tiles]
    key_base = bounds_ref[2 * tiles + 1]
    key_lane = lax.broadcasted_iota(jnp.int32, (K_TILE, lanes), 1)
    held = {}
    for head in range(heads):
        scale = scale_ref[head]
        for tile in range(tiles):
            q_raw = proj_ref[tile * Q_TILE : (tile + 1) * Q_TILE, head * lanes : (head + 1) * lanes]
            q_tile = (
                q_raw * lax.rsqrt(jnp.sum(q_raw * q_raw, axis=1, keepdims=True) + EPSILON) * scale
            ).astype(jnp.bfloat16)
            q_seg = qseg_ref[tile * Q_TILE : (tile + 1) * Q_TILE, :]
            q_pos = first + tile * Q_TILE + lax.broadcasted_iota(jnp.int32, (Q_TILE, K_TILE), 0)

            def step(block, carry, q_tile=q_tile, q_seg=q_seg, q_pos=q_pos, head=head, scale=scale):
                top, total, acc = carry
                shard = block // shard_blocks
                row_at = pl.multiple_of((block % shard_blocks) * K_TILE, K_TILE)
                key_at = pl.multiple_of(block * K_TILE, K_TILE)
                kv_blk = kv_ref[shard, pl.ds(row_at, K_TILE), head * lanes : (head + 1) * lanes]
                kv_f = kv_blk.astype(jnp.float32)
                k_sq = jnp.where(key_lane < half, kv_f * kv_f, 0.0)
                k_unit = (
                    kv_f * lax.rsqrt(jnp.sum(k_sq, axis=1, keepdims=True) + EPSILON) * scale
                ).astype(jnp.bfloat16)
                k_seg = kseg_ref[:, pl.ds(key_at, K_TILE)]
                scores = factor * lax.dot_general(
                    q_tile, k_unit, (((1,), (1,)), ((), ())), preferred_element_type=jnp.float32
                )
                k_pos = key_base + key_at + lax.broadcasted_iota(jnp.int32, (Q_TILE, K_TILE), 1)
                allowed = (q_seg == k_seg) & (k_pos <= q_pos)
                scores = jnp.where(allowed, scores, NEG_LARGE)
                new_top = jnp.maximum(top, jnp.max(scores, axis=1, keepdims=True))
                weights = jnp.where(allowed, jnp.exp(scores - new_top), 0.0)
                rescale = jnp.exp(top - new_top)
                new_total = total * rescale + jnp.sum(weights, axis=1, keepdims=True)
                update = jnp.dot(
                    weights.astype(jnp.bfloat16), kv_blk, preferred_element_type=jnp.float32
                )
                return (new_top, new_total, acc * rescale + update)

            start = (
                jnp.full((Q_TILE, 1), NEG_LARGE, jnp.float32),
                jnp.zeros((Q_TILE, 1), jnp.float32),
                jnp.zeros((Q_TILE, lanes), jnp.float32),
            )
            top, total, acc = lax.fori_loop(
                bounds_ref[tile], bounds_ref[tiles + tile] + 1, step, start
            )
            result = acc / total
            pair = head // 2
            rows_at = slice(tile * Q_TILE, (tile + 1) * Q_TILE)
            if head % 2 == 0:
                held[tile] = pltpu.roll(result, half, 1)
                if head == heads - 1:
                    out_ref[rows_at, pair * lanes : (pair + 1) * lanes] = held[tile].astype(
                        out_ref.dtype
                    )
            else:
                joined = jnp.where(
                    lax.broadcasted_iota(jnp.int32, (Q_TILE, lanes), 1) < half, held[tile], result
                )
                out_ref[rows_at, pair * lanes : (pair + 1) * lanes] = joined.astype(out_ref.dtype)


def flash_attend(bounds, proj, gathered, scale_pad, query_segs, key_segs, factor, half):
    rows = query_segs.shape[0]
    heads, _, lanes = scale_pad.shape
    keys = key_segs.shape[1]
    vmem = pl.BlockSpec(memory_space=pltpu.VMEM)
    return pl.pallas_call(
        functools.partial(attend_kernel, factor=factor, half=half),
        out_shape=jax.ShapeDtypeStruct((rows, -(-heads // 2) * lanes), jnp.bfloat16),
        in_specs=[pl.BlockSpec(memory_space=pltpu.SMEM)] + [vmem] * 5,
        out_specs=vmem,
        cost_estimate=pl.CostEstimate(
            flops=4 * heads * rows * keys * lanes,
            transcendentals=heads * rows * keys,
            bytes_accessed=heads * keys * lanes * 2,
        ),
    )(bounds, proj, gathered, scale_pad, query_segs, key_segs)


def body(
    hidden,
    segment_ids,
    page_slot,
    in_proj,
    out_proj,
    up_proj,
    down_proj,
    score_scale,
    mlp_scale,
    step_rates,
):
    seq_count = lax.axis_size("seq")
    seq_index = lax.axis_index("seq")
    local_tokens = segment_ids.shape[0]
    heads_dev, head_dim = score_scale.shape
    model_width = hidden.shape[1]
    hidden_dev = down_proj.shape[0]
    pages_dev = local_tokens // PAGE
    channels = heads_dev * 2 * head_dim
    state_own = unit_rows(hidden.astype(jnp.float32)).astype(jnp.bfloat16)
    gathered_state = gather_rows(state_own, "tensor")
    lanes = 2 * head_dim
    projected = jnp.dot(
        gathered_state,
        in_proj.reshape(model_width, heads_dev * 3 * head_dim),
        preferred_element_type=jnp.float32,
    )
    width = 3 * head_dim
    query_pad = jnp.concatenate(
        sum(
            [
                [
                    projected[:, h * width : h * width + head_dim],
                    jnp.zeros((local_tokens, head_dim), jnp.float32),
                ]
                for h in range(heads_dev)
            ],
            [],
        ),
        axis=1,
    )
    key_value = jnp.concatenate(
        [projected[:, h * width + head_dim : (h + 1) * width] for h in range(heads_dev)], axis=1
    ).astype(jnp.bfloat16)
    first_token = seq_index * local_tokens
    seg_rows = -(-local_tokens // channels)
    seg_flat = jnp.pad(segment_ids, (0, seg_rows * channels - local_tokens))
    kv_ext = jnp.concatenate(
        [key_value, seg_flat.astype(jnp.bfloat16).reshape(seg_rows, channels)], axis=0
    )
    longest = seq_count * local_tokens // 2
    back = min(seq_count - 1, -(-(longest - 1) // local_tokens))
    arrived = []
    for shift in range(back, 0, -1):
        pairs = [(j, j + shift) for j in range(seq_count - shift)]
        arrived.append(lax.ppermute(kv_ext, "seq", pairs))
    window = jnp.stack(arrived + [kv_ext])
    gathered = lax.all_gather(kv_ext, "seq", axis=0, tiled=False)
    window_first = (seq_index - back) * local_tokens
    window_shard = seq_index - back + jnp.arange(back + 1, dtype=jnp.int32)
    seg_piece = (
        window[:, local_tokens:].reshape(back + 1, seg_rows * channels)[:, :local_tokens]
        .astype(jnp.int32)
    )
    seg_piece = jnp.where(window_shard[:, None] >= 0, seg_piece, -1).reshape(-1)
    piece_rows = (back + 1) * local_tokens
    scale_pad = jnp.pad(score_scale, ((0, 0), (0, lanes - head_dim))).reshape(heads_dev, 1, lanes)
    tiles = local_tokens // Q_TILE
    tile_first = first_token + Q_TILE * jnp.arange(tiles, dtype=jnp.int32)
    tile_seg = segment_ids.reshape(tiles, Q_TILE)[:, 0]
    block_last_seg = seg_piece.reshape(piece_rows // K_TILE, K_TILE)[:, -1]
    block_lo = jnp.sum(
        (block_last_seg[None, :] < tile_seg[:, None]).astype(jnp.int32), axis=1
    )
    block_hi = (tile_first + Q_TILE - 1 - window_first) // K_TILE
    bounds = jnp.concatenate(
        [block_lo, block_hi, first_token[None], window_first[None]]
    ).astype(jnp.int32)
    heads_pad = flash_attend(
        bounds,
        query_pad,
        window,
        scale_pad,
        segment_ids.reshape(local_tokens, 1),
        seg_piece.reshape(1, piece_rows),
        math.sqrt(head_dim),
        head_dim,
    )
    heads_flat = heads_pad[:, : heads_dev * head_dim]
    slots_dev = page_slot.shape[0] // seq_count
    my_slots = seq_index * slots_dev + jnp.arange(slots_dev, dtype=jnp.int32)
    page_ids = jnp.arange(page_slot.shape[0], dtype=jnp.int32)
    source_page = jnp.sum(
        jnp.where(page_slot[None, :] == my_slots[:, None], page_ids[None, :], 0), axis=1
    )
    page_cache = jnp.stack(
        [
            lax.dynamic_slice(
                gathered,
                (source_page[j] // pages_dev, (source_page[j] % pages_dev) * PAGE, 0),
                (1, PAGE, channels),
            )[0]
            for j in range(slots_dev)
        ]
    )
    chosen = heads_flat
    attn_own = scatter_sum(
        jnp.dot(chosen, out_proj, preferred_element_type=jnp.float32).astype(jnp.bfloat16),
        "tensor",
    )
    state_f = state_own.astype(jnp.float32)
    middle = unit_rows(state_f + step_rates[0] * (unit_rows(attn_own) - state_f))
    mid_rows = gather_rows(middle.astype(jnp.bfloat16), "tensor")
    both = jnp.einsum("td,dkf->tkf", mid_rows, up_proj, preferred_element_type=jnp.float32)
    act = (
        both[:, 0] * mlp_scale[0] * jax.nn.silu(both[:, 1] * mlp_scale[1] * math.sqrt(model_width))
    ).astype(jnp.bfloat16)
    chosen = act
    mlp_own = scatter_sum(
        jnp.dot(chosen, down_proj, preferred_element_type=jnp.float32).astype(jnp.bfloat16),
        "tensor",
    )
    final = unit_rows(middle + step_rates[1] * (unit_rows(mlp_own) - middle))
    out_state = (math.sqrt(model_width) * final).astype(jnp.bfloat16)
    return (out_state, page_cache)


def solution(mesh):
    return jax.shard_map(
        body,
        mesh=mesh,
        in_specs=(
            P(("seq", "tensor"), None),
            P("seq"),
            P(),
            P(None, "tensor", None),
            P("tensor", None),
            P(None, None, "tensor"),
            P("tensor", None),
            P("tensor", None),
            P(None, "tensor"),
            P(),
        ),
        out_specs=(P(("seq", "tensor"), None), P("seq", None, "tensor")),
        check_vma=False,
    )
```

```python
import functools
import math

import jax
import jax.numpy as jnp
from jax import lax
from jax.experimental import pallas as pl
from jax.experimental.pallas import tpu as pltpu
from jax.sharding import PartitionSpec as P

PAGE = 128


EPSILON = 1e-06
NEG_LARGE = -1e30


def unit_rows(matrix):
    return matrix * lax.rsqrt(jnp.sum(matrix * matrix, axis=-1, keepdims=True) + EPSILON)


def gather_rows(part, axis):
    count = lax.axis_size(axis)
    index = lax.axis_index(axis)
    rows = part.shape[0]
    out = jnp.zeros((count * rows, *part.shape[1:]), part.dtype)
    out = lax.dynamic_update_slice_in_dim(out, part, index * rows, 0)
    for shift in range(1, count):
        pairs = [(j, (j + shift) % count) for j in range(count)]
        came = lax.ppermute(part, axis, pairs)
        out = lax.dynamic_update_slice_in_dim(out, came, ((index - shift) % count) * rows, 0)
    return out


def scatter_sum(whole, axis):
    count = lax.axis_size(axis)
    index = lax.axis_index(axis)
    blocks = whole.reshape(count, whole.shape[0] // count, *whole.shape[1:])
    total = lax.dynamic_index_in_dim(blocks, index, 0, keepdims=False).astype(jnp.float32)
    for shift in range(1, count):
        pairs = [(j, (j + shift) % count) for j in range(count)]
        send = lax.dynamic_index_in_dim(blocks, (index + shift) % count, 0, keepdims=False)
        total = total + lax.ppermute(send, axis, pairs).astype(jnp.float32)
    return total


Q_TILE = 256
K_TILE = 256


def attend_kernel(
    bounds_ref, proj_ref, kv_ref, scale_ref, qseg_ref, kseg_ref, out_ref, *, factor, half
):
    rows = qseg_ref.shape[0]
    heads = scale_ref.shape[0]
    lanes = 2 * half
    shard_blocks = (kv_ref.shape[1] - kv_ref.shape[1] % K_TILE) // K_TILE
    tiles = rows // Q_TILE
    first = bounds_ref[2 * tiles]
    flags_at = 2 * tiles + 1
    blocks = kseg_ref.shape[1] // K_TILE
    fold = factor == 2.0 ** round(math.log2(factor))
    key_lane = lax.broadcasted_iota(jnp.int32, (K_TILE, lanes), 1)
    held = {}
    for head in range(heads):
        scale = scale_ref[head]
        for tile in range(tiles):
            q_raw = proj_ref[tile * Q_TILE : (tile + 1) * Q_TILE, head * lanes : (head + 1) * lanes]
            q_tile = (
                q_raw * lax.rsqrt(jnp.sum(q_raw * q_raw, axis=1, keepdims=True) + EPSILON) * scale
            ).astype(jnp.bfloat16)
            if fold:
                q_tile = q_tile * jnp.asarray(factor, jnp.bfloat16)
            q_seg = qseg_ref[tile * Q_TILE : (tile + 1) * Q_TILE, :]
            q_pos = first + tile * Q_TILE + lax.broadcasted_iota(jnp.int32, (Q_TILE, K_TILE), 0)

            def step(block, carry, q_tile=q_tile, q_seg=q_seg, q_pos=q_pos, head=head, scale=scale,
                     tile=tile):
                top, total, acc = carry
                shard = block // shard_blocks
                row_at = pl.multiple_of((block % shard_blocks) * K_TILE, K_TILE)
                key_at = pl.multiple_of(block * K_TILE, K_TILE)
                kv_blk = kv_ref[shard, pl.ds(row_at, K_TILE), head * lanes : (head + 1) * lanes]
                kv_f = kv_blk.astype(jnp.float32)
                k_sq = jnp.where(key_lane < half, kv_f * kv_f, 0.0)
                k_unit = (
                    kv_f * lax.rsqrt(jnp.sum(k_sq, axis=1, keepdims=True) + EPSILON) * scale
                ).astype(jnp.bfloat16)
                scores = lax.dot_general(
                    q_tile, k_unit, (((1,), (1,)), ((), ())), preferred_element_type=jnp.float32
                )
                if not fold:
                    scores = factor * scores

                def masked(scores):
                    k_seg = kseg_ref[:, pl.ds(key_at, K_TILE)]
                    k_pos = key_at + lax.broadcasted_iota(jnp.int32, (Q_TILE, K_TILE), 1)
                    allowed = (q_seg == k_seg) & (k_pos <= q_pos)
                    return jnp.where(allowed, scores, -jnp.inf)

                scores = lax.cond(
                    bounds_ref[flags_at + tile * blocks + block] > 0,
                    lambda scores: scores,
                    masked,
                    scores,
                )
                new_top = jnp.maximum(top, jnp.max(scores, axis=1, keepdims=True))
                weights = jnp.exp(scores - new_top)
                rescale = jnp.exp(top - new_top)
                new_total = total * rescale + jnp.sum(weights, axis=1, keepdims=True)
                update = jnp.dot(
                    weights.astype(jnp.bfloat16), kv_blk, preferred_element_type=jnp.float32
                )
                return (new_top, new_total, acc * rescale + update)

            start = (
                jnp.full((Q_TILE, 1), NEG_LARGE, jnp.float32),
                jnp.zeros((Q_TILE, 1), jnp.float32),
                jnp.zeros((Q_TILE, lanes), jnp.float32),
            )
            top, total, acc = lax.fori_loop(
                bounds_ref[tile], bounds_ref[tiles + tile] + 1, step, start
            )
            result = acc / total
            pair = head // 2
            rows_at = slice(tile * Q_TILE, (tile + 1) * Q_TILE)
            if head % 2 == 0:
                held[tile] = pltpu.roll(result, half, 1)
                if head == heads - 1:
                    out_ref[rows_at, pair * lanes : (pair + 1) * lanes] = held[tile].astype(
                        out_ref.dtype
                    )
            else:
                joined = jnp.where(
                    lax.broadcasted_iota(jnp.int32, (Q_TILE, lanes), 1) < half, held[tile], result
                )
                out_ref[rows_at, pair * lanes : (pair + 1) * lanes] = joined.astype(out_ref.dtype)


def flash_attend(bounds, proj, gathered, scale_pad, query_segs, key_segs, factor, half):
    rows = query_segs.shape[0]
    heads, _, lanes = scale_pad.shape
    keys = key_segs.shape[1]
    vmem = pl.BlockSpec(memory_space=pltpu.VMEM)
    return pl.pallas_call(
        functools.partial(attend_kernel, factor=factor, half=half),
        out_shape=jax.ShapeDtypeStruct((rows, -(-heads // 2) * lanes), jnp.bfloat16),
        in_specs=[pl.BlockSpec(memory_space=pltpu.SMEM)] + [vmem] * 5,
        out_specs=vmem,
        cost_estimate=pl.CostEstimate(
            flops=4 * heads * rows * keys * lanes,
            transcendentals=heads * rows * keys,
            bytes_accessed=heads * keys * lanes * 2,
        ),
    )(bounds, proj, gathered, scale_pad, query_segs, key_segs)


def body(
    hidden,
    segment_ids,
    page_slot,
    in_proj,
    out_proj,
    up_proj,
    down_proj,
    score_scale,
    mlp_scale,
    step_rates,
):
    seq_count = lax.axis_size("seq")
    seq_index = lax.axis_index("seq")
    local_tokens = segment_ids.shape[0]
    heads_dev, head_dim = score_scale.shape
    model_width = hidden.shape[1]
    hidden_dev = down_proj.shape[0]
    pages_dev = local_tokens // PAGE
    channels = heads_dev * 2 * head_dim
    state_own = unit_rows(hidden.astype(jnp.float32)).astype(jnp.bfloat16)
    gathered_state = gather_rows(state_own, "tensor")
    lanes = 2 * head_dim
    projected = jnp.dot(
        gathered_state,
        in_proj.reshape(model_width, heads_dev * 3 * head_dim),
        preferred_element_type=jnp.float32,
    )
    width = 3 * head_dim
    query_pad = jnp.concatenate(
        sum(
            [
                [
                    projected[:, h * width : h * width + head_dim],
                    jnp.zeros((local_tokens, head_dim), jnp.float32),
                ]
                for h in range(heads_dev)
            ],
            [],
        ),
        axis=1,
    )
    key_value = jnp.concatenate(
        [projected[:, h * width + head_dim : (h + 1) * width] for h in range(heads_dev)], axis=1
    ).astype(jnp.bfloat16)
    first_token = seq_index * local_tokens
    seg_rows = -(-local_tokens // channels)
    seg_flat = jnp.pad(segment_ids, (0, seg_rows * channels - local_tokens))
    kv_ext = jnp.concatenate(
        [key_value, seg_flat.astype(jnp.bfloat16).reshape(seg_rows, channels)], axis=0
    )
    gathered = lax.all_gather(kv_ext, "seq", axis=0, tiled=False)
    seg_piece = (
        gathered[:, local_tokens:].reshape(seq_count, seg_rows * channels)[:, :local_tokens]
        .reshape(-1)
        .astype(jnp.int32)
    )
    piece_rows = seq_count * local_tokens
    scale_pad = jnp.pad(score_scale, ((0, 0), (0, lanes - head_dim))).reshape(heads_dev, 1, lanes)
    tiles = local_tokens // Q_TILE
    tile_first = first_token + Q_TILE * jnp.arange(tiles, dtype=jnp.int32)
    tile_seg = segment_ids.reshape(tiles, Q_TILE)[:, 0]
    block_last_seg = seg_piece.reshape(piece_rows // K_TILE, K_TILE)[:, -1]
    block_lo = jnp.sum(
        (block_last_seg[None, :] < tile_seg[:, None]).astype(jnp.int32), axis=1
    )
    block_hi = (tile_first + Q_TILE - 1) // K_TILE
    block_first_seg = seg_piece.reshape(piece_rows // K_TILE, K_TILE)[:, 0]
    block_last_key = K_TILE * jnp.arange(piece_rows // K_TILE, dtype=jnp.int32) + K_TILE - 1
    tile_last_seg = segment_ids.reshape(tiles, Q_TILE)[:, -1]
    whole_block = (block_last_key[None, :] <= tile_first[:, None]) & (
        block_first_seg[None, :] == tile_last_seg[:, None]
    )
    bounds = jnp.concatenate(
        [block_lo, block_hi, first_token[None], whole_block.reshape(-1).astype(jnp.int32)]
    ).astype(jnp.int32)
    heads_pad = flash_attend(
        bounds,
        query_pad,
        gathered,
        scale_pad,
        segment_ids.reshape(local_tokens, 1),
        seg_piece.reshape(1, piece_rows),
        math.sqrt(head_dim),
        head_dim,
    )
    heads_flat = heads_pad[:, : heads_dev * head_dim]
    slots_dev = page_slot.shape[0] // seq_count
    my_slots = seq_index * slots_dev + jnp.arange(slots_dev, dtype=jnp.int32)
    page_ids = jnp.arange(page_slot.shape[0], dtype=jnp.int32)
    source_page = jnp.sum(
        jnp.where(page_slot[None, :] == my_slots[:, None], page_ids[None, :], 0), axis=1
    )
    page_cache = jnp.stack(
        [
            lax.dynamic_slice(
                gathered,
                (source_page[j] // pages_dev, (source_page[j] % pages_dev) * PAGE, 0),
                (1, PAGE, channels),
            )[0]
            for j in range(slots_dev)
        ]
    )
    chosen = heads_flat
    attn_own = scatter_sum(
        jnp.dot(chosen, out_proj, preferred_element_type=jnp.float32).astype(jnp.bfloat16),
        "tensor",
    )
    state_f = state_own.astype(jnp.float32)
    middle = unit_rows(state_f + step_rates[0] * (unit_rows(attn_own) - state_f))
    mid_rows = gather_rows(middle.astype(jnp.bfloat16), "tensor")
    both = jnp.einsum("td,dkf->tkf", mid_rows, up_proj, preferred_element_type=jnp.float32)
    act = (
        both[:, 0] * mlp_scale[0] * jax.nn.silu(both[:, 1] * mlp_scale[1] * math.sqrt(model_width))
    ).astype(jnp.bfloat16)
    chosen = act
    mlp_own = scatter_sum(
        jnp.dot(chosen, down_proj, preferred_element_type=jnp.float32).astype(jnp.bfloat16),
        "tensor",
    )
    final = unit_rows(middle + step_rates[1] * (unit_rows(mlp_own) - middle))
    out_state = (math.sqrt(model_width) * final).astype(jnp.bfloat16)
    return (out_state, page_cache)


def solution(mesh):
    return jax.shard_map(
        body,
        mesh=mesh,
        in_specs=(
            P(("seq", "tensor"), None),
            P("seq"),
            P(),
            P(None, "tensor", None),
            P("tensor", None),
            P(None, None, "tensor"),
            P("tensor", None),
            P("tensor", None),
            P(None, "tensor"),
            P(),
        ),
        out_specs=(P(("seq", "tensor"), None), P("seq", None, "tensor")),
        check_vma=False,
    )
```

```python
import functools
import math

import jax
import jax.numpy as jnp
from jax import lax
from jax.experimental import pallas as pl
from jax.experimental.pallas import tpu as pltpu
from jax.sharding import PartitionSpec as P

PAGE = 128


EPSILON = 1e-06
NEG_LARGE = -1e30


def unit_rows(matrix):
    return matrix * lax.rsqrt(jnp.sum(matrix * matrix, axis=-1, keepdims=True) + EPSILON)


def gather_rows(part, axis):
    count = lax.axis_size(axis)
    index = lax.axis_index(axis)
    rows = part.shape[0]
    out = jnp.zeros((count * rows, *part.shape[1:]), part.dtype)
    out = lax.dynamic_update_slice_in_dim(out, part, index * rows, 0)
    for shift in range(1, count):
        pairs = [(j, (j + shift) % count) for j in range(count)]
        came = lax.ppermute(part, axis, pairs)
        out = lax.dynamic_update_slice_in_dim(out, came, ((index - shift) % count) * rows, 0)
    return out


def scatter_sum(whole, axis):
    count = lax.axis_size(axis)
    index = lax.axis_index(axis)
    blocks = whole.reshape(count, whole.shape[0] // count, *whole.shape[1:])
    total = lax.dynamic_index_in_dim(blocks, index, 0, keepdims=False).astype(jnp.float32)
    for shift in range(1, count):
        pairs = [(j, (j + shift) % count) for j in range(count)]
        send = lax.dynamic_index_in_dim(blocks, (index + shift) % count, 0, keepdims=False)
        total = total + lax.ppermute(send, axis, pairs).astype(jnp.float32)
    return total


Q_TILE = 512
K_TILE = 256


def attend_kernel(
    bounds_ref, proj_ref, kv_ref, scale_ref, qseg_ref, kseg_ref, out_ref, *, factor, half
):
    rows = qseg_ref.shape[0]
    heads = scale_ref.shape[0]
    lanes = 2 * half
    shard_blocks = (kv_ref.shape[1] - kv_ref.shape[1] % K_TILE) // K_TILE
    tiles = rows // Q_TILE
    first = bounds_ref[2 * tiles]
    key_lane = lax.broadcasted_iota(jnp.int32, (K_TILE, lanes), 1)
    held = {}
    for head in range(heads):
        scale = scale_ref[head]
        for tile in range(tiles):
            q_raw = proj_ref[tile * Q_TILE : (tile + 1) * Q_TILE, head * lanes : (head + 1) * lanes]
            q_tile = (
                q_raw * lax.rsqrt(jnp.sum(q_raw * q_raw, axis=1, keepdims=True) + EPSILON) * scale
            ).astype(jnp.bfloat16)
            q_seg = qseg_ref[tile * Q_TILE : (tile + 1) * Q_TILE, :]
            q_pos = first + tile * Q_TILE + lax.broadcasted_iota(jnp.int32, (Q_TILE, K_TILE), 0)

            def step(block, carry, q_tile=q_tile, q_seg=q_seg, q_pos=q_pos, head=head, scale=scale):
                top, total, acc = carry
                shard = block // shard_blocks
                row_at = pl.multiple_of((block % shard_blocks) * K_TILE, K_TILE)
                key_at = pl.multiple_of(block * K_TILE, K_TILE)
                kv_blk = kv_ref[shard, pl.ds(row_at, K_TILE), head * lanes : (head + 1) * lanes]
                kv_f = kv_blk.astype(jnp.float32)
                k_sq = jnp.where(key_lane < half, kv_f * kv_f, 0.0)
                k_unit = (
                    kv_f * lax.rsqrt(jnp.sum(k_sq, axis=1, keepdims=True) + EPSILON) * scale
                ).astype(jnp.bfloat16)
                k_seg = kseg_ref[:, pl.ds(key_at, K_TILE)]
                scores = factor * lax.dot_general(
                    q_tile, k_unit, (((1,), (1,)), ((), ())), preferred_element_type=jnp.float32
                )
                k_pos = key_at + lax.broadcasted_iota(jnp.int32, (Q_TILE, K_TILE), 1)
                allowed = (q_seg == k_seg) & (k_pos <= q_pos)
                scores = jnp.where(allowed, scores, NEG_LARGE)
                new_top = jnp.maximum(top, jnp.max(scores, axis=1, keepdims=True))
                weights = jnp.where(allowed, jnp.exp(scores - new_top), 0.0)
                rescale = jnp.exp(top - new_top)
                new_total = total * rescale + jnp.sum(weights, axis=1, keepdims=True)
                update = jnp.dot(
                    weights.astype(jnp.bfloat16), kv_blk, preferred_element_type=jnp.float32
                )
                return (new_top, new_total, acc * rescale + update)

            start = (
                jnp.full((Q_TILE, 1), NEG_LARGE, jnp.float32),
                jnp.zeros((Q_TILE, 1), jnp.float32),
                jnp.zeros((Q_TILE, lanes), jnp.float32),
            )
            top, total, acc = lax.fori_loop(
                bounds_ref[tile], bounds_ref[tiles + tile] + 1, step, start
            )
            result = acc / total
            pair = head // 2
            rows_at = slice(tile * Q_TILE, (tile + 1) * Q_TILE)
            if head % 2 == 0:
                held[tile] = pltpu.roll(result, half, 1)
                if head == heads - 1:
                    out_ref[rows_at, pair * lanes : (pair + 1) * lanes] = held[tile].astype(
                        out_ref.dtype
                    )
            else:
                joined = jnp.where(
                    lax.broadcasted_iota(jnp.int32, (Q_TILE, lanes), 1) < half, held[tile], result
                )
                out_ref[rows_at, pair * lanes : (pair + 1) * lanes] = joined.astype(out_ref.dtype)


def flash_attend(bounds, proj, gathered, scale_pad, query_segs, key_segs, factor, half):
    rows = query_segs.shape[0]
    heads, _, lanes = scale_pad.shape
    keys = key_segs.shape[1]
    vmem = pl.BlockSpec(memory_space=pltpu.VMEM)
    return pl.pallas_call(
        functools.partial(attend_kernel, factor=factor, half=half),
        out_shape=jax.ShapeDtypeStruct((rows, -(-heads // 2) * lanes), jnp.bfloat16),
        in_specs=[pl.BlockSpec(memory_space=pltpu.SMEM)] + [vmem] * 5,
        out_specs=vmem,
        cost_estimate=pl.CostEstimate(
            flops=4 * heads * rows * keys * lanes,
            transcendentals=heads * rows * keys,
            bytes_accessed=heads * keys * lanes * 2,
        ),
    )(bounds, proj, gathered, scale_pad, query_segs, key_segs)


def body(
    hidden,
    segment_ids,
    page_slot,
    in_proj,
    out_proj,
    up_proj,
    down_proj,
    score_scale,
    mlp_scale,
    step_rates,
):
    seq_count = lax.axis_size("seq")
    seq_index = lax.axis_index("seq")
    local_tokens = segment_ids.shape[0]
    heads_dev, head_dim = score_scale.shape
    model_width = hidden.shape[1]
    hidden_dev = down_proj.shape[0]
    pages_dev = local_tokens // PAGE
    channels = heads_dev * 2 * head_dim
    state_own = unit_rows(hidden.astype(jnp.float32)).astype(jnp.bfloat16)
    gathered_state = gather_rows(state_own, "tensor")
    lanes = 2 * head_dim
    projected = jnp.dot(
        gathered_state,
        in_proj.reshape(model_width, heads_dev * 3 * head_dim),
        preferred_element_type=jnp.float32,
    )
    width = 3 * head_dim
    query_pad = jnp.concatenate(
        sum(
            [
                [
                    projected[:, h * width : h * width + head_dim],
                    jnp.zeros((local_tokens, head_dim), jnp.float32),
                ]
                for h in range(heads_dev)
            ],
            [],
        ),
        axis=1,
    )
    key_value = jnp.concatenate(
        [projected[:, h * width + head_dim : (h + 1) * width] for h in range(heads_dev)], axis=1
    ).astype(jnp.bfloat16)
    first_token = seq_index * local_tokens
    seg_rows = -(-local_tokens // channels)
    seg_flat = jnp.pad(segment_ids, (0, seg_rows * channels - local_tokens))
    kv_ext = jnp.concatenate(
        [key_value, seg_flat.astype(jnp.bfloat16).reshape(seg_rows, channels)], axis=0
    )
    gathered = lax.all_gather(kv_ext, "seq", axis=0, tiled=False)
    seg_piece = (
        gathered[:, local_tokens:].reshape(seq_count, seg_rows * channels)[:, :local_tokens]
        .reshape(-1)
        .astype(jnp.int32)
    )
    piece_rows = seq_count * local_tokens
    scale_pad = jnp.pad(score_scale, ((0, 0), (0, lanes - head_dim))).reshape(heads_dev, 1, lanes)
    tiles = local_tokens // Q_TILE
    tile_first = first_token + Q_TILE * jnp.arange(tiles, dtype=jnp.int32)
    tile_seg = segment_ids.reshape(tiles, Q_TILE)[:, 0]
    block_last_seg = seg_piece.reshape(piece_rows // K_TILE, K_TILE)[:, -1]
    block_lo = jnp.sum(
        (block_last_seg[None, :] < tile_seg[:, None]).astype(jnp.int32), axis=1
    )
    block_hi = (tile_first + Q_TILE - 1) // K_TILE
    bounds = jnp.concatenate([block_lo, block_hi, first_token[None]]).astype(jnp.int32)
    heads_pad = flash_attend(
        bounds,
        query_pad,
        gathered,
        scale_pad,
        segment_ids.reshape(local_tokens, 1),
        seg_piece.reshape(1, piece_rows),
        math.sqrt(head_dim),
        head_dim,
    )
    heads_flat = heads_pad[:, : heads_dev * head_dim]
    slots_dev = page_slot.shape[0] // seq_count
    my_slots = seq_index * slots_dev + jnp.arange(slots_dev, dtype=jnp.int32)
    page_ids = jnp.arange(page_slot.shape[0], dtype=jnp.int32)
    source_page = jnp.sum(
        jnp.where(page_slot[None, :] == my_slots[:, None], page_ids[None, :], 0), axis=1
    )
    page_cache = jnp.stack(
        [
            lax.dynamic_slice(
                gathered,
                (source_page[j] // pages_dev, (source_page[j] % pages_dev) * PAGE, 0),
                (1, PAGE, channels),
            )[0]
            for j in range(slots_dev)
        ]
    )
    chosen = heads_flat
    attn_own = scatter_sum(
        jnp.dot(chosen, out_proj, preferred_element_type=jnp.float32).astype(jnp.bfloat16),
        "tensor",
    )
    state_f = state_own.astype(jnp.float32)
    middle = unit_rows(state_f + step_rates[0] * (unit_rows(attn_own) - state_f))
    mid_rows = gather_rows(middle.astype(jnp.bfloat16), "tensor")
    both = jnp.einsum("td,dkf->tkf", mid_rows, up_proj, preferred_element_type=jnp.float32)
    act = (
        both[:, 0] * mlp_scale[0] * jax.nn.silu(both[:, 1] * mlp_scale[1] * math.sqrt(model_width))
    ).astype(jnp.bfloat16)
    chosen = act
    mlp_own = scatter_sum(
        jnp.dot(chosen, down_proj, preferred_element_type=jnp.float32).astype(jnp.bfloat16),
        "tensor",
    )
    final = unit_rows(middle + step_rates[1] * (unit_rows(mlp_own) - middle))
    out_state = (math.sqrt(model_width) * final).astype(jnp.bfloat16)
    return (out_state, page_cache)


def solution(mesh):
    return jax.shard_map(
        body,
        mesh=mesh,
        in_specs=(
            P(("seq", "tensor"), None),
            P("seq"),
            P(),
            P(None, "tensor", None),
            P("tensor", None),
            P(None, None, "tensor"),
            P("tensor", None),
            P("tensor", None),
            P(None, "tensor"),
            P(),
        ),
        out_specs=(P(("seq", "tensor"), None), P("seq", None, "tensor")),
        check_vma=False,
    )
```

```python
import functools
import math

import jax
import jax.numpy as jnp
from jax import lax
from jax.experimental import pallas as pl
from jax.experimental.pallas import tpu as pltpu
from jax.sharding import PartitionSpec as P

PAGE = 128


EPSILON = 1e-06
NEG_LARGE = -1e30


def unit_rows(matrix):
    return matrix * lax.rsqrt(jnp.sum(matrix * matrix, axis=-1, keepdims=True) + EPSILON)


def gather_rows(part, axis):
    count = lax.axis_size(axis)
    index = lax.axis_index(axis)
    rows = part.shape[0]
    out = jnp.zeros((count * rows, *part.shape[1:]), part.dtype)
    out = lax.dynamic_update_slice_in_dim(out, part, index * rows, 0)
    for shift in range(1, count):
        pairs = [(j, (j + shift) % count) for j in range(count)]
        came = lax.ppermute(part, axis, pairs)
        out = lax.dynamic_update_slice_in_dim(out, came, ((index - shift) % count) * rows, 0)
    return out


def scatter_sum(whole, axis):
    count = lax.axis_size(axis)
    index = lax.axis_index(axis)
    blocks = whole.reshape(count, whole.shape[0] // count, *whole.shape[1:])
    total = lax.dynamic_index_in_dim(blocks, index, 0, keepdims=False).astype(jnp.float32)
    for shift in range(1, count):
        pairs = [(j, (j + shift) % count) for j in range(count)]
        send = lax.dynamic_index_in_dim(blocks, (index + shift) % count, 0, keepdims=False)
        total = total + lax.ppermute(send, axis, pairs).astype(jnp.float32)
    return total


Q_TILE = 256
K_TILE = 256


def attend_kernel(
    bounds_ref, proj_ref, kv_ref, scale_ref, qseg_ref, kseg_ref, out_ref, *, factor, half
):
    rows = qseg_ref.shape[0]
    heads = scale_ref.shape[0]
    lanes = 2 * half
    shard_blocks = (kv_ref.shape[1] - kv_ref.shape[1] % K_TILE) // K_TILE
    tiles = rows // Q_TILE
    first = bounds_ref[2 * tiles]
    key_lane = lax.broadcasted_iota(jnp.int32, (K_TILE, lanes), 1)
    held = {}
    for head in range(heads):
        scale = scale_ref[head]
        for tile in range(tiles):
            q_raw = proj_ref[tile * Q_TILE : (tile + 1) * Q_TILE, head * lanes : (head + 1) * lanes]
            q_tile = (
                q_raw * lax.rsqrt(jnp.sum(q_raw * q_raw, axis=1, keepdims=True) + EPSILON) * scale
            ).astype(jnp.bfloat16)
            q_seg = qseg_ref[tile * Q_TILE : (tile + 1) * Q_TILE, :]
            q_pos = first + tile * Q_TILE + lax.broadcasted_iota(jnp.int32, (Q_TILE, K_TILE), 0)
            q_norm = jnp.sqrt(
                jnp.sum(jnp.square(q_tile.astype(jnp.float32)), axis=1, keepdims=True)
            )
            shift = factor * q_norm * (jnp.max(scale) * (1.0 + 2.0**-6))

            def step(block, carry, q_tile=q_tile, q_seg=q_seg, q_pos=q_pos, head=head, scale=scale,
                     shift=shift):
                total, acc = carry
                shard = block // shard_blocks
                row_at = pl.multiple_of((block % shard_blocks) * K_TILE, K_TILE)
                key_at = pl.multiple_of(block * K_TILE, K_TILE)
                kv_blk = kv_ref[shard, pl.ds(row_at, K_TILE), head * lanes : (head + 1) * lanes]
                kv_f = kv_blk.astype(jnp.float32)
                k_sq = jnp.where(key_lane < half, kv_f * kv_f, 0.0)
                k_unit = (
                    kv_f * lax.rsqrt(jnp.sum(k_sq, axis=1, keepdims=True) + EPSILON) * scale
                ).astype(jnp.bfloat16)
                k_seg = kseg_ref[:, pl.ds(key_at, K_TILE)]
                scores = factor * lax.dot_general(
                    q_tile, k_unit, (((1,), (1,)), ((), ())), preferred_element_type=jnp.float32
                )
                k_pos = key_at + lax.broadcasted_iota(jnp.int32, (Q_TILE, K_TILE), 1)
                allowed = (q_seg == k_seg) & (k_pos <= q_pos)
                weights = jnp.where(allowed, jnp.exp(scores - shift), 0.0)
                new_total = total + jnp.sum(weights, axis=1, keepdims=True)
                update = jnp.dot(
                    weights.astype(jnp.bfloat16), kv_blk, preferred_element_type=jnp.float32
                )
                return (new_total, acc + update)

            start = (
                jnp.zeros((Q_TILE, 1), jnp.float32),
                jnp.zeros((Q_TILE, lanes), jnp.float32),
            )
            total, acc = lax.fori_loop(
                bounds_ref[tile], bounds_ref[tiles + tile] + 1, step, start
            )
            result = acc / total
            pair = head // 2
            rows_at = slice(tile * Q_TILE, (tile + 1) * Q_TILE)
            if head % 2 == 0:
                held[tile] = pltpu.roll(result, half, 1)
                if head == heads - 1:
                    out_ref[rows_at, pair * lanes : (pair + 1) * lanes] = held[tile].astype(
                        out_ref.dtype
                    )
            else:
                joined = jnp.where(
                    lax.broadcasted_iota(jnp.int32, (Q_TILE, lanes), 1) < half, held[tile], result
                )
                out_ref[rows_at, pair * lanes : (pair + 1) * lanes] = joined.astype(out_ref.dtype)


def flash_attend(bounds, proj, gathered, scale_pad, query_segs, key_segs, factor, half):
    rows = query_segs.shape[0]
    heads, _, lanes = scale_pad.shape
    keys = key_segs.shape[1]
    vmem = pl.BlockSpec(memory_space=pltpu.VMEM)
    return pl.pallas_call(
        functools.partial(attend_kernel, factor=factor, half=half),
        out_shape=jax.ShapeDtypeStruct((rows, -(-heads // 2) * lanes), jnp.bfloat16),
        in_specs=[pl.BlockSpec(memory_space=pltpu.SMEM)] + [vmem] * 5,
        out_specs=vmem,
        cost_estimate=pl.CostEstimate(
            flops=4 * heads * rows * keys * lanes,
            transcendentals=heads * rows * keys,
            bytes_accessed=heads * keys * lanes * 2,
        ),
    )(bounds, proj, gathered, scale_pad, query_segs, key_segs)


def body(
    hidden,
    segment_ids,
    page_slot,
    in_proj,
    out_proj,
    up_proj,
    down_proj,
    score_scale,
    mlp_scale,
    step_rates,
):
    seq_count = lax.axis_size("seq")
    seq_index = lax.axis_index("seq")
    local_tokens = segment_ids.shape[0]
    heads_dev, head_dim = score_scale.shape
    model_width = hidden.shape[1]
    hidden_dev = down_proj.shape[0]
    pages_dev = local_tokens // PAGE
    channels = heads_dev * 2 * head_dim
    state_own = unit_rows(hidden.astype(jnp.float32)).astype(jnp.bfloat16)
    gathered_state = gather_rows(state_own, "tensor")
    lanes = 2 * head_dim
    projected = jnp.dot(
        gathered_state,
        in_proj.reshape(model_width, heads_dev * 3 * head_dim),
        preferred_element_type=jnp.float32,
    )
    width = 3 * head_dim
    query_pad = jnp.concatenate(
        sum(
            [
                [
                    projected[:, h * width : h * width + head_dim],
                    jnp.zeros((local_tokens, head_dim), jnp.float32),
                ]
                for h in range(heads_dev)
            ],
            [],
        ),
        axis=1,
    )
    key_value = jnp.concatenate(
        [projected[:, h * width + head_dim : (h + 1) * width] for h in range(heads_dev)], axis=1
    ).astype(jnp.bfloat16)
    first_token = seq_index * local_tokens
    seg_rows = -(-local_tokens // channels)
    seg_flat = jnp.pad(segment_ids, (0, seg_rows * channels - local_tokens))
    kv_ext = jnp.concatenate(
        [key_value, seg_flat.astype(jnp.bfloat16).reshape(seg_rows, channels)], axis=0
    )
    gathered = lax.all_gather(kv_ext, "seq", axis=0, tiled=False)
    seg_piece = (
        gathered[:, local_tokens:].reshape(seq_count, seg_rows * channels)[:, :local_tokens]
        .reshape(-1)
        .astype(jnp.int32)
    )
    piece_rows = seq_count * local_tokens
    scale_pad = jnp.pad(score_scale, ((0, 0), (0, lanes - head_dim))).reshape(heads_dev, 1, lanes)
    tiles = local_tokens // Q_TILE
    tile_first = first_token + Q_TILE * jnp.arange(tiles, dtype=jnp.int32)
    tile_seg = segment_ids.reshape(tiles, Q_TILE)[:, 0]
    block_last_seg = seg_piece.reshape(piece_rows // K_TILE, K_TILE)[:, -1]
    block_lo = jnp.sum(
        (block_last_seg[None, :] < tile_seg[:, None]).astype(jnp.int32), axis=1
    )
    block_hi = (tile_first + Q_TILE - 1) // K_TILE
    bounds = jnp.concatenate([block_lo, block_hi, first_token[None]]).astype(jnp.int32)
    heads_pad = flash_attend(
        bounds,
        query_pad,
        gathered,
        scale_pad,
        segment_ids.reshape(local_tokens, 1),
        seg_piece.reshape(1, piece_rows),
        math.sqrt(head_dim),
        head_dim,
    )
    heads_flat = heads_pad[:, : heads_dev * head_dim]
    slots_dev = page_slot.shape[0] // seq_count
    my_slots = seq_index * slots_dev + jnp.arange(slots_dev, dtype=jnp.int32)
    page_ids = jnp.arange(page_slot.shape[0], dtype=jnp.int32)
    source_page = jnp.sum(
        jnp.where(page_slot[None, :] == my_slots[:, None], page_ids[None, :], 0), axis=1
    )
    page_cache = jnp.stack(
        [
            lax.dynamic_slice(
                gathered,
                (source_page[j] // pages_dev, (source_page[j] % pages_dev) * PAGE, 0),
                (1, PAGE, channels),
            )[0]
            for j in range(slots_dev)
        ]
    )
    chosen = heads_flat
    attn_own = scatter_sum(
        jnp.dot(chosen, out_proj, preferred_element_type=jnp.float32).astype(jnp.bfloat16),
        "tensor",
    )
    state_f = state_own.astype(jnp.float32)
    middle = unit_rows(state_f + step_rates[0] * (unit_rows(attn_own) - state_f))
    mid_rows = gather_rows(middle.astype(jnp.bfloat16), "tensor")
    both = jnp.einsum("td,dkf->tkf", mid_rows, up_proj, preferred_element_type=jnp.float32)
    act = (
        both[:, 0] * mlp_scale[0] * jax.nn.silu(both[:, 1] * mlp_scale[1] * math.sqrt(model_width))
    ).astype(jnp.bfloat16)
    chosen = act
    mlp_own = scatter_sum(
        jnp.dot(chosen, down_proj, preferred_element_type=jnp.float32).astype(jnp.bfloat16),
        "tensor",
    )
    final = unit_rows(middle + step_rates[1] * (unit_rows(mlp_own) - middle))
    out_state = (math.sqrt(model_width) * final).astype(jnp.bfloat16)
    return (out_state, page_cache)


def solution(mesh):
    return jax.shard_map(
        body,
        mesh=mesh,
        in_specs=(
            P(("seq", "tensor"), None),
            P("seq"),
            P(),
            P(None, "tensor", None),
            P("tensor", None),
            P(None, None, "tensor"),
            P("tensor", None),
            P("tensor", None),
            P(None, "tensor"),
            P(),
        ),
        out_specs=(P(("seq", "tensor"), None), P("seq", None, "tensor")),
        check_vma=False,
    )
```

```python
import functools
import math

import jax
import jax.numpy as jnp
from jax import lax
from jax.experimental import pallas as pl
from jax.experimental.pallas import tpu as pltpu
from jax.sharding import PartitionSpec as P

PAGE = 128


EPSILON = 1e-06
NEG_LARGE = -1e30


def unit_rows(matrix):
    return matrix * lax.rsqrt(jnp.sum(matrix * matrix, axis=-1, keepdims=True) + EPSILON)


def gather_rows(part, axis):
    count = lax.axis_size(axis)
    index = lax.axis_index(axis)
    rows = part.shape[0]
    out = jnp.zeros((count * rows, *part.shape[1:]), part.dtype)
    out = lax.dynamic_update_slice_in_dim(out, part, index * rows, 0)
    for shift in range(1, count):
        pairs = [(j, (j + shift) % count) for j in range(count)]
        came = lax.ppermute(part, axis, pairs)
        out = lax.dynamic_update_slice_in_dim(out, came, ((index - shift) % count) * rows, 0)
    return out


def scatter_sum(whole, axis):
    count = lax.axis_size(axis)
    index = lax.axis_index(axis)
    blocks = whole.reshape(count, whole.shape[0] // count, *whole.shape[1:])
    total = lax.dynamic_index_in_dim(blocks, index, 0, keepdims=False).astype(jnp.float32)
    for shift in range(1, count):
        pairs = [(j, (j + shift) % count) for j in range(count)]
        send = lax.dynamic_index_in_dim(blocks, (index + shift) % count, 0, keepdims=False)
        total = total + lax.ppermute(send, axis, pairs).astype(jnp.float32)
    return total


Q_TILE = 256
K_TILE = 256


def attend_kernel(
    bounds_ref, proj_ref, kv_ref, scale_ref, qseg_ref, kseg_ref, out_ref, *, factor, half
):
    rows = qseg_ref.shape[0]
    heads = scale_ref.shape[0]
    lanes = 2 * half
    shard_blocks = (kv_ref.shape[1] - kv_ref.shape[1] % K_TILE) // K_TILE
    tiles = rows // Q_TILE
    first = bounds_ref[2 * tiles]
    flags_at = 2 * tiles + 1
    blocks = kseg_ref.shape[1] // K_TILE
    fold = factor == 2.0 ** round(math.log2(factor))
    key_lane = lax.broadcasted_iota(jnp.int32, (K_TILE, lanes), 1)
    held = {}
    for head in range(heads):
        scale = scale_ref[head]
        for tile in range(tiles):
            q_raw = proj_ref[tile * Q_TILE : (tile + 1) * Q_TILE, head * lanes : (head + 1) * lanes]
            q_tile = (
                q_raw * lax.rsqrt(jnp.sum(q_raw * q_raw, axis=1, keepdims=True) + EPSILON) * scale
            ).astype(jnp.bfloat16)
            q_seg = qseg_ref[tile * Q_TILE : (tile + 1) * Q_TILE, :]
            q_pos = first + tile * Q_TILE + lax.broadcasted_iota(jnp.int32, (Q_TILE, K_TILE), 0)
            q_norm = jnp.sqrt(
                jnp.sum(jnp.square(q_tile.astype(jnp.float32)), axis=1, keepdims=True)
            )
            shift = factor * q_norm * (jnp.max(scale) * (1.0 + 2.0**-6))
            if fold:
                q_tile = q_tile * jnp.asarray(factor, jnp.bfloat16)

            def step(block, acc, q_tile=q_tile, q_seg=q_seg, q_pos=q_pos, head=head, scale=scale,
                     shift=shift, tile=tile):
                shard = block // shard_blocks
                row_at = pl.multiple_of((block % shard_blocks) * K_TILE, K_TILE)
                key_at = pl.multiple_of(block * K_TILE, K_TILE)
                kv_blk = kv_ref[shard, pl.ds(row_at, K_TILE), head * lanes : (head + 1) * lanes]
                kv_f = kv_blk.astype(jnp.float32)
                k_sq = jnp.where(key_lane < half, kv_f * kv_f, 0.0)
                k_unit = (
                    kv_f * lax.rsqrt(jnp.sum(k_sq, axis=1, keepdims=True) + EPSILON) * scale
                ).astype(jnp.bfloat16)
                scores = lax.dot_general(
                    q_tile, k_unit, (((1,), (1,)), ((), ())), preferred_element_type=jnp.float32
                )
                if not fold:
                    scores = factor * scores

                def masked(scores):
                    k_seg = kseg_ref[:, pl.ds(key_at, K_TILE)]
                    k_pos = key_at + lax.broadcasted_iota(jnp.int32, (Q_TILE, K_TILE), 1)
                    allowed = (q_seg == k_seg) & (k_pos <= q_pos)
                    return jnp.where(allowed, scores, -jnp.inf)

                scores = lax.cond(
                    bounds_ref[flags_at + tile * blocks + block] > 0,
                    lambda scores: scores,
                    masked,
                    scores,
                )
                weights = jnp.exp(scores - shift).astype(jnp.bfloat16)
                kv_sum = jnp.where(key_lane == 0, jnp.ones_like(kv_blk), kv_blk)
                return acc + jnp.dot(weights, kv_sum, preferred_element_type=jnp.float32)

            acc = lax.fori_loop(
                bounds_ref[tile],
                bounds_ref[tiles + tile] + 1,
                step,
                jnp.zeros((Q_TILE, lanes), jnp.float32),
            )
            total = acc[:, 0:1]
            result = acc / total
            pair = head // 2
            rows_at = slice(tile * Q_TILE, (tile + 1) * Q_TILE)
            if head % 2 == 0:
                held[tile] = pltpu.roll(result, half, 1)
                if head == heads - 1:
                    out_ref[rows_at, pair * lanes : (pair + 1) * lanes] = held[tile].astype(
                        out_ref.dtype
                    )
            else:
                joined = jnp.where(
                    lax.broadcasted_iota(jnp.int32, (Q_TILE, lanes), 1) < half, held[tile], result
                )
                out_ref[rows_at, pair * lanes : (pair + 1) * lanes] = joined.astype(out_ref.dtype)


def flash_attend(bounds, proj, gathered, scale_pad, query_segs, key_segs, factor, half):
    rows = query_segs.shape[0]
    heads, _, lanes = scale_pad.shape
    keys = key_segs.shape[1]
    vmem = pl.BlockSpec(memory_space=pltpu.VMEM)
    return pl.pallas_call(
        functools.partial(attend_kernel, factor=factor, half=half),
        out_shape=jax.ShapeDtypeStruct((rows, -(-heads // 2) * lanes), jnp.bfloat16),
        in_specs=[pl.BlockSpec(memory_space=pltpu.SMEM)] + [vmem] * 5,
        out_specs=vmem,
        cost_estimate=pl.CostEstimate(
            flops=4 * heads * rows * keys * lanes,
            transcendentals=heads * rows * keys,
            bytes_accessed=heads * keys * lanes * 2,
        ),
    )(bounds, proj, gathered, scale_pad, query_segs, key_segs)


def body(
    hidden,
    segment_ids,
    page_slot,
    in_proj,
    out_proj,
    up_proj,
    down_proj,
    score_scale,
    mlp_scale,
    step_rates,
):
    seq_count = lax.axis_size("seq")
    seq_index = lax.axis_index("seq")
    local_tokens = segment_ids.shape[0]
    heads_dev, head_dim = score_scale.shape
    model_width = hidden.shape[1]
    hidden_dev = down_proj.shape[0]
    pages_dev = local_tokens // PAGE
    channels = heads_dev * 2 * head_dim
    state_own = unit_rows(hidden.astype(jnp.float32)).astype(jnp.bfloat16)
    gathered_state = gather_rows(state_own, "tensor")
    lanes = 2 * head_dim
    projected = jnp.dot(
        gathered_state,
        in_proj.reshape(model_width, heads_dev * 3 * head_dim),
        preferred_element_type=jnp.float32,
    )
    width = 3 * head_dim
    query_pad = jnp.concatenate(
        sum(
            [
                [
                    projected[:, h * width : h * width + head_dim],
                    jnp.zeros((local_tokens, head_dim), jnp.float32),
                ]
                for h in range(heads_dev)
            ],
            [],
        ),
        axis=1,
    )
    key_value = jnp.concatenate(
        [projected[:, h * width + head_dim : (h + 1) * width] for h in range(heads_dev)], axis=1
    ).astype(jnp.bfloat16)
    first_token = seq_index * local_tokens
    seg_rows = -(-local_tokens // channels)
    seg_flat = jnp.pad(segment_ids, (0, seg_rows * channels - local_tokens))
    kv_ext = jnp.concatenate(
        [key_value, seg_flat.astype(jnp.bfloat16).reshape(seg_rows, channels)], axis=0
    )
    gathered = lax.all_gather(kv_ext, "seq", axis=0, tiled=False)
    seg_piece = (
        gathered[:, local_tokens:].reshape(seq_count, seg_rows * channels)[:, :local_tokens]
        .reshape(-1)
        .astype(jnp.int32)
    )
    piece_rows = seq_count * local_tokens
    scale_pad = jnp.pad(score_scale, ((0, 0), (0, lanes - head_dim))).reshape(heads_dev, 1, lanes)
    tiles = local_tokens // Q_TILE
    tile_first = first_token + Q_TILE * jnp.arange(tiles, dtype=jnp.int32)
    tile_seg = segment_ids.reshape(tiles, Q_TILE)[:, 0]
    block_last_seg = seg_piece.reshape(piece_rows // K_TILE, K_TILE)[:, -1]
    block_lo = jnp.sum(
        (block_last_seg[None, :] < tile_seg[:, None]).astype(jnp.int32), axis=1
    )
    block_hi = (tile_first + Q_TILE - 1) // K_TILE
    block_first_seg = seg_piece.reshape(piece_rows // K_TILE, K_TILE)[:, 0]
    block_last_key = K_TILE * jnp.arange(piece_rows // K_TILE, dtype=jnp.int32) + K_TILE - 1
    tile_last_seg = segment_ids.reshape(tiles, Q_TILE)[:, -1]
    whole_block = (block_last_key[None, :] <= tile_first[:, None]) & (
        block_first_seg[None, :] == tile_last_seg[:, None]
    )
    bounds = jnp.concatenate(
        [block_lo, block_hi, first_token[None], whole_block.reshape(-1).astype(jnp.int32)]
    ).astype(jnp.int32)
    heads_pad = flash_attend(
        bounds,
        query_pad,
        gathered,
        scale_pad,
        segment_ids.reshape(local_tokens, 1),
        seg_piece.reshape(1, piece_rows),
        math.sqrt(head_dim),
        head_dim,
    )
    heads_flat = heads_pad[:, : heads_dev * head_dim]
    slots_dev = page_slot.shape[0] // seq_count
    my_slots = seq_index * slots_dev + jnp.arange(slots_dev, dtype=jnp.int32)
    page_ids = jnp.arange(page_slot.shape[0], dtype=jnp.int32)
    source_page = jnp.sum(
        jnp.where(page_slot[None, :] == my_slots[:, None], page_ids[None, :], 0), axis=1
    )
    page_cache = jnp.stack(
        [
            lax.dynamic_slice(
                gathered,
                (source_page[j] // pages_dev, (source_page[j] % pages_dev) * PAGE, 0),
                (1, PAGE, channels),
            )[0]
            for j in range(slots_dev)
        ]
    )
    chosen = heads_flat
    attn_own = scatter_sum(
        jnp.dot(chosen, out_proj, preferred_element_type=jnp.float32).astype(jnp.bfloat16),
        "tensor",
    )
    state_f = state_own.astype(jnp.float32)
    middle = unit_rows(state_f + step_rates[0] * (unit_rows(attn_own) - state_f))
    mid_rows = gather_rows(middle.astype(jnp.bfloat16), "tensor")
    both = jnp.einsum("td,dkf->tkf", mid_rows, up_proj, preferred_element_type=jnp.float32)
    act = (
        both[:, 0] * mlp_scale[0] * jax.nn.silu(both[:, 1] * mlp_scale[1] * math.sqrt(model_width))
    ).astype(jnp.bfloat16)
    chosen = act
    mlp_own = scatter_sum(
        jnp.dot(chosen, down_proj, preferred_element_type=jnp.float32).astype(jnp.bfloat16),
        "tensor",
    )
    final = unit_rows(middle + step_rates[1] * (unit_rows(mlp_own) - middle))
    out_state = (math.sqrt(model_width) * final).astype(jnp.bfloat16)
    return (out_state, page_cache)


def solution(mesh):
    return jax.shard_map(
        body,
        mesh=mesh,
        in_specs=(
            P(("seq", "tensor"), None),
            P("seq"),
            P(),
            P(None, "tensor", None),
            P("tensor", None),
            P(None, None, "tensor"),
            P("tensor", None),
            P("tensor", None),
            P(None, "tensor"),
            P(),
        ),
        out_specs=(P(("seq", "tensor"), None), P("seq", None, "tensor")),
        check_vma=False,
    )
```

```python
import functools
import math

import jax
import jax.numpy as jnp
from jax import lax
from jax.experimental import pallas as pl
from jax.experimental.pallas import tpu as pltpu
from jax.sharding import PartitionSpec as P

PAGE = 128


EPSILON = 1e-06
NEG_LARGE = -1e30


def unit_rows(matrix):
    return matrix * lax.rsqrt(jnp.sum(matrix * matrix, axis=-1, keepdims=True) + EPSILON)


def gather_rows(part, axis):
    count = lax.axis_size(axis)
    index = lax.axis_index(axis)
    rows = part.shape[0]
    out = jnp.zeros((count * rows, *part.shape[1:]), part.dtype)
    out = lax.dynamic_update_slice_in_dim(out, part, index * rows, 0)
    for shift in range(1, count):
        pairs = [(j, (j + shift) % count) for j in range(count)]
        came = lax.ppermute(part, axis, pairs)
        out = lax.dynamic_update_slice_in_dim(out, came, ((index - shift) % count) * rows, 0)
    return out


def scatter_sum(whole, axis):
    count = lax.axis_size(axis)
    index = lax.axis_index(axis)
    blocks = whole.reshape(count, whole.shape[0] // count, *whole.shape[1:])
    total = lax.dynamic_index_in_dim(blocks, index, 0, keepdims=False).astype(jnp.float32)
    for shift in range(1, count):
        pairs = [(j, (j + shift) % count) for j in range(count)]
        send = lax.dynamic_index_in_dim(blocks, (index + shift) % count, 0, keepdims=False)
        total = total + lax.ppermute(send, axis, pairs).astype(jnp.float32)
    return total


Q_TILE = 256
K_TILE = 256


def attend_kernel(
    bounds_ref, proj_ref, kv_ref, scale_ref, qseg_ref, kseg_ref, out_ref, *, factor, half
):
    rows = qseg_ref.shape[0]
    heads = scale_ref.shape[0]
    lanes = 2 * half
    shard_blocks = (kv_ref.shape[1] - kv_ref.shape[1] % K_TILE) // K_TILE
    tiles = rows // Q_TILE
    first = bounds_ref[2 * tiles]
    fold = factor == 2.0 ** round(math.log2(factor))
    key_lane = lax.broadcasted_iota(jnp.int32, (K_TILE, lanes), 1)
    held = {}
    for head in range(heads):
        scale = scale_ref[head]
        for tile in range(tiles):
            q_raw = proj_ref[tile * Q_TILE : (tile + 1) * Q_TILE, head * lanes : (head + 1) * lanes]
            q_tile = (
                q_raw * lax.rsqrt(jnp.sum(q_raw * q_raw, axis=1, keepdims=True) + EPSILON) * scale
            ).astype(jnp.bfloat16)
            q_seg = qseg_ref[tile * Q_TILE : (tile + 1) * Q_TILE, :]
            q_pos = first + tile * Q_TILE + lax.broadcasted_iota(jnp.int32, (Q_TILE, K_TILE), 0)
            q_norm = jnp.sqrt(
                jnp.sum(jnp.square(q_tile.astype(jnp.float32)), axis=1, keepdims=True)
            )
            shift = factor * q_norm * (jnp.max(scale) * (1.0 + 2.0**-6))
            if fold:
                q_tile = q_tile * jnp.asarray(factor, jnp.bfloat16)

            def step(block, acc, q_tile=q_tile, q_seg=q_seg, q_pos=q_pos, head=head, scale=scale,
                     shift=shift):
                shard = block // shard_blocks
                row_at = pl.multiple_of((block % shard_blocks) * K_TILE, K_TILE)
                key_at = pl.multiple_of(block * K_TILE, K_TILE)
                kv_blk = kv_ref[shard, pl.ds(row_at, K_TILE), head * lanes : (head + 1) * lanes]
                kv_f = kv_blk.astype(jnp.float32)
                k_sq = jnp.where(key_lane < half, kv_f * kv_f, 0.0)
                k_unit = (
                    kv_f * lax.rsqrt(jnp.sum(k_sq, axis=1, keepdims=True) + EPSILON) * scale
                ).astype(jnp.bfloat16)
                k_seg = kseg_ref[:, pl.ds(key_at, K_TILE)]
                scores = lax.dot_general(
                    q_tile, k_unit, (((1,), (1,)), ((), ())), preferred_element_type=jnp.float32
                )
                if not fold:
                    scores = factor * scores
                k_pos = key_at + lax.broadcasted_iota(jnp.int32, (Q_TILE, K_TILE), 1)
                allowed = (q_seg == k_seg) & (k_pos <= q_pos)
                weights = jnp.where(allowed, jnp.exp(scores - shift), 0.0).astype(jnp.bfloat16)
                kv_sum = jnp.where(key_lane == 0, jnp.ones_like(kv_blk), kv_blk)
                return acc + jnp.dot(weights, kv_sum, preferred_element_type=jnp.float32)

            acc = lax.fori_loop(
                bounds_ref[tile],
                bounds_ref[tiles + tile] + 1,
                step,
                jnp.zeros((Q_TILE, lanes), jnp.float32),
            )
            total = acc[:, 0:1]
            result = acc / total
            pair = head // 2
            rows_at = slice(tile * Q_TILE, (tile + 1) * Q_TILE)
            if head % 2 == 0:
                held[tile] = pltpu.roll(result, half, 1)
                if head == heads - 1:
                    out_ref[rows_at, pair * lanes : (pair + 1) * lanes] = held[tile].astype(
                        out_ref.dtype
                    )
            else:
                joined = jnp.where(
                    lax.broadcasted_iota(jnp.int32, (Q_TILE, lanes), 1) < half, held[tile], result
                )
                out_ref[rows_at, pair * lanes : (pair + 1) * lanes] = joined.astype(out_ref.dtype)


def flash_attend(bounds, proj, gathered, scale_pad, query_segs, key_segs, factor, half):
    rows = query_segs.shape[0]
    heads, _, lanes = scale_pad.shape
    keys = key_segs.shape[1]
    vmem = pl.BlockSpec(memory_space=pltpu.VMEM)
    return pl.pallas_call(
        functools.partial(attend_kernel, factor=factor, half=half),
        out_shape=jax.ShapeDtypeStruct((rows, -(-heads // 2) * lanes), jnp.bfloat16),
        in_specs=[pl.BlockSpec(memory_space=pltpu.SMEM)] + [vmem] * 5,
        out_specs=vmem,
        cost_estimate=pl.CostEstimate(
            flops=4 * heads * rows * keys * lanes,
            transcendentals=heads * rows * keys,
            bytes_accessed=heads * keys * lanes * 2,
        ),
    )(bounds, proj, gathered, scale_pad, query_segs, key_segs)


def body(
    hidden,
    segment_ids,
    page_slot,
    in_proj,
    out_proj,
    up_proj,
    down_proj,
    score_scale,
    mlp_scale,
    step_rates,
):
    seq_count = lax.axis_size("seq")
    seq_index = lax.axis_index("seq")
    local_tokens = segment_ids.shape[0]
    heads_dev, head_dim = score_scale.shape
    model_width = hidden.shape[1]
    hidden_dev = down_proj.shape[0]
    pages_dev = local_tokens // PAGE
    channels = heads_dev * 2 * head_dim
    state_own = unit_rows(hidden.astype(jnp.float32)).astype(jnp.bfloat16)
    gathered_state = gather_rows(state_own, "tensor")
    lanes = 2 * head_dim
    projected = jnp.dot(
        gathered_state,
        in_proj.reshape(model_width, heads_dev * 3 * head_dim),
        preferred_element_type=jnp.float32,
    )
    width = 3 * head_dim
    query_pad = jnp.concatenate(
        sum(
            [
                [
                    projected[:, h * width : h * width + head_dim],
                    jnp.zeros((local_tokens, head_dim), jnp.float32),
                ]
                for h in range(heads_dev)
            ],
            [],
        ),
        axis=1,
    )
    key_value = jnp.concatenate(
        [projected[:, h * width + head_dim : (h + 1) * width] for h in range(heads_dev)], axis=1
    ).astype(jnp.bfloat16)
    first_token = seq_index * local_tokens
    seg_rows = -(-local_tokens // channels)
    seg_flat = jnp.pad(segment_ids, (0, seg_rows * channels - local_tokens))
    kv_ext = jnp.concatenate(
        [key_value, seg_flat.astype(jnp.bfloat16).reshape(seg_rows, channels)], axis=0
    )
    gathered = lax.all_gather(kv_ext, "seq", axis=0, tiled=False)
    seg_piece = (
        gathered[:, local_tokens:].reshape(seq_count, seg_rows * channels)[:, :local_tokens]
        .reshape(-1)
        .astype(jnp.int32)
    )
    piece_rows = seq_count * local_tokens
    scale_pad = jnp.pad(score_scale, ((0, 0), (0, lanes - head_dim))).reshape(heads_dev, 1, lanes)
    tiles = local_tokens // Q_TILE
    tile_first = first_token + Q_TILE * jnp.arange(tiles, dtype=jnp.int32)
    tile_seg = segment_ids.reshape(tiles, Q_TILE)[:, 0]
    block_last_seg = seg_piece.reshape(piece_rows // K_TILE, K_TILE)[:, -1]
    block_lo = jnp.sum(
        (block_last_seg[None, :] < tile_seg[:, None]).astype(jnp.int32), axis=1
    )
    block_hi = (tile_first + Q_TILE - 1) // K_TILE
    bounds = jnp.concatenate([block_lo, block_hi, first_token[None]]).astype(jnp.int32)
    heads_pad = flash_attend(
        bounds,
        query_pad,
        gathered,
        scale_pad,
        segment_ids.reshape(local_tokens, 1),
        seg_piece.reshape(1, piece_rows),
        math.sqrt(head_dim),
        head_dim,
    )
    heads_flat = heads_pad[:, : heads_dev * head_dim]
    slots_dev = page_slot.shape[0] // seq_count
    my_slots = seq_index * slots_dev + jnp.arange(slots_dev, dtype=jnp.int32)
    page_ids = jnp.arange(page_slot.shape[0], dtype=jnp.int32)
    source_page = jnp.sum(
        jnp.where(page_slot[None, :] == my_slots[:, None], page_ids[None, :], 0), axis=1
    )
    page_cache = jnp.stack(
        [
            lax.dynamic_slice(
                gathered,
                (source_page[j] // pages_dev, (source_page[j] % pages_dev) * PAGE, 0),
                (1, PAGE, channels),
            )[0]
            for j in range(slots_dev)
        ]
    )
    chosen = heads_flat
    attn_own = scatter_sum(
        jnp.dot(chosen, out_proj, preferred_element_type=jnp.float32).astype(jnp.bfloat16),
        "tensor",
    )
    state_f = state_own.astype(jnp.float32)
    middle = unit_rows(state_f + step_rates[0] * (unit_rows(attn_own) - state_f))
    mid_rows = gather_rows(middle.astype(jnp.bfloat16), "tensor")
    both = jnp.einsum("td,dkf->tkf", mid_rows, up_proj, preferred_element_type=jnp.float32)
    act = (
        both[:, 0] * mlp_scale[0] * jax.nn.silu(both[:, 1] * mlp_scale[1] * math.sqrt(model_width))
    ).astype(jnp.bfloat16)
    chosen = act
    mlp_own = scatter_sum(
        jnp.dot(chosen, down_proj, preferred_element_type=jnp.float32).astype(jnp.bfloat16),
        "tensor",
    )
    final = unit_rows(middle + step_rates[1] * (unit_rows(mlp_own) - middle))
    out_state = (math.sqrt(model_width) * final).astype(jnp.bfloat16)
    return (out_state, page_cache)


def solution(mesh):
    return jax.shard_map(
        body,
        mesh=mesh,
        in_specs=(
            P(("seq", "tensor"), None),
            P("seq"),
            P(),
            P(None, "tensor", None),
            P("tensor", None),
            P(None, None, "tensor"),
            P("tensor", None),
            P("tensor", None),
            P(None, "tensor"),
            P(),
        ),
        out_specs=(P(("seq", "tensor"), None), P("seq", None, "tensor")),
        check_vma=False,
    )
```

```python
import functools
import math

import jax
import jax.numpy as jnp
from jax import lax
from jax.experimental import pallas as pl
from jax.experimental.pallas import tpu as pltpu
from jax.sharding import PartitionSpec as P

PAGE = 128


EPSILON = 1e-06
NEG_LARGE = -1e30


def unit_rows(matrix):
    return matrix * lax.rsqrt(jnp.sum(matrix * matrix, axis=-1, keepdims=True) + EPSILON)


def gather_rows(part, axis):
    count = lax.axis_size(axis)
    index = lax.axis_index(axis)
    rows = part.shape[0]
    out = jnp.zeros((count * rows, *part.shape[1:]), part.dtype)
    out = lax.dynamic_update_slice_in_dim(out, part, index * rows, 0)
    for shift in range(1, count):
        pairs = [(j, (j + shift) % count) for j in range(count)]
        came = lax.ppermute(part, axis, pairs)
        out = lax.dynamic_update_slice_in_dim(out, came, ((index - shift) % count) * rows, 0)
    return out


def scatter_sum(whole, axis):
    count = lax.axis_size(axis)
    index = lax.axis_index(axis)
    blocks = whole.reshape(count, whole.shape[0] // count, *whole.shape[1:])
    total = lax.dynamic_index_in_dim(blocks, index, 0, keepdims=False).astype(jnp.float32)
    for shift in range(1, count):
        pairs = [(j, (j + shift) % count) for j in range(count)]
        send = lax.dynamic_index_in_dim(blocks, (index + shift) % count, 0, keepdims=False)
        total = total + lax.ppermute(send, axis, pairs).astype(jnp.float32)
    return total


Q_TILE = 512
K_TILE = 256


def attend_kernel(
    bounds_ref, proj_ref, kv_ref, scale_ref, qseg_ref, kseg_ref, out_ref, *, factor, half
):
    rows = qseg_ref.shape[0]
    heads = scale_ref.shape[0]
    lanes = 2 * half
    shard_blocks = (kv_ref.shape[1] - kv_ref.shape[1] % K_TILE) // K_TILE
    tiles = rows // Q_TILE
    first = bounds_ref[2 * tiles]
    fold = factor == 2.0 ** round(math.log2(factor))
    key_lane = lax.broadcasted_iota(jnp.int32, (K_TILE, lanes), 1)
    held = {}
    for head in range(heads):
        scale = scale_ref[head]
        for tile in range(tiles):
            q_raw = proj_ref[tile * Q_TILE : (tile + 1) * Q_TILE, head * lanes : (head + 1) * lanes]
            q_tile = (
                q_raw * lax.rsqrt(jnp.sum(q_raw * q_raw, axis=1, keepdims=True) + EPSILON) * scale
            ).astype(jnp.bfloat16)
            q_seg = qseg_ref[tile * Q_TILE : (tile + 1) * Q_TILE, :]
            q_pos = first + tile * Q_TILE + lax.broadcasted_iota(jnp.int32, (Q_TILE, K_TILE), 0)
            q_norm = jnp.sqrt(
                jnp.sum(jnp.square(q_tile.astype(jnp.float32)), axis=1, keepdims=True)
            )
            shift = factor * q_norm * (jnp.max(scale) * (1.0 + 2.0**-6))
            if fold:
                q_tile = q_tile * jnp.asarray(factor, jnp.bfloat16)

            def step(block, acc, q_tile=q_tile, q_seg=q_seg, q_pos=q_pos, head=head, scale=scale,
                     shift=shift):
                shard = block // shard_blocks
                row_at = pl.multiple_of((block % shard_blocks) * K_TILE, K_TILE)
                key_at = pl.multiple_of(block * K_TILE, K_TILE)
                kv_blk = kv_ref[shard, pl.ds(row_at, K_TILE), head * lanes : (head + 1) * lanes]
                kv_f = kv_blk.astype(jnp.float32)
                k_sq = jnp.where(key_lane < half, kv_f * kv_f, 0.0)
                k_unit = (
                    kv_f * lax.rsqrt(jnp.sum(k_sq, axis=1, keepdims=True) + EPSILON) * scale
                ).astype(jnp.bfloat16)
                k_seg = kseg_ref[:, pl.ds(key_at, K_TILE)]
                scores = lax.dot_general(
                    q_tile, k_unit, (((1,), (1,)), ((), ())), preferred_element_type=jnp.float32
                )
                if not fold:
                    scores = factor * scores
                k_pos = key_at + lax.broadcasted_iota(jnp.int32, (Q_TILE, K_TILE), 1)
                allowed = (q_seg == k_seg) & (k_pos <= q_pos)
                weights = jnp.where(allowed, jnp.exp(scores - shift), 0.0).astype(jnp.bfloat16)
                kv_sum = jnp.where(key_lane == 0, jnp.ones_like(kv_blk), kv_blk)
                return acc + jnp.dot(weights, kv_sum, preferred_element_type=jnp.float32)

            acc = lax.fori_loop(
                bounds_ref[tile],
                bounds_ref[tiles + tile] + 1,
                step,
                jnp.zeros((Q_TILE, lanes), jnp.float32),
            )
            total = acc[:, 0:1]
            result = acc / total
            pair = head // 2
            rows_at = slice(tile * Q_TILE, (tile + 1) * Q_TILE)
            if head % 2 == 0:
                held[tile] = pltpu.roll(result, half, 1)
                if head == heads - 1:
                    out_ref[rows_at, pair * lanes : (pair + 1) * lanes] = held[tile].astype(
                        out_ref.dtype
                    )
            else:
                joined = jnp.where(
                    lax.broadcasted_iota(jnp.int32, (Q_TILE, lanes), 1) < half, held[tile], result
                )
                out_ref[rows_at, pair * lanes : (pair + 1) * lanes] = joined.astype(out_ref.dtype)


def flash_attend(bounds, proj, gathered, scale_pad, query_segs, key_segs, factor, half):
    rows = query_segs.shape[0]
    heads, _, lanes = scale_pad.shape
    keys = key_segs.shape[1]
    vmem = pl.BlockSpec(memory_space=pltpu.VMEM)
    return pl.pallas_call(
        functools.partial(attend_kernel, factor=factor, half=half),
        out_shape=jax.ShapeDtypeStruct((rows, -(-heads // 2) * lanes), jnp.bfloat16),
        in_specs=[pl.BlockSpec(memory_space=pltpu.SMEM)] + [vmem] * 5,
        out_specs=vmem,
        cost_estimate=pl.CostEstimate(
            flops=4 * heads * rows * keys * lanes,
            transcendentals=heads * rows * keys,
            bytes_accessed=heads * keys * lanes * 2,
        ),
    )(bounds, proj, gathered, scale_pad, query_segs, key_segs)


def body(
    hidden,
    segment_ids,
    page_slot,
    in_proj,
    out_proj,
    up_proj,
    down_proj,
    score_scale,
    mlp_scale,
    step_rates,
):
    seq_count = lax.axis_size("seq")
    seq_index = lax.axis_index("seq")
    local_tokens = segment_ids.shape[0]
    heads_dev, head_dim = score_scale.shape
    model_width = hidden.shape[1]
    hidden_dev = down_proj.shape[0]
    pages_dev = local_tokens // PAGE
    channels = heads_dev * 2 * head_dim
    state_own = unit_rows(hidden.astype(jnp.float32)).astype(jnp.bfloat16)
    gathered_state = gather_rows(state_own, "tensor")
    lanes = 2 * head_dim
    projected = jnp.dot(
        gathered_state,
        in_proj.reshape(model_width, heads_dev * 3 * head_dim),
        preferred_element_type=jnp.float32,
    )
    width = 3 * head_dim
    query_pad = jnp.concatenate(
        sum(
            [
                [
                    projected[:, h * width : h * width + head_dim],
                    jnp.zeros((local_tokens, head_dim), jnp.float32),
                ]
                for h in range(heads_dev)
            ],
            [],
        ),
        axis=1,
    )
    key_value = jnp.concatenate(
        [projected[:, h * width + head_dim : (h + 1) * width] for h in range(heads_dev)], axis=1
    ).astype(jnp.bfloat16)
    first_token = seq_index * local_tokens
    seg_rows = -(-local_tokens // channels)
    seg_flat = jnp.pad(segment_ids, (0, seg_rows * channels - local_tokens))
    kv_ext = jnp.concatenate(
        [key_value, seg_flat.astype(jnp.bfloat16).reshape(seg_rows, channels)], axis=0
    )
    gathered = lax.all_gather(kv_ext, "seq", axis=0, tiled=False)
    seg_piece = (
        gathered[:, local_tokens:].reshape(seq_count, seg_rows * channels)[:, :local_tokens]
        .reshape(-1)
        .astype(jnp.int32)
    )
    piece_rows = seq_count * local_tokens
    scale_pad = jnp.pad(score_scale, ((0, 0), (0, lanes - head_dim))).reshape(heads_dev, 1, lanes)
    tiles = local_tokens // Q_TILE
    tile_first = first_token + Q_TILE * jnp.arange(tiles, dtype=jnp.int32)
    tile_seg = segment_ids.reshape(tiles, Q_TILE)[:, 0]
    block_last_seg = seg_piece.reshape(piece_rows // K_TILE, K_TILE)[:, -1]
    block_lo = jnp.sum(
        (block_last_seg[None, :] < tile_seg[:, None]).astype(jnp.int32), axis=1
    )
    block_hi = (tile_first + Q_TILE - 1) // K_TILE
    bounds = jnp.concatenate([block_lo, block_hi, first_token[None]]).astype(jnp.int32)
    heads_pad = flash_attend(
        bounds,
        query_pad,
        gathered,
        scale_pad,
        segment_ids.reshape(local_tokens, 1),
        seg_piece.reshape(1, piece_rows),
        math.sqrt(head_dim),
        head_dim,
    )
    heads_flat = heads_pad[:, : heads_dev * head_dim]
    slots_dev = page_slot.shape[0] // seq_count
    my_slots = seq_index * slots_dev + jnp.arange(slots_dev, dtype=jnp.int32)
    page_ids = jnp.arange(page_slot.shape[0], dtype=jnp.int32)
    source_page = jnp.sum(
        jnp.where(page_slot[None, :] == my_slots[:, None], page_ids[None, :], 0), axis=1
    )
    page_cache = jnp.stack(
        [
            lax.dynamic_slice(
                gathered,
                (source_page[j] // pages_dev, (source_page[j] % pages_dev) * PAGE, 0),
                (1, PAGE, channels),
            )[0]
            for j in range(slots_dev)
        ]
    )
    chosen = heads_flat
    attn_own = scatter_sum(
        jnp.dot(chosen, out_proj, preferred_element_type=jnp.float32).astype(jnp.bfloat16),
        "tensor",
    )
    state_f = state_own.astype(jnp.float32)
    middle = unit_rows(state_f + step_rates[0] * (unit_rows(attn_own) - state_f))
    mid_rows = gather_rows(middle.astype(jnp.bfloat16), "tensor")
    both = jnp.einsum("td,dkf->tkf", mid_rows, up_proj, preferred_element_type=jnp.float32)
    act = (
        both[:, 0] * mlp_scale[0] * jax.nn.silu(both[:, 1] * mlp_scale[1] * math.sqrt(model_width))
    ).astype(jnp.bfloat16)
    chosen = act
    mlp_own = scatter_sum(
        jnp.dot(chosen, down_proj, preferred_element_type=jnp.float32).astype(jnp.bfloat16),
        "tensor",
    )
    final = unit_rows(middle + step_rates[1] * (unit_rows(mlp_own) - middle))
    out_state = (math.sqrt(model_width) * final).astype(jnp.bfloat16)
    return (out_state, page_cache)


def solution(mesh):
    return jax.shard_map(
        body,
        mesh=mesh,
        in_specs=(
            P(("seq", "tensor"), None),
            P("seq"),
            P(),
            P(None, "tensor", None),
            P("tensor", None),
            P(None, None, "tensor"),
            P("tensor", None),
            P("tensor", None),
            P(None, "tensor"),
            P(),
        ),
        out_specs=(P(("seq", "tensor"), None), P("seq", None, "tensor")),
        check_vma=False,
    )
```

```python
import functools
import math

import jax
import jax.numpy as jnp
from jax import lax
from jax.experimental import pallas as pl
from jax.experimental.pallas import tpu as pltpu
from jax.sharding import PartitionSpec as P

PAGE = 128


EPSILON = 1e-06
NEG_LARGE = -1e30


def unit_rows(matrix):
    return matrix * lax.rsqrt(jnp.sum(matrix * matrix, axis=-1, keepdims=True) + EPSILON)


def gather_rows(part, axis):
    count = lax.axis_size(axis)
    index = lax.axis_index(axis)
    rows = part.shape[0]
    out = jnp.zeros((count * rows, *part.shape[1:]), part.dtype)
    out = lax.dynamic_update_slice_in_dim(out, part, index * rows, 0)
    for shift in range(1, count):
        pairs = [(j, (j + shift) % count) for j in range(count)]
        came = lax.ppermute(part, axis, pairs)
        out = lax.dynamic_update_slice_in_dim(out, came, ((index - shift) % count) * rows, 0)
    return out


def scatter_sum(whole, axis):
    count = lax.axis_size(axis)
    index = lax.axis_index(axis)
    blocks = whole.reshape(count, whole.shape[0] // count, *whole.shape[1:])
    total = lax.dynamic_index_in_dim(blocks, index, 0, keepdims=False).astype(jnp.float32)
    for shift in range(1, count):
        pairs = [(j, (j + shift) % count) for j in range(count)]
        send = lax.dynamic_index_in_dim(blocks, (index + shift) % count, 0, keepdims=False)
        total = total + lax.ppermute(send, axis, pairs).astype(jnp.float32)
    return total


Q_TILE = 512
K_TILE = 512


def attend_kernel(
    bounds_ref, proj_ref, kv_ref, scale_ref, qseg_ref, kseg_ref, out_ref, *, factor, half
):
    rows = qseg_ref.shape[0]
    heads = scale_ref.shape[0]
    lanes = 2 * half
    shard_blocks = (kv_ref.shape[1] - kv_ref.shape[1] % K_TILE) // K_TILE
    tiles = rows // Q_TILE
    first = bounds_ref[2 * tiles]
    fold = factor == 2.0 ** round(math.log2(factor))
    key_lane = lax.broadcasted_iota(jnp.int32, (K_TILE, lanes), 1)
    held = {}
    for head in range(heads):
        scale = scale_ref[head]
        for tile in range(tiles):
            q_raw = proj_ref[tile * Q_TILE : (tile + 1) * Q_TILE, head * lanes : (head + 1) * lanes]
            q_tile = (
                q_raw * lax.rsqrt(jnp.sum(q_raw * q_raw, axis=1, keepdims=True) + EPSILON) * scale
            ).astype(jnp.bfloat16)
            q_seg = qseg_ref[tile * Q_TILE : (tile + 1) * Q_TILE, :]
            q_pos = first + tile * Q_TILE + lax.broadcasted_iota(jnp.int32, (Q_TILE, K_TILE), 0)
            q_norm = jnp.sqrt(
                jnp.sum(jnp.square(q_tile.astype(jnp.float32)), axis=1, keepdims=True)
            )
            shift = factor * q_norm * (jnp.max(scale) * (1.0 + 2.0**-6))
            if fold:
                q_tile = q_tile * jnp.asarray(factor, jnp.bfloat16)

            def step(block, acc, q_tile=q_tile, q_seg=q_seg, q_pos=q_pos, head=head, scale=scale,
                     shift=shift):
                shard = block // shard_blocks
                row_at = pl.multiple_of((block % shard_blocks) * K_TILE, K_TILE)
                key_at = pl.multiple_of(block * K_TILE, K_TILE)
                kv_blk = kv_ref[shard, pl.ds(row_at, K_TILE), head * lanes : (head + 1) * lanes]
                kv_f = kv_blk.astype(jnp.float32)
                k_sq = jnp.where(key_lane < half, kv_f * kv_f, 0.0)
                k_unit = (
                    kv_f * lax.rsqrt(jnp.sum(k_sq, axis=1, keepdims=True) + EPSILON) * scale
                ).astype(jnp.bfloat16)
                k_seg = kseg_ref[:, pl.ds(key_at, K_TILE)]
                scores = lax.dot_general(
                    q_tile, k_unit, (((1,), (1,)), ((), ())), preferred_element_type=jnp.float32
                )
                if not fold:
                    scores = factor * scores
                k_pos = key_at + lax.broadcasted_iota(jnp.int32, (Q_TILE, K_TILE), 1)
                allowed = (q_seg == k_seg) & (k_pos <= q_pos)
                weights = jnp.where(allowed, jnp.exp(scores - shift), 0.0).astype(jnp.bfloat16)
                kv_sum = jnp.where(key_lane == 0, jnp.ones_like(kv_blk), kv_blk)
                return acc + jnp.dot(weights, kv_sum, preferred_element_type=jnp.float32)

            acc = lax.fori_loop(
                bounds_ref[tile],
                bounds_ref[tiles + tile] + 1,
                step,
                jnp.zeros((Q_TILE, lanes), jnp.float32),
            )
            total = acc[:, 0:1]
            result = acc / total
            pair = head // 2
            rows_at = slice(tile * Q_TILE, (tile + 1) * Q_TILE)
            if head % 2 == 0:
                held[tile] = pltpu.roll(result, half, 1)
                if head == heads - 1:
                    out_ref[rows_at, pair * lanes : (pair + 1) * lanes] = held[tile].astype(
                        out_ref.dtype
                    )
            else:
                joined = jnp.where(
                    lax.broadcasted_iota(jnp.int32, (Q_TILE, lanes), 1) < half, held[tile], result
                )
                out_ref[rows_at, pair * lanes : (pair + 1) * lanes] = joined.astype(out_ref.dtype)


def flash_attend(bounds, proj, gathered, scale_pad, query_segs, key_segs, factor, half):
    rows = query_segs.shape[0]
    heads, _, lanes = scale_pad.shape
    keys = key_segs.shape[1]
    vmem = pl.BlockSpec(memory_space=pltpu.VMEM)
    return pl.pallas_call(
        functools.partial(attend_kernel, factor=factor, half=half),
        out_shape=jax.ShapeDtypeStruct((rows, -(-heads // 2) * lanes), jnp.bfloat16),
        in_specs=[pl.BlockSpec(memory_space=pltpu.SMEM)] + [vmem] * 5,
        out_specs=vmem,
        cost_estimate=pl.CostEstimate(
            flops=4 * heads * rows * keys * lanes,
            transcendentals=heads * rows * keys,
            bytes_accessed=heads * keys * lanes * 2,
        ),
    )(bounds, proj, gathered, scale_pad, query_segs, key_segs)


def body(
    hidden,
    segment_ids,
    page_slot,
    in_proj,
    out_proj,
    up_proj,
    down_proj,
    score_scale,
    mlp_scale,
    step_rates,
):
    seq_count = lax.axis_size("seq")
    seq_index = lax.axis_index("seq")
    local_tokens = segment_ids.shape[0]
    heads_dev, head_dim = score_scale.shape
    model_width = hidden.shape[1]
    hidden_dev = down_proj.shape[0]
    pages_dev = local_tokens // PAGE
    channels = heads_dev * 2 * head_dim
    state_own = unit_rows(hidden.astype(jnp.float32)).astype(jnp.bfloat16)
    gathered_state = gather_rows(state_own, "tensor")
    lanes = 2 * head_dim
    projected = jnp.dot(
        gathered_state,
        in_proj.reshape(model_width, heads_dev * 3 * head_dim),
        preferred_element_type=jnp.float32,
    )
    width = 3 * head_dim
    query_pad = jnp.concatenate(
        sum(
            [
                [
                    projected[:, h * width : h * width + head_dim],
                    jnp.zeros((local_tokens, head_dim), jnp.float32),
                ]
                for h in range(heads_dev)
            ],
            [],
        ),
        axis=1,
    )
    key_value = jnp.concatenate(
        [projected[:, h * width + head_dim : (h + 1) * width] for h in range(heads_dev)], axis=1
    ).astype(jnp.bfloat16)
    first_token = seq_index * local_tokens
    seg_rows = -(-local_tokens // channels)
    seg_flat = jnp.pad(segment_ids, (0, seg_rows * channels - local_tokens))
    kv_ext = jnp.concatenate(
        [key_value, seg_flat.astype(jnp.bfloat16).reshape(seg_rows, channels)], axis=0
    )
    gathered = lax.all_gather(kv_ext, "seq", axis=0, tiled=False)
    seg_piece = (
        gathered[:, local_tokens:].reshape(seq_count, seg_rows * channels)[:, :local_tokens]
        .reshape(-1)
        .astype(jnp.int32)
    )
    piece_rows = seq_count * local_tokens
    scale_pad = jnp.pad(score_scale, ((0, 0), (0, lanes - head_dim))).reshape(heads_dev, 1, lanes)
    tiles = local_tokens // Q_TILE
    tile_first = first_token + Q_TILE * jnp.arange(tiles, dtype=jnp.int32)
    tile_seg = segment_ids.reshape(tiles, Q_TILE)[:, 0]
    block_last_seg = seg_piece.reshape(piece_rows // K_TILE, K_TILE)[:, -1]
    block_lo = jnp.sum(
        (block_last_seg[None, :] < tile_seg[:, None]).astype(jnp.int32), axis=1
    )
    block_hi = (tile_first + Q_TILE - 1) // K_TILE
    bounds = jnp.concatenate([block_lo, block_hi, first_token[None]]).astype(jnp.int32)
    heads_pad = flash_attend(
        bounds,
        query_pad,
        gathered,
        scale_pad,
        segment_ids.reshape(local_tokens, 1),
        seg_piece.reshape(1, piece_rows),
        math.sqrt(head_dim),
        head_dim,
    )
    heads_flat = heads_pad[:, : heads_dev * head_dim]
    slots_dev = page_slot.shape[0] // seq_count
    my_slots = seq_index * slots_dev + jnp.arange(slots_dev, dtype=jnp.int32)
    page_ids = jnp.arange(page_slot.shape[0], dtype=jnp.int32)
    source_page = jnp.sum(
        jnp.where(page_slot[None, :] == my_slots[:, None], page_ids[None, :], 0), axis=1
    )
    page_cache = jnp.stack(
        [
            lax.dynamic_slice(
                gathered,
                (source_page[j] // pages_dev, (source_page[j] % pages_dev) * PAGE, 0),
                (1, PAGE, channels),
            )[0]
            for j in range(slots_dev)
        ]
    )
    chosen = heads_flat
    attn_own = scatter_sum(
        jnp.dot(chosen, out_proj, preferred_element_type=jnp.float32).astype(jnp.bfloat16),
        "tensor",
    )
    state_f = state_own.astype(jnp.float32)
    middle = unit_rows(state_f + step_rates[0] * (unit_rows(attn_own) - state_f))
    mid_rows = gather_rows(middle.astype(jnp.bfloat16), "tensor")
    both = jnp.einsum("td,dkf->tkf", mid_rows, up_proj, preferred_element_type=jnp.float32)
    act = (
        both[:, 0] * mlp_scale[0] * jax.nn.silu(both[:, 1] * mlp_scale[1] * math.sqrt(model_width))
    ).astype(jnp.bfloat16)
    chosen = act
    mlp_own = scatter_sum(
        jnp.dot(chosen, down_proj, preferred_element_type=jnp.float32).astype(jnp.bfloat16),
        "tensor",
    )
    final = unit_rows(middle + step_rates[1] * (unit_rows(mlp_own) - middle))
    out_state = (math.sqrt(model_width) * final).astype(jnp.bfloat16)
    return (out_state, page_cache)


def solution(mesh):
    return jax.shard_map(
        body,
        mesh=mesh,
        in_specs=(
            P(("seq", "tensor"), None),
            P("seq"),
            P(),
            P(None, "tensor", None),
            P("tensor", None),
            P(None, None, "tensor"),
            P("tensor", None),
            P("tensor", None),
            P(None, "tensor"),
            P(),
        ),
        out_specs=(P(("seq", "tensor"), None), P("seq", None, "tensor")),
        check_vma=False,
    )
```

```python
import functools
import math

import jax
import jax.numpy as jnp
from jax import lax
from jax.experimental import pallas as pl
from jax.experimental.pallas import tpu as pltpu
from jax.sharding import PartitionSpec as P

PAGE = 128


EPSILON = 1e-06
NEG_LARGE = -1e30


def unit_rows(matrix):
    return matrix * lax.rsqrt(jnp.sum(matrix * matrix, axis=-1, keepdims=True) + EPSILON)


def gather_rows(part, axis):
    count = lax.axis_size(axis)
    index = lax.axis_index(axis)
    rows = part.shape[0]
    out = jnp.zeros((count * rows, *part.shape[1:]), part.dtype)
    out = lax.dynamic_update_slice_in_dim(out, part, index * rows, 0)
    for shift in range(1, count):
        pairs = [(j, (j + shift) % count) for j in range(count)]
        came = lax.ppermute(part, axis, pairs)
        out = lax.dynamic_update_slice_in_dim(out, came, ((index - shift) % count) * rows, 0)
    return out


def scatter_sum(whole, axis):
    count = lax.axis_size(axis)
    index = lax.axis_index(axis)
    blocks = whole.reshape(count, whole.shape[0] // count, *whole.shape[1:])
    total = lax.dynamic_index_in_dim(blocks, index, 0, keepdims=False).astype(jnp.float32)
    for shift in range(1, count):
        pairs = [(j, (j + shift) % count) for j in range(count)]
        send = lax.dynamic_index_in_dim(blocks, (index + shift) % count, 0, keepdims=False)
        total = total + lax.ppermute(send, axis, pairs).astype(jnp.float32)
    return total


Q_TILE = 512
K_TILE = 512


def attend_kernel(
    bounds_ref, proj_ref, kv_ref, scale_ref, qseg_ref, kseg_ref, out_ref, *, factor, half
):
    rows = qseg_ref.shape[0]
    heads = scale_ref.shape[0]
    lanes = 2 * half
    shard_blocks = (kv_ref.shape[1] - kv_ref.shape[1] % K_TILE) // K_TILE
    tiles = rows // Q_TILE
    first = bounds_ref[2 * tiles]
    fold = factor == 2.0 ** round(math.log2(factor))
    key_lane = lax.broadcasted_iota(jnp.int32, (K_TILE, lanes), 1)
    held = {}
    for head in range(heads):
        scale = scale_ref[head]
        for tile in range(tiles):
            q_raw = proj_ref[tile * Q_TILE : (tile + 1) * Q_TILE, head * lanes : (head + 1) * lanes]
            q_tile = (
                q_raw * lax.rsqrt(jnp.sum(q_raw * q_raw, axis=1, keepdims=True) + EPSILON) * scale
            ).astype(jnp.bfloat16)
            q_seg = qseg_ref[tile * Q_TILE : (tile + 1) * Q_TILE, :]
            q_pos = first + tile * Q_TILE + lax.broadcasted_iota(jnp.int32, (Q_TILE, K_TILE), 0)
            q_norm = jnp.sqrt(
                jnp.sum(jnp.square(q_tile.astype(jnp.float32)), axis=1, keepdims=True)
            )
            shift = factor * q_norm * (jnp.max(scale) * (1.0 + 2.0**-6))
            if fold:
                q_tile = q_tile * jnp.asarray(factor, jnp.bfloat16)

            def step(block, acc, q_tile=q_tile, q_seg=q_seg, q_pos=q_pos, head=head, scale=scale,
                     shift=shift):
                shard = block // shard_blocks
                row_at = pl.multiple_of((block % shard_blocks) * K_TILE, K_TILE)
                key_at = pl.multiple_of(block * K_TILE, K_TILE)
                kv_blk = kv_ref[shard, pl.ds(row_at, K_TILE), head * lanes : (head + 1) * lanes]
                kv_f = kv_blk.astype(jnp.float32)
                k_sq = jnp.where(key_lane < half, kv_f * kv_f, 0.0)
                k_unit = (
                    kv_f * lax.rsqrt(jnp.sum(k_sq, axis=1, keepdims=True) + EPSILON) * scale
                ).astype(jnp.bfloat16)
                scores = lax.dot_general(
                    q_tile, k_unit, (((1,), (1,)), ((), ())), preferred_element_type=jnp.float32
                )
                if not fold:
                    scores = factor * scores
                k_pos = key_at + lax.broadcasted_iota(jnp.int32, (Q_TILE, K_TILE), 1)
                allowed = (k_pos >= q_seg) & (k_pos <= q_pos)
                weights = jnp.where(allowed, jnp.exp(scores - shift), 0.0).astype(jnp.bfloat16)
                kv_sum = jnp.where(key_lane == 0, jnp.ones_like(kv_blk), kv_blk)
                return acc + jnp.dot(weights, kv_sum, preferred_element_type=jnp.float32)

            acc = lax.fori_loop(
                bounds_ref[tile],
                bounds_ref[tiles + tile] + 1,
                step,
                jnp.zeros((Q_TILE, lanes), jnp.float32),
            )
            total = acc[:, 0:1]
            result = acc / total
            pair = head // 2
            rows_at = slice(tile * Q_TILE, (tile + 1) * Q_TILE)
            if head % 2 == 0:
                held[tile] = pltpu.roll(result, half, 1)
                if head == heads - 1:
                    out_ref[rows_at, pair * lanes : (pair + 1) * lanes] = held[tile].astype(
                        out_ref.dtype
                    )
            else:
                joined = jnp.where(
                    lax.broadcasted_iota(jnp.int32, (Q_TILE, lanes), 1) < half, held[tile], result
                )
                out_ref[rows_at, pair * lanes : (pair + 1) * lanes] = joined.astype(out_ref.dtype)


def flash_attend(bounds, proj, gathered, scale_pad, query_segs, key_segs, factor, half):
    rows = query_segs.shape[0]
    heads, _, lanes = scale_pad.shape
    keys = key_segs.shape[1]
    vmem = pl.BlockSpec(memory_space=pltpu.VMEM)
    return pl.pallas_call(
        functools.partial(attend_kernel, factor=factor, half=half),
        out_shape=jax.ShapeDtypeStruct((rows, -(-heads // 2) * lanes), jnp.bfloat16),
        in_specs=[pl.BlockSpec(memory_space=pltpu.SMEM)] + [vmem] * 5,
        out_specs=vmem,
        cost_estimate=pl.CostEstimate(
            flops=4 * heads * rows * keys * lanes,
            transcendentals=heads * rows * keys,
            bytes_accessed=heads * keys * lanes * 2,
        ),
    )(bounds, proj, gathered, scale_pad, query_segs, key_segs)


def body(
    hidden,
    segment_ids,
    page_slot,
    in_proj,
    out_proj,
    up_proj,
    down_proj,
    score_scale,
    mlp_scale,
    step_rates,
):
    seq_count = lax.axis_size("seq")
    seq_index = lax.axis_index("seq")
    local_tokens = segment_ids.shape[0]
    heads_dev, head_dim = score_scale.shape
    model_width = hidden.shape[1]
    hidden_dev = down_proj.shape[0]
    pages_dev = local_tokens // PAGE
    channels = heads_dev * 2 * head_dim
    state_own = unit_rows(hidden.astype(jnp.float32)).astype(jnp.bfloat16)
    gathered_state = gather_rows(state_own, "tensor")
    lanes = 2 * head_dim
    projected = jnp.dot(
        gathered_state,
        in_proj.reshape(model_width, heads_dev * 3 * head_dim),
        preferred_element_type=jnp.float32,
    )
    width = 3 * head_dim
    query_pad = jnp.concatenate(
        sum(
            [
                [
                    projected[:, h * width : h * width + head_dim],
                    jnp.zeros((local_tokens, head_dim), jnp.float32),
                ]
                for h in range(heads_dev)
            ],
            [],
        ),
        axis=1,
    )
    key_value = jnp.concatenate(
        [projected[:, h * width + head_dim : (h + 1) * width] for h in range(heads_dev)], axis=1
    ).astype(jnp.bfloat16)
    first_token = seq_index * local_tokens
    seg_rows = -(-local_tokens // channels)
    seg_flat = jnp.pad(segment_ids, (0, seg_rows * channels - local_tokens))
    kv_ext = jnp.concatenate(
        [key_value, seg_flat.astype(jnp.bfloat16).reshape(seg_rows, channels)], axis=0
    )
    gathered = lax.all_gather(kv_ext, "seq", axis=0, tiled=False)
    seg_piece = (
        gathered[:, local_tokens:].reshape(seq_count, seg_rows * channels)[:, :local_tokens]
        .reshape(-1)
        .astype(jnp.int32)
    )
    piece_rows = seq_count * local_tokens
    scale_pad = jnp.pad(score_scale, ((0, 0), (0, lanes - head_dim))).reshape(heads_dev, 1, lanes)
    tiles = local_tokens // Q_TILE
    tile_first = first_token + Q_TILE * jnp.arange(tiles, dtype=jnp.int32)
    tile_seg = segment_ids.reshape(tiles, Q_TILE)[:, 0]
    block_last_seg = seg_piece.reshape(piece_rows // K_TILE, K_TILE)[:, -1]
    block_lo = jnp.sum(
        (block_last_seg[None, :] < tile_seg[:, None]).astype(jnp.int32), axis=1
    )
    block_hi = (tile_first + Q_TILE - 1) // K_TILE
    bounds = jnp.concatenate([block_lo, block_hi, first_token[None]]).astype(jnp.int32)
    segment_start = jnp.sum(
        (seg_piece[None, :] < segment_ids[:, None]).astype(jnp.int32), axis=1
    )
    heads_pad = flash_attend(
        bounds,
        query_pad,
        gathered,
        scale_pad,
        segment_start.reshape(local_tokens, 1),
        seg_piece.reshape(1, piece_rows),
        math.sqrt(head_dim),
        head_dim,
    )
    heads_flat = heads_pad[:, : heads_dev * head_dim]
    slots_dev = page_slot.shape[0] // seq_count
    my_slots = seq_index * slots_dev + jnp.arange(slots_dev, dtype=jnp.int32)
    page_ids = jnp.arange(page_slot.shape[0], dtype=jnp.int32)
    source_page = jnp.sum(
        jnp.where(page_slot[None, :] == my_slots[:, None], page_ids[None, :], 0), axis=1
    )
    page_cache = jnp.stack(
        [
            lax.dynamic_slice(
                gathered,
                (source_page[j] // pages_dev, (source_page[j] % pages_dev) * PAGE, 0),
                (1, PAGE, channels),
            )[0]
            for j in range(slots_dev)
        ]
    )
    chosen = heads_flat
    attn_own = scatter_sum(
        jnp.dot(chosen, out_proj, preferred_element_type=jnp.float32).astype(jnp.bfloat16),
        "tensor",
    )
    state_f = state_own.astype(jnp.float32)
    middle = unit_rows(state_f + step_rates[0] * (unit_rows(attn_own) - state_f))
    mid_rows = gather_rows(middle.astype(jnp.bfloat16), "tensor")
    both = jnp.einsum("td,dkf->tkf", mid_rows, up_proj, preferred_element_type=jnp.float32)
    act = (
        both[:, 0] * mlp_scale[0] * jax.nn.silu(both[:, 1] * mlp_scale[1] * math.sqrt(model_width))
    ).astype(jnp.bfloat16)
    chosen = act
    mlp_own = scatter_sum(
        jnp.dot(chosen, down_proj, preferred_element_type=jnp.float32).astype(jnp.bfloat16),
        "tensor",
    )
    final = unit_rows(middle + step_rates[1] * (unit_rows(mlp_own) - middle))
    out_state = (math.sqrt(model_width) * final).astype(jnp.bfloat16)
    return (out_state, page_cache)


def solution(mesh):
    return jax.shard_map(
        body,
        mesh=mesh,
        in_specs=(
            P(("seq", "tensor"), None),
            P("seq"),
            P(),
            P(None, "tensor", None),
            P("tensor", None),
            P(None, None, "tensor"),
            P("tensor", None),
            P("tensor", None),
            P(None, "tensor"),
            P(),
        ),
        out_specs=(P(("seq", "tensor"), None), P("seq", None, "tensor")),
        check_vma=False,
    )
```

```python
import functools
import math

import jax
import jax.numpy as jnp
from jax import lax
from jax.experimental import pallas as pl
from jax.experimental.pallas import tpu as pltpu
from jax.sharding import PartitionSpec as P

PAGE = 128


EPSILON = 1e-06
NEG_LARGE = -1e30


def unit_rows(matrix):
    return matrix * lax.rsqrt(jnp.sum(matrix * matrix, axis=-1, keepdims=True) + EPSILON)


def gather_rows(part, axis):
    count = lax.axis_size(axis)
    index = lax.axis_index(axis)
    parts = [part]
    for shift in range(1, count):
        pairs = [(j, (j + shift) % count) for j in range(count)]
        parts.append(lax.ppermute(part, axis, pairs))
    order = (index - jnp.arange(count, dtype=jnp.int32)) % count
    return jnp.take(jnp.stack(parts), order, axis=0).reshape(-1, *part.shape[1:])


def scatter_sum(whole, axis):
    count = lax.axis_size(axis)
    index = lax.axis_index(axis)
    blocks = whole.reshape(count, whole.shape[0] // count, *whole.shape[1:])
    total = lax.dynamic_index_in_dim(blocks, index, 0, keepdims=False).astype(jnp.float32)
    for shift in range(1, count):
        pairs = [(j, (j + shift) % count) for j in range(count)]
        send = lax.dynamic_index_in_dim(blocks, (index + shift) % count, 0, keepdims=False)
        total = total + lax.ppermute(send, axis, pairs).astype(jnp.float32)
    return total


Q_TILE = 512
K_TILE = 512


def attend_kernel(
    bounds_ref, proj_ref, kv_ref, scale_ref, qseg_ref, kseg_ref, out_ref, *, factor, half
):
    rows = qseg_ref.shape[0]
    heads = scale_ref.shape[0]
    lanes = 2 * half
    shard_blocks = (kv_ref.shape[1] - kv_ref.shape[1] % K_TILE) // K_TILE
    tiles = rows // Q_TILE
    first = bounds_ref[2 * tiles]
    fold = factor == 2.0 ** round(math.log2(factor))
    key_lane = lax.broadcasted_iota(jnp.int32, (K_TILE, lanes), 1)
    held = {}
    for head in range(heads):
        scale = scale_ref[head]
        for tile in range(tiles):
            q_raw = proj_ref[tile * Q_TILE : (tile + 1) * Q_TILE, head * lanes : (head + 1) * lanes]
            q_tile = (
                q_raw * lax.rsqrt(jnp.sum(q_raw * q_raw, axis=1, keepdims=True) + EPSILON) * scale
            ).astype(jnp.bfloat16)
            q_seg = qseg_ref[tile * Q_TILE : (tile + 1) * Q_TILE, :]
            q_pos = first + tile * Q_TILE + lax.broadcasted_iota(jnp.int32, (Q_TILE, K_TILE), 0)
            q_norm = jnp.sqrt(
                jnp.sum(jnp.square(q_tile.astype(jnp.float32)), axis=1, keepdims=True)
            )
            shift = factor * q_norm * (jnp.max(scale) * (1.0 + 2.0**-6))
            if fold:
                q_tile = q_tile * jnp.asarray(factor, jnp.bfloat16)

            def step(block, acc, q_tile=q_tile, q_seg=q_seg, q_pos=q_pos, head=head, scale=scale,
                     shift=shift):
                shard = block // shard_blocks
                row_at = pl.multiple_of((block % shard_blocks) * K_TILE, K_TILE)
                key_at = pl.multiple_of(block * K_TILE, K_TILE)
                kv_blk = kv_ref[shard, pl.ds(row_at, K_TILE), head * lanes : (head + 1) * lanes]
                kv_f = kv_blk.astype(jnp.float32)
                k_sq = jnp.where(key_lane < half, kv_f * kv_f, 0.0)
                k_unit = (
                    kv_f * lax.rsqrt(jnp.sum(k_sq, axis=1, keepdims=True) + EPSILON) * scale
                ).astype(jnp.bfloat16)
                k_seg = kseg_ref[:, pl.ds(key_at, K_TILE)]
                scores = lax.dot_general(
                    q_tile, k_unit, (((1,), (1,)), ((), ())), preferred_element_type=jnp.float32
                )
                if not fold:
                    scores = factor * scores
                k_pos = key_at + lax.broadcasted_iota(jnp.int32, (Q_TILE, K_TILE), 1)
                allowed = (q_seg == k_seg) & (k_pos <= q_pos)
                weights = jnp.where(allowed, jnp.exp(scores - shift), 0.0).astype(jnp.bfloat16)
                kv_sum = jnp.where(key_lane == 0, jnp.ones_like(kv_blk), kv_blk)
                return acc + jnp.dot(weights, kv_sum, preferred_element_type=jnp.float32)

            acc = lax.fori_loop(
                bounds_ref[tile],
                bounds_ref[tiles + tile] + 1,
                step,
                jnp.zeros((Q_TILE, lanes), jnp.float32),
            )
            total = acc[:, 0:1]
            result = acc / total
            pair = head // 2
            rows_at = slice(tile * Q_TILE, (tile + 1) * Q_TILE)
            if head % 2 == 0:
                held[tile] = pltpu.roll(result, half, 1)
                if head == heads - 1:
                    out_ref[rows_at, pair * lanes : (pair + 1) * lanes] = held[tile].astype(
                        out_ref.dtype
                    )
            else:
                joined = jnp.where(
                    lax.broadcasted_iota(jnp.int32, (Q_TILE, lanes), 1) < half, held[tile], result
                )
                out_ref[rows_at, pair * lanes : (pair + 1) * lanes] = joined.astype(out_ref.dtype)


def flash_attend(bounds, proj, gathered, scale_pad, query_segs, key_segs, factor, half):
    rows = query_segs.shape[0]
    heads, _, lanes = scale_pad.shape
    keys = key_segs.shape[1]
    vmem = pl.BlockSpec(memory_space=pltpu.VMEM)
    return pl.pallas_call(
        functools.partial(attend_kernel, factor=factor, half=half),
        out_shape=jax.ShapeDtypeStruct((rows, -(-heads // 2) * lanes), jnp.bfloat16),
        in_specs=[pl.BlockSpec(memory_space=pltpu.SMEM)] + [vmem] * 5,
        out_specs=vmem,
        cost_estimate=pl.CostEstimate(
            flops=4 * heads * rows * keys * lanes,
            transcendentals=heads * rows * keys,
            bytes_accessed=heads * keys * lanes * 2,
        ),
    )(bounds, proj, gathered, scale_pad, query_segs, key_segs)


def body(
    hidden,
    segment_ids,
    page_slot,
    in_proj,
    out_proj,
    up_proj,
    down_proj,
    score_scale,
    mlp_scale,
    step_rates,
):
    seq_count = lax.axis_size("seq")
    seq_index = lax.axis_index("seq")
    local_tokens = segment_ids.shape[0]
    heads_dev, head_dim = score_scale.shape
    model_width = hidden.shape[1]
    hidden_dev = down_proj.shape[0]
    pages_dev = local_tokens // PAGE
    channels = heads_dev * 2 * head_dim
    state_own = unit_rows(hidden.astype(jnp.float32)).astype(jnp.bfloat16)
    gathered_state = gather_rows(state_own, "tensor")
    lanes = 2 * head_dim
    projected = jnp.dot(
        gathered_state,
        in_proj.reshape(model_width, heads_dev * 3 * head_dim),
        preferred_element_type=jnp.float32,
    )
    width = 3 * head_dim
    query_pad = jnp.concatenate(
        sum(
            [
                [
                    projected[:, h * width : h * width + head_dim],
                    jnp.zeros((local_tokens, head_dim), jnp.float32),
                ]
                for h in range(heads_dev)
            ],
            [],
        ),
        axis=1,
    )
    key_value = jnp.concatenate(
        [projected[:, h * width + head_dim : (h + 1) * width] for h in range(heads_dev)], axis=1
    ).astype(jnp.bfloat16)
    first_token = seq_index * local_tokens
    seg_rows = -(-local_tokens // channels)
    seg_flat = jnp.pad(segment_ids, (0, seg_rows * channels - local_tokens))
    kv_ext = jnp.concatenate(
        [key_value, seg_flat.astype(jnp.bfloat16).reshape(seg_rows, channels)], axis=0
    )
    gathered = lax.all_gather(kv_ext, "seq", axis=0, tiled=False)
    seg_piece = (
        gathered[:, local_tokens:].reshape(seq_count, seg_rows * channels)[:, :local_tokens]
        .reshape(-1)
        .astype(jnp.int32)
    )
    piece_rows = seq_count * local_tokens
    scale_pad = jnp.pad(score_scale, ((0, 0), (0, lanes - head_dim))).reshape(heads_dev, 1, lanes)
    tiles = local_tokens // Q_TILE
    tile_first = first_token + Q_TILE * jnp.arange(tiles, dtype=jnp.int32)
    tile_seg = segment_ids.reshape(tiles, Q_TILE)[:, 0]
    block_last_seg = seg_piece.reshape(piece_rows // K_TILE, K_TILE)[:, -1]
    block_lo = jnp.sum(
        (block_last_seg[None, :] < tile_seg[:, None]).astype(jnp.int32), axis=1
    )
    block_hi = (tile_first + Q_TILE - 1) // K_TILE
    bounds = jnp.concatenate([block_lo, block_hi, first_token[None]]).astype(jnp.int32)
    heads_pad = flash_attend(
        bounds,
        query_pad,
        gathered,
        scale_pad,
        segment_ids.reshape(local_tokens, 1),
        seg_piece.reshape(1, piece_rows),
        math.sqrt(head_dim),
        head_dim,
    )
    heads_flat = heads_pad[:, : heads_dev * head_dim]
    slots_dev = page_slot.shape[0] // seq_count
    my_slots = seq_index * slots_dev + jnp.arange(slots_dev, dtype=jnp.int32)
    page_ids = jnp.arange(page_slot.shape[0], dtype=jnp.int32)
    source_page = jnp.sum(
        jnp.where(page_slot[None, :] == my_slots[:, None], page_ids[None, :], 0), axis=1
    )
    page_cache = jnp.stack(
        [
            lax.dynamic_slice(
                gathered,
                (source_page[j] // pages_dev, (source_page[j] % pages_dev) * PAGE, 0),
                (1, PAGE, channels),
            )[0]
            for j in range(slots_dev)
        ]
    )
    chosen = heads_flat
    attn_own = scatter_sum(
        jnp.dot(chosen, out_proj, preferred_element_type=jnp.float32).astype(jnp.bfloat16),
        "tensor",
    )
    state_f = state_own.astype(jnp.float32)
    middle = unit_rows(state_f + step_rates[0] * (unit_rows(attn_own) - state_f))
    mid_rows = gather_rows(middle.astype(jnp.bfloat16), "tensor")
    both = jnp.einsum("td,dkf->tkf", mid_rows, up_proj, preferred_element_type=jnp.float32)
    act = (
        both[:, 0] * mlp_scale[0] * jax.nn.silu(both[:, 1] * mlp_scale[1] * math.sqrt(model_width))
    ).astype(jnp.bfloat16)
    chosen = act
    mlp_own = scatter_sum(
        jnp.dot(chosen, down_proj, preferred_element_type=jnp.float32).astype(jnp.bfloat16),
        "tensor",
    )
    final = unit_rows(middle + step_rates[1] * (unit_rows(mlp_own) - middle))
    out_state = (math.sqrt(model_width) * final).astype(jnp.bfloat16)
    return (out_state, page_cache)


def solution(mesh):
    return jax.shard_map(
        body,
        mesh=mesh,
        in_specs=(
            P(("seq", "tensor"), None),
            P("seq"),
            P(),
            P(None, "tensor", None),
            P("tensor", None),
            P(None, None, "tensor"),
            P("tensor", None),
            P("tensor", None),
            P(None, "tensor"),
            P(),
        ),
        out_specs=(P(("seq", "tensor"), None), P("seq", None, "tensor")),
        check_vma=False,
    )
```

```python
import functools
import math

import jax
import jax.numpy as jnp
from jax import lax
from jax.experimental import pallas as pl
from jax.experimental.pallas import tpu as pltpu
from jax.sharding import PartitionSpec as P

PAGE = 128


EPSILON = 1e-06
NEG_LARGE = -1e30


def unit_rows(matrix):
    return matrix * lax.rsqrt(jnp.sum(matrix * matrix, axis=-1, keepdims=True) + EPSILON)


def gather_rows(part, axis):
    count = lax.axis_size(axis)
    index = lax.axis_index(axis)
    rows = part.shape[0]
    out = jnp.zeros((count * rows, *part.shape[1:]), part.dtype)
    out = lax.dynamic_update_slice_in_dim(out, part, index * rows, 0)
    for shift in range(1, count):
        pairs = [(j, (j + shift) % count) for j in range(count)]
        came = lax.ppermute(part, axis, pairs)
        out = lax.dynamic_update_slice_in_dim(out, came, ((index - shift) % count) * rows, 0)
    return out


def scatter_sum(whole, axis):
    count = lax.axis_size(axis)
    index = lax.axis_index(axis)
    blocks = whole.reshape(count, whole.shape[0] // count, *whole.shape[1:])
    total = lax.dynamic_index_in_dim(blocks, index, 0, keepdims=False).astype(jnp.float32)
    for shift in range(1, count):
        pairs = [(j, (j + shift) % count) for j in range(count)]
        send = lax.dynamic_index_in_dim(blocks, (index + shift) % count, 0, keepdims=False)
        total = total + lax.ppermute(send, axis, pairs).astype(jnp.float32)
    return total


Q_TILE = 512
K_TILE = 512


def attend_kernel(
    bounds_ref, proj_ref, kv_ref, scale_ref, qseg_ref, kseg_ref, out_ref, *, factor, half
):
    rows = qseg_ref.shape[0]
    heads = scale_ref.shape[0]
    lanes = 2 * half
    shard_blocks = (kv_ref.shape[1] - kv_ref.shape[1] % K_TILE) // K_TILE
    tiles = rows // Q_TILE
    first = bounds_ref[2 * tiles]
    fold = factor == 2.0 ** round(math.log2(factor))
    key_lane = lax.broadcasted_iota(jnp.int32, (K_TILE, lanes), 1)
    lane_pick = (lax.broadcasted_iota(jnp.int32, (lanes, lanes), 0) < half).astype(jnp.float32)
    held = {}
    for head in range(heads):
        scale = scale_ref[head]
        for tile in range(tiles):
            q_raw = proj_ref[tile * Q_TILE : (tile + 1) * Q_TILE, head * lanes : (head + 1) * lanes]
            q_tile = (
                q_raw * lax.rsqrt(jnp.sum(q_raw * q_raw, axis=1, keepdims=True) + EPSILON) * scale
            ).astype(jnp.bfloat16)
            q_seg = qseg_ref[tile * Q_TILE : (tile + 1) * Q_TILE, :]
            q_pos = first + tile * Q_TILE + lax.broadcasted_iota(jnp.int32, (Q_TILE, K_TILE), 0)
            q_norm = jnp.sqrt(
                jnp.sum(jnp.square(q_tile.astype(jnp.float32)), axis=1, keepdims=True)
            )
            shift = factor * q_norm * (jnp.max(scale) * (1.0 + 2.0**-6))
            if fold:
                q_tile = q_tile * jnp.asarray(factor, jnp.bfloat16)

            def step(block, acc, q_tile=q_tile, q_seg=q_seg, q_pos=q_pos, head=head, scale=scale,
                     shift=shift):
                shard = block // shard_blocks
                row_at = pl.multiple_of((block % shard_blocks) * K_TILE, K_TILE)
                key_at = pl.multiple_of(block * K_TILE, K_TILE)
                kv_blk = kv_ref[shard, pl.ds(row_at, K_TILE), head * lanes : (head + 1) * lanes]
                kv_f = kv_blk.astype(jnp.float32)
                k_sum = jnp.dot(
                    kv_f * kv_f, lane_pick, precision=lax.Precision.HIGHEST,
                    preferred_element_type=jnp.float32,
                )
                k_unit = (kv_f * lax.rsqrt(k_sum + EPSILON) * scale).astype(jnp.bfloat16)
                k_seg = kseg_ref[:, pl.ds(key_at, K_TILE)]
                scores = lax.dot_general(
                    q_tile, k_unit, (((1,), (1,)), ((), ())), preferred_element_type=jnp.float32
                )
                if not fold:
                    scores = factor * scores
                k_pos = key_at + lax.broadcasted_iota(jnp.int32, (Q_TILE, K_TILE), 1)
                allowed = (q_seg == k_seg) & (k_pos <= q_pos)
                weights = jnp.where(allowed, jnp.exp(scores - shift), 0.0).astype(jnp.bfloat16)
                kv_sum = jnp.where(key_lane == 0, jnp.ones_like(kv_blk), kv_blk)
                return acc + jnp.dot(weights, kv_sum, preferred_element_type=jnp.float32)

            acc = lax.fori_loop(
                bounds_ref[tile],
                bounds_ref[tiles + tile] + 1,
                step,
                jnp.zeros((Q_TILE, lanes), jnp.float32),
            )
            total = acc[:, 0:1]
            result = acc / total
            pair = head // 2
            rows_at = slice(tile * Q_TILE, (tile + 1) * Q_TILE)
            if head % 2 == 0:
                held[tile] = pltpu.roll(result, half, 1)
                if head == heads - 1:
                    out_ref[rows_at, pair * lanes : (pair + 1) * lanes] = held[tile].astype(
                        out_ref.dtype
                    )
            else:
                joined = jnp.where(
                    lax.broadcasted_iota(jnp.int32, (Q_TILE, lanes), 1) < half, held[tile], result
                )
                out_ref[rows_at, pair * lanes : (pair + 1) * lanes] = joined.astype(out_ref.dtype)


def flash_attend(bounds, proj, gathered, scale_pad, query_segs, key_segs, factor, half):
    rows = query_segs.shape[0]
    heads, _, lanes = scale_pad.shape
    keys = key_segs.shape[1]
    vmem = pl.BlockSpec(memory_space=pltpu.VMEM)
    return pl.pallas_call(
        functools.partial(attend_kernel, factor=factor, half=half),
        out_shape=jax.ShapeDtypeStruct((rows, -(-heads // 2) * lanes), jnp.bfloat16),
        in_specs=[pl.BlockSpec(memory_space=pltpu.SMEM)] + [vmem] * 5,
        out_specs=vmem,
        cost_estimate=pl.CostEstimate(
            flops=4 * heads * rows * keys * lanes,
            transcendentals=heads * rows * keys,
            bytes_accessed=heads * keys * lanes * 2,
        ),
    )(bounds, proj, gathered, scale_pad, query_segs, key_segs)


def body(
    hidden,
    segment_ids,
    page_slot,
    in_proj,
    out_proj,
    up_proj,
    down_proj,
    score_scale,
    mlp_scale,
    step_rates,
):
    seq_count = lax.axis_size("seq")
    seq_index = lax.axis_index("seq")
    local_tokens = segment_ids.shape[0]
    heads_dev, head_dim = score_scale.shape
    model_width = hidden.shape[1]
    hidden_dev = down_proj.shape[0]
    pages_dev = local_tokens // PAGE
    channels = heads_dev * 2 * head_dim
    state_own = unit_rows(hidden.astype(jnp.float32)).astype(jnp.bfloat16)
    gathered_state = gather_rows(state_own, "tensor")
    lanes = 2 * head_dim
    projected = jnp.dot(
        gathered_state,
        in_proj.reshape(model_width, heads_dev * 3 * head_dim),
        preferred_element_type=jnp.float32,
    )
    width = 3 * head_dim
    query_pad = jnp.concatenate(
        sum(
            [
                [
                    projected[:, h * width : h * width + head_dim],
                    jnp.zeros((local_tokens, head_dim), jnp.float32),
                ]
                for h in range(heads_dev)
            ],
            [],
        ),
        axis=1,
    )
    key_value = jnp.concatenate(
        [projected[:, h * width + head_dim : (h + 1) * width] for h in range(heads_dev)], axis=1
    ).astype(jnp.bfloat16)
    first_token = seq_index * local_tokens
    seg_rows = -(-local_tokens // channels)
    seg_flat = jnp.pad(segment_ids, (0, seg_rows * channels - local_tokens))
    kv_ext = jnp.concatenate(
        [key_value, seg_flat.astype(jnp.bfloat16).reshape(seg_rows, channels)], axis=0
    )
    gathered = lax.all_gather(kv_ext, "seq", axis=0, tiled=False)
    seg_piece = (
        gathered[:, local_tokens:].reshape(seq_count, seg_rows * channels)[:, :local_tokens]
        .reshape(-1)
        .astype(jnp.int32)
    )
    piece_rows = seq_count * local_tokens
    scale_pad = jnp.pad(score_scale, ((0, 0), (0, lanes - head_dim))).reshape(heads_dev, 1, lanes)
    tiles = local_tokens // Q_TILE
    tile_first = first_token + Q_TILE * jnp.arange(tiles, dtype=jnp.int32)
    tile_seg = segment_ids.reshape(tiles, Q_TILE)[:, 0]
    block_last_seg = seg_piece.reshape(piece_rows // K_TILE, K_TILE)[:, -1]
    block_lo = jnp.sum(
        (block_last_seg[None, :] < tile_seg[:, None]).astype(jnp.int32), axis=1
    )
    block_hi = (tile_first + Q_TILE - 1) // K_TILE
    bounds = jnp.concatenate([block_lo, block_hi, first_token[None]]).astype(jnp.int32)
    heads_pad = flash_attend(
        bounds,
        query_pad,
        gathered,
        scale_pad,
        segment_ids.reshape(local_tokens, 1),
        seg_piece.reshape(1, piece_rows),
        math.sqrt(head_dim),
        head_dim,
    )
    heads_flat = heads_pad[:, : heads_dev * head_dim]
    slots_dev = page_slot.shape[0] // seq_count
    my_slots = seq_index * slots_dev + jnp.arange(slots_dev, dtype=jnp.int32)
    page_ids = jnp.arange(page_slot.shape[0], dtype=jnp.int32)
    source_page = jnp.sum(
        jnp.where(page_slot[None, :] == my_slots[:, None], page_ids[None, :], 0), axis=1
    )
    page_cache = jnp.stack(
        [
            lax.dynamic_slice(
                gathered,
                (source_page[j] // pages_dev, (source_page[j] % pages_dev) * PAGE, 0),
                (1, PAGE, channels),
            )[0]
            for j in range(slots_dev)
        ]
    )
    chosen = heads_flat
    attn_own = scatter_sum(
        jnp.dot(chosen, out_proj, preferred_element_type=jnp.float32).astype(jnp.bfloat16),
        "tensor",
    )
    state_f = state_own.astype(jnp.float32)
    middle = unit_rows(state_f + step_rates[0] * (unit_rows(attn_own) - state_f))
    mid_rows = gather_rows(middle.astype(jnp.bfloat16), "tensor")
    both = jnp.einsum("td,dkf->tkf", mid_rows, up_proj, preferred_element_type=jnp.float32)
    act = (
        both[:, 0] * mlp_scale[0] * jax.nn.silu(both[:, 1] * mlp_scale[1] * math.sqrt(model_width))
    ).astype(jnp.bfloat16)
    chosen = act
    mlp_own = scatter_sum(
        jnp.dot(chosen, down_proj, preferred_element_type=jnp.float32).astype(jnp.bfloat16),
        "tensor",
    )
    final = unit_rows(middle + step_rates[1] * (unit_rows(mlp_own) - middle))
    out_state = (math.sqrt(model_width) * final).astype(jnp.bfloat16)
    return (out_state, page_cache)


def solution(mesh):
    return jax.shard_map(
        body,
        mesh=mesh,
        in_specs=(
            P(("seq", "tensor"), None),
            P("seq"),
            P(),
            P(None, "tensor", None),
            P("tensor", None),
            P(None, None, "tensor"),
            P("tensor", None),
            P("tensor", None),
            P(None, "tensor"),
            P(),
        ),
        out_specs=(P(("seq", "tensor"), None), P("seq", None, "tensor")),
        check_vma=False,
    )
```
